512 devices in a mesh: sub: 128 (over z, x, core), crow: 4 (over y).
Axes of the slice: x: 4, y: 4, z: 16, core: 2. Of those that a mesh axis runs over, the one named last changes fastest.
Arguments:
- deflation: bfloat16 [128, 12288, 128], P('sub', 'crow'), as said below
- diag_op: bfloat16 [128, 96, 128, 128], P('sub', 'crow'), as said below
- upper_op: bfloat16 [128, 96, 128, 128], P('sub', 'crow'), may hold values from -0.022094727 to 0.022094727
- tile_blocks: int32 [128, 4, 16], P('sub', 'crow'), may hold values from 0 to 23
- pair_counts: int32 [128, 8], P('sub'), may hold values from 0 to 8, as said below
- pivot_owner: int32 [128], P('sub'), may hold values from 0 to 3
Outputs:
- schur_self: float32 [16384, 128], P(('sub', 'crow'))
- schur_coupling: float32 [16384, 1024], P(('sub', 'crow'))
- panel: float32 [16384, 32], P(('sub', 'crow'))
The draws below stay inside these ranges and needn't reach their ends.
Inputs may be any that keep to these rules, and one draw needn't show every extreme that they name: deflation has independent columns of different scales. Each diag_op block is symmetric with a positive diagonal, and every A_s is symmetric positive definite. pair_counts[s, j] equals pair_counts[s + o[j], 7 - j], is 0 where s + o[j] lies outside 0 to 127, and the pair of subdomains 0 and 1 shares 8 tiles.
All inputs are finite; a program needn't handle non-finite values.
Results may differ from the reference program's by a relative error of at most 0.0029.
Values may be sent and summed in bfloat16 or wider, within the bound.
No kernel may reach another device: no remote copies, remote signals or barrier semaphores. Data moves between devices by JAX's collectives and lax.ppermute only.
A program may use at most 64 MiB of HBM per device.

```python
import math
import jax
import jax.numpy as jnp
from jax import lax

K = 128
TB = 128
RB_DEV = 24
TPD = 2
NB = 8
SUBS = 128
GX = 16
RBS = 96
ROWS = 12288
MAXT = 8
N_CROW = 4


coupling_bound = 0.0221


def draw_deflation(key, part):
    first_key, second_key = jax.random.split(key, 2)
    column_scale = jnp.exp(jax.random.uniform(second_key, (K,), jnp.float32, math.log(0.5), math.log(2.0)))
    values = jnp.clip(jax.random.normal(first_key, (SUBS, ROWS, K), jnp.float32), -6.0, 6.0) * column_scale
    return (values / math.sqrt(TB)).astype(jnp.bfloat16)


def draw_diag_op(key, part):
    first_key, second_key = jax.random.split(key)
    noise = jax.random.uniform(first_key, (SUBS, RBS, TB, TB), jnp.float32, -coupling_bound, coupling_bound)
    symmetric = (noise + jnp.swapaxes(noise, 2, 3)) * 0.7071
    top_value = 4.0
    diagonal = jnp.exp(jax.random.uniform(second_key, (SUBS, RBS, TB), jnp.float32, 0.0, math.log(top_value)))
    return (symmetric + diagonal[..., None] * jnp.eye(TB, dtype=jnp.float32)).astype(jnp.bfloat16)


def draw_pair_counts(key, part):
    first_key, second_key = jax.random.split(jax.random.fold_in(key, 7))
    base_load = jax.random.randint(first_key, (SUBS, SUBS), 0, MAXT // 2 + 1)
    heavy = (jax.random.randint(second_key, (SUBS,), 0, 4) == 0).astype(jnp.int32)
    indices = jnp.arange(SUBS, dtype=jnp.int32)
    lower_index = jnp.minimum(indices[:, None], indices[None, :])
    upper_index = jnp.maximum(indices[:, None], indices[None, :])
    symmetric = base_load[lower_index, upper_index]
    pair_load = jnp.minimum(MAXT, symmetric + 6 * (heavy[:, None] + heavy[None, :]))
    pair_load = pair_load.at[0, 1].set(MAXT).at[1, 0].set(MAXT)
    offsets = [-GX - 1, -GX, -GX + 1, -1, 1, GX - 1, GX, GX + 1]
    columns = []
    for offset_value in offsets:
        target = indices + offset_value
        inside = (target >= 0) & (target < SUBS)
        clipped = jnp.clip(target, 0, SUBS - 1)
        columns.append(jnp.where(inside, pair_load[indices, clipped], 0))
    return jnp.stack(columns, 1).astype(jnp.int32)


def set_ends(values, key, smallest, high):
    longest = values.shape.index(max(values.shape))
    spots = []
    for shift in (0, 1):
        where = [jax.random.randint(jax.random.fold_in(key, axis), (), 0, length) for axis, length in enumerate(values.shape)]
        where[longest] = (where[longest] + shift) % values.shape[longest]
        spots.append(tuple(where))
    return values.at[spots[0]].set(smallest).at[spots[1]].set(high)


def block_levels(key, extent, cuts, low, high):
    gain = 1.0
    for position, shards_of in cuts:
        draws = jax.random.uniform(jax.random.fold_in(jax.random.fold_in(key, 6), position), (shards_of,), jnp.float32, low / len(cuts), high / len(cuts))
        gain = gain * jnp.repeat(jnp.exp(draws), extent[position] // shards_of).reshape((-1,) + (1,) * (len(extent) - 1 - position))
    return gain


def setup_inputs(seed: int = 0) -> dict:
    key_of = jax.random.split(jax.random.key(seed), 7)
    deflation = draw_deflation(jax.random.fold_in(key_of[6], 71), 0)
    diag_op = draw_diag_op(jax.random.fold_in(key_of[6], 71), 0)
    upper_op = jnp.clip(jax.random.uniform(key_of[2], (SUBS, RBS, TB, TB), jnp.float32, -0.022094727, 0.022094727) * block_levels(key_of[2], (SUBS, RBS, TB, TB), ((0, 128), (1, 4)), -0.4, 0.0), -0.022094727, 0.022094727).astype(jnp.bfloat16)
    tile_blocks = set_ends(jax.random.randint(key_of[3], (SUBS, N_CROW, NB * TPD), 0, RB_DEV), jax.random.fold_in(key_of[3], 1), 0, RB_DEV - 1).astype(jnp.int32)
    pair_counts = draw_pair_counts(jax.random.fold_in(key_of[6], 71), 0)
    pivot_owner = set_ends(jax.random.randint(key_of[5], (SUBS,), 0, N_CROW), jax.random.fold_in(key_of[5], 1), 0, N_CROW - 1).astype(jnp.int32)
    return dict(deflation=deflation, diag_op=diag_op, upper_op=upper_op, tile_blocks=tile_blocks, pair_counts=pair_counts, pivot_owner=pivot_owner)


def neighbour_offsets(across):
    return [-across - 1, -across, -across + 1, -1, 1, across - 1, across, across + 1]

def reference(deflation, diag_op, upper_op, tile_blocks, pair_counts, pivot_owner):
    sub_total, row_total, coarse_width = deflation.shape
    block_total, tile_rows = (diag_op.shape[1], diag_op.shape[2])
    block_share = block_total // N_CROW
    slot_count = pair_counts.shape[1]
    per_slot = tile_blocks.shape[2] // slot_count
    row_share = coarse_width // N_CROW

    def apply_local(index):
        vectors = deflation[index].astype(jnp.float32).reshape(block_total, tile_rows, coarse_width)
        diagonal = diag_op[index].astype(jnp.float32)
        upper_blocks = upper_op[index].astype(jnp.float32)
        zero_rows = jnp.zeros((1, tile_rows, coarse_width), jnp.float32)
        zero_block = jnp.zeros((1, tile_rows, tile_rows), jnp.float32)
        before = jnp.concatenate([zero_rows, vectors[:-1]], 0)
        after = jnp.concatenate([vectors[1:], zero_rows], 0)
        lower_blocks = jnp.concatenate([zero_block, upper_blocks[:-1]], 0)
        product = jnp.einsum('bij,bjk->bik', diagonal, vectors) + jnp.einsum('bij,bjk->bik', upper_blocks, after) + jnp.einsum('bji,bjk->bik', lower_blocks, before)
        return product.astype(jnp.bfloat16)
    applied = lax.map(apply_local, jnp.arange(sub_total, dtype=jnp.int32))
    offsets = jnp.array(neighbour_offsets(GX), jnp.int32)
    crow_ids = jnp.arange(N_CROW, dtype=jnp.int32)
    unit_ids = jnp.arange(per_slot, dtype=jnp.int32)
    slot_ids = jnp.arange(slot_count, dtype=jnp.int32)
    opposite = (slot_count - 1 - slot_ids).astype(jnp.int32)

    def coarse_row(index):
        vectors = deflation[index].astype(jnp.float32)
        vector_blocks = vectors.reshape(block_total, tile_rows, coarse_width)
        applied_rows = applied[index].astype(jnp.float32).reshape(row_total, coarse_width)
        gram_part = jnp.einsum('nr,nk->rk', vectors, applied_rows)
        own_blocks = tile_blocks[index].reshape(N_CROW, slot_count, per_slot) + crow_ids[:, None, None] * block_share
        target = index + offsets
        clipped = jnp.clip(target, 0, sub_total - 1).astype(jnp.int32)
        far_lists = tile_blocks[clipped].reshape(slot_count, N_CROW, slot_count, per_slot)
        far_pick = far_lists[slot_ids, :, opposite, :]
        far_blocks = jnp.transpose(far_pick, (1, 0, 2)) + crow_ids[:, None, None] * block_share
        live_mask = crow_ids[:, None, None] * per_slot + unit_ids[None, None, :] < pair_counts[index][None, :, None]
        own_tiles = vector_blocks[own_blocks] * live_mask[..., None, None].astype(jnp.float32)
        far_tiles = applied[clipped[None, :, None], far_blocks].astype(jnp.float32)
        coupling = jnp.einsum('cjutr,cjutk->rjk', own_tiles, far_tiles)
        whole = jnp.concatenate([gram_part[:, None, :], coupling], 1).reshape(coarse_width, (slot_count + 1) * coarse_width)
        owner_index = pivot_owner[index]
        leading = lax.dynamic_slice_in_dim(whole, owner_index * row_share, row_share, 0)
        pivot_block = lax.dynamic_slice_in_dim(leading, owner_index * row_share, row_share, 1)
        factor = jnp.linalg.cholesky(pivot_block)
        solved = jax.scipy.linalg.solve_triangular(factor, leading, lower=True)
        columns = lax.dynamic_slice_in_dim(whole, owner_index * row_share, row_share, 1)
        panel_rows = jax.scipy.linalg.solve_triangular(factor, columns.T, lower=True).T
        updated = whole - jnp.dot(panel_rows, solved, precision=lax.Precision.HIGHEST)
        return (updated[:, :coarse_width], updated[:, coarse_width:], panel_rows)
    self_part, coupling_part, panel_part = lax.map(coarse_row, jnp.arange(sub_total, dtype=jnp.int32))
    return (self_part.reshape(sub_total * coarse_width, coarse_width), coupling_part.reshape(sub_total * coarse_width, slot_count * coarse_width), panel_part.reshape(sub_total * coarse_width, row_share))
```

```python
import jax
import jax.numpy as jnp
from jax import lax
from jax.sharding import PartitionSpec as P


def padded_2(block, sides, width):
    for axis, dim in sides:
        count = lax.axis_size(axis)
        forward = [(i, i + 1) for i in range(count - 1)]
        backward = [(target, source) for source, target in forward]
        low = lax.ppermute(
            lax.slice_in_dim(block, block.shape[dim] - width, None, axis=dim), axis, forward
        )
        high = lax.ppermute(lax.slice_in_dim(block, 0, width, axis=dim), axis, backward)
        block = jnp.concatenate([low, block, high], axis=dim)
    return block


def shifted(value, axis, steps):
    count = lax.axis_size(axis)
    initial, last = (max(0, -steps), min(count, count - steps))
    return lax.ppermute(value, axis, [(source, source + steps) for source in range(initial, last)])


def broadcast(shard, axis, root):
    mine = lax.axis_index(axis) == root
    return lax.psum(jnp.where(mine, shard, jnp.zeros_like(shard)), axis)


def neighbour_offsets(across):
    return [-across - 1, -across, -across + 1, -1, 1, across - 1, across, across + 1]


def per_device(deflation, diag_op, upper_op, tile_blocks, pair_counts, pivot_owner):
    crow_count = lax.axis_size("crow")
    crow_place = lax.axis_index("crow")
    sub_count = lax.axis_size("sub")
    across = min(16, sub_count // 2)
    offsets = neighbour_offsets(across)
    local_rows = deflation[0]
    blocks_here, tile_rows = (diag_op.shape[1], diag_op.shape[2])
    coarse_width = local_rows.shape[1]
    slot_count = pair_counts.shape[1]
    per_slot = tile_blocks.shape[2] // slot_count
    padded = padded_2(local_rows, (("crow", 0),), tile_rows)
    stacked = padded.reshape(blocks_here + 2, tile_rows, coarse_width)
    centre = stacked[1:-1]
    previous_upper = shifted(upper_op[0, blocks_here - 1], "crow", 1)
    lower_blocks = jnp.concatenate([previous_upper[None], upper_op[0, :-1]], 0)
    product = (
        jnp.einsum("bij,bjk->bik", diag_op[0], centre, preferred_element_type=jnp.float32)
        + jnp.einsum("bij,bjk->bik", upper_op[0], stacked[2:], preferred_element_type=jnp.float32)
        + jnp.einsum("bji,bjk->bik", lower_blocks, stacked[:-2], preferred_element_type=jnp.float32)
    )
    applied = product.astype(jnp.bfloat16)
    chosen = tile_blocks[0, 0]
    own_tiles = centre[chosen].reshape(slot_count, per_slot, tile_rows, coarse_width)
    outgoing = applied[chosen].reshape(slot_count, per_slot, tile_rows, coarse_width)
    position = crow_place * per_slot + jnp.arange(per_slot, dtype=jnp.int32)
    live_mask = (position[None, :] < pair_counts[0][:, None]).astype(jnp.bfloat16)
    own_masked = own_tiles * live_mask[:, :, None, None]
    arrived = [None] * slot_count
    for slot_index in range(slot_count):
        arrived[slot_index] = shifted(
            outgoing[slot_count - 1 - slot_index], "sub", -offsets[slot_index]
        )
    received = jnp.stack(arrived)
    flat_vectors = centre.reshape(blocks_here * tile_rows, coarse_width)
    flat_applied = applied.reshape(blocks_here * tile_rows, coarse_width)
    row_share = coarse_width // crow_count
    owner_index = pivot_owner[0]
    gram_part = jnp.einsum(
        "nr,nk->rk", flat_vectors, flat_applied, preferred_element_type=jnp.float32
    )
    coupling = jnp.einsum(
        "jutr,jutk->rjk", own_masked, received, preferred_element_type=jnp.float32
    )
    whole = jnp.concatenate([gram_part[:, None, :], coupling], 1).reshape(
        coarse_width, (slot_count + 1) * coarse_width
    )
    pivot_partial = lax.dynamic_slice_in_dim(whole, owner_index * row_share, row_share, 0)

    def payload(target):
        rows = lax.dynamic_slice_in_dim(whole, target * row_share, row_share, 0)
        return jnp.concatenate([rows, pivot_partial], 0)

    pieces = [payload(crow_place)]
    for step in range(1, crow_count):
        target = (crow_place + step) % crow_count
        pairs = [(i, (i + step) % crow_count) for i in range(crow_count)]
        pieces.append(lax.ppermute(payload(target), "crow", pairs))
    if crow_count == 4:
        total = (pieces[0] + pieces[2]) + (pieces[1] + pieces[3])
    else:
        total = sum(pieces[1:], pieces[0])
    own_rows = total[:row_share]
    leading = total[row_share:]
    pivot_block = lax.dynamic_slice_in_dim(leading, owner_index * row_share, row_share, 1)
    factor = jnp.linalg.cholesky(pivot_block)
    solved = jax.scipy.linalg.solve_triangular(factor, leading, lower=True)
    columns = lax.dynamic_slice_in_dim(own_rows, owner_index * row_share, row_share, 1)
    panel_rows = jax.scipy.linalg.solve_triangular(factor, columns.T, lower=True).T
    updated = own_rows - jnp.dot(panel_rows, solved, precision=lax.Precision.HIGHEST)
    return (updated[:, :coarse_width], updated[:, coarse_width:], panel_rows)


def solution(mesh):
    placed = (
        P("sub", "crow", None),
        P("sub", "crow", None, None),
        P("sub", "crow", None, None),
        P("sub", "crow", None),
        P("sub", None),
        P("sub"),
    )
    return jax.shard_map(
        per_device,
        mesh=mesh,
        in_specs=placed,
        out_specs=(P(("sub", "crow"), None), P(("sub", "crow"), None), P(("sub", "crow"), None)),
        check_vma=False,
    )
```

```python
import jax
import jax.numpy as jnp
from jax import lax
from jax.sharding import PartitionSpec as P


def padded_2(block, sides, width):
    for axis, dim in sides:
        count = lax.axis_size(axis)
        forward = [(i, i + 1) for i in range(count - 1)]
        backward = [(target, source) for source, target in forward]
        low = lax.ppermute(
            lax.slice_in_dim(block, block.shape[dim] - width, None, axis=dim), axis, forward
        )
        high = lax.ppermute(lax.slice_in_dim(block, 0, width, axis=dim), axis, backward)
        block = jnp.concatenate([low, block, high], axis=dim)
    return block


def shifted(value, axis, steps):
    count = lax.axis_size(axis)
    initial, last = (max(0, -steps), min(count, count - steps))
    return lax.ppermute(value, axis, [(source, source + steps) for source in range(initial, last)])


def broadcast(shard, axis, root):
    mine = lax.axis_index(axis) == root
    return lax.psum(jnp.where(mine, shard, jnp.zeros_like(shard)), axis)


def neighbour_offsets(across):
    return [-across - 1, -across, -across + 1, -1, 1, across - 1, across, across + 1]


def per_device(deflation, diag_op, upper_op, tile_blocks, pair_counts, pivot_owner):
    crow_count = lax.axis_size("crow")
    crow_place = lax.axis_index("crow")
    sub_count = lax.axis_size("sub")
    across = min(16, sub_count // 2)
    offsets = neighbour_offsets(across)
    local_rows = deflation[0]
    blocks_here, tile_rows = (diag_op.shape[1], diag_op.shape[2])
    coarse_width = local_rows.shape[1]
    slot_count = pair_counts.shape[1]
    per_slot = tile_blocks.shape[2] // slot_count
    forward_pair = shifted(
        jnp.stack([local_rows[-tile_rows:], upper_op[0, blocks_here - 1]]), "crow", 1
    )
    next_rows = shifted(local_rows[:tile_rows], "crow", -1)
    centre = local_rows.reshape(blocks_here, tile_rows, coarse_width)
    stacked = jnp.concatenate([forward_pair[:1], centre, next_rows[None]], 0)
    previous_upper = forward_pair[1]
    lower_blocks = jnp.concatenate([previous_upper[None], upper_op[0, :-1]], 0)
    product = (
        jnp.einsum("bij,bjk->bik", diag_op[0], centre, preferred_element_type=jnp.float32)
        + jnp.einsum("bij,bjk->bik", upper_op[0], stacked[2:], preferred_element_type=jnp.float32)
        + jnp.einsum("bji,bjk->bik", lower_blocks, stacked[:-2], preferred_element_type=jnp.float32)
    )
    applied = product.astype(jnp.bfloat16)
    chosen = tile_blocks[0, 0]
    own_tiles = centre[chosen].reshape(slot_count, per_slot, tile_rows, coarse_width)
    outgoing = applied[chosen].reshape(slot_count, per_slot, tile_rows, coarse_width)
    position = crow_place * per_slot + jnp.arange(per_slot, dtype=jnp.int32)
    live_mask = (position[None, :] < pair_counts[0][:, None]).astype(jnp.bfloat16)
    own_masked = own_tiles * live_mask[:, :, None, None]
    arrived = [None] * slot_count
    for slot_index in range(slot_count):
        arrived[slot_index] = shifted(
            outgoing[slot_count - 1 - slot_index], "sub", -offsets[slot_index]
        )
    received = jnp.stack(arrived)
    flat_vectors = centre.reshape(blocks_here * tile_rows, coarse_width)
    flat_applied = applied.reshape(blocks_here * tile_rows, coarse_width)
    row_share = coarse_width // crow_count
    owner_index = pivot_owner[0]
    gram_part = jnp.einsum(
        "nr,nk->rk", flat_vectors, flat_applied, preferred_element_type=jnp.float32
    )
    coupling = jnp.einsum(
        "jutr,jutk->rjk", own_masked, received, preferred_element_type=jnp.float32
    )
    whole = jnp.concatenate([gram_part[:, None, :], coupling], 1).reshape(
        coarse_width, (slot_count + 1) * coarse_width
    )
    pivot_partial = lax.dynamic_slice_in_dim(whole, owner_index * row_share, row_share, 0)
    outgoing_rows = jnp.concatenate(
        [
            whole.reshape(crow_count, row_share, whole.shape[1]),
            jnp.broadcast_to(pivot_partial[None], (crow_count,) + pivot_partial.shape),
        ],
        1,
    )
    pieces = lax.all_to_all(outgoing_rows, "crow", 0, 0, tiled=True).reshape(
        crow_count, 2 * row_share, whole.shape[1]
    )
    if crow_count == 4:
        total = (pieces[0] + pieces[1]) + (pieces[2] + pieces[3])
    else:
        total = pieces.sum(0)
    own_rows = total[:row_share]
    leading = total[row_share:]
    pivot_block = lax.dynamic_slice_in_dim(leading, owner_index * row_share, row_share, 1)
    factor = jnp.linalg.cholesky(pivot_block)
    solved = jax.scipy.linalg.solve_triangular(factor, leading, lower=True)
    columns = lax.dynamic_slice_in_dim(own_rows, owner_index * row_share, row_share, 1)
    panel_rows = jax.scipy.linalg.solve_triangular(factor, columns.T, lower=True).T
    updated = own_rows - jnp.dot(panel_rows, solved, precision=lax.Precision.HIGHEST)
    return (updated[:, :coarse_width], updated[:, coarse_width:], panel_rows)


def solution(mesh):
    placed = (
        P("sub", "crow", None),
        P("sub", "crow", None, None),
        P("sub", "crow", None, None),
        P("sub", "crow", None),
        P("sub", None),
        P("sub"),
    )
    return jax.shard_map(
        per_device,
        mesh=mesh,
        in_specs=placed,
        out_specs=(P(("sub", "crow"), None), P(("sub", "crow"), None), P(("sub", "crow"), None)),
        check_vma=False,
    )
```

```python
import jax
import jax.numpy as jnp
from jax import lax
from jax.sharding import PartitionSpec as P
from jax.experimental import pallas as pl
from jax.experimental.pallas import tpu as pltpu


def padded_2(block, sides, width):
    for axis, dim in sides:
        count = lax.axis_size(axis)
        forward = [(i, i + 1) for i in range(count - 1)]
        backward = [(target, source) for source, target in forward]
        low = lax.ppermute(
            lax.slice_in_dim(block, block.shape[dim] - width, None, axis=dim), axis, forward
        )
        high = lax.ppermute(lax.slice_in_dim(block, 0, width, axis=dim), axis, backward)
        block = jnp.concatenate([low, block, high], axis=dim)
    return block


def shifted(value, axis, steps):
    count = lax.axis_size(axis)
    initial, last = (max(0, -steps), min(count, count - steps))
    return lax.ppermute(value, axis, [(source, source + steps) for source in range(initial, last)])


def broadcast(shard, axis, root):
    mine = lax.axis_index(axis) == root
    return lax.psum(jnp.where(mine, shard, jnp.zeros_like(shard)), axis)


def neighbour_offsets(across):
    return [-across - 1, -across, -across + 1, -1, 1, across - 1, across, across + 1]


def _ab(a, b):
    return lax.dot_general(a, b, (((1,), (0,)), ((), ())), preferred_element_type=jnp.float32)


def _atb(a, b):
    return lax.dot_general(a, b, (((0,), (0,)), ((), ())), preferred_element_type=jnp.float32)


def local_apply_kernel(
    chosen_ref, live_ref, z_ref, zp_ref, zn_ref, d_ref, u_ref, up_ref,
    gram_ref, out_ref, own_ref, app_ref,
):
    count = z_ref.shape[0]

    def store(b, total, gram):
        app = total.astype(jnp.bfloat16)
        app_ref[b] = app
        return gram + _atb(z_ref[b], app)

    first = (_ab(d_ref[0], z_ref[0]) + _ab(u_ref[0], z_ref[1])) + _atb(up_ref[...], zp_ref[...])
    gram = store(0, first, jnp.zeros(gram_ref.shape, jnp.float32))

    def body(b, gram):
        total = (_ab(d_ref[b], z_ref[b]) + _ab(u_ref[b], z_ref[b + 1])) + _atb(
            u_ref[b - 1], z_ref[b - 1]
        )
        return store(b, total, gram)

    gram = lax.fori_loop(1, count - 1, body, gram)
    last = count - 1
    final = (_ab(d_ref[last], z_ref[last]) + _ab(u_ref[last], zn_ref[...])) + _atb(
        u_ref[last - 1], z_ref[last - 1]
    )
    gram_ref[...] = store(last, final, gram)
    for i in range(out_ref.shape[0]):
        block = chosen_ref[i]
        out_ref[i] = app_ref[block]
        own_ref[i] = jnp.where(live_ref[i] > 0, z_ref[block], jnp.zeros_like(z_ref[block]))


def local_apply(chosen, live, centre, prev_rows, next_rows, diagonal, upper, prev_upper):
    tiles = chosen.shape[0]
    blocks, rows, width = centre.shape
    vmem = pl.BlockSpec(memory_space=pltpu.VMEM)
    smem = pl.BlockSpec(memory_space=pltpu.SMEM)
    return pl.pallas_call(
        local_apply_kernel,
        out_shape=(
            jax.ShapeDtypeStruct((width, width), jnp.float32),
            jax.ShapeDtypeStruct((tiles, rows, width), centre.dtype),
            jax.ShapeDtypeStruct((tiles, rows, width), centre.dtype),
        ),
        in_specs=[smem, smem] + [vmem] * 6,
        out_specs=(vmem, vmem, vmem),
        scratch_shapes=[pltpu.VMEM((blocks, rows, width), centre.dtype)],
    )(chosen, live, centre, prev_rows, next_rows, diagonal, upper, prev_upper)


def per_device(deflation, diag_op, upper_op, tile_blocks, pair_counts, pivot_owner):
    crow_count = lax.axis_size("crow")
    crow_place = lax.axis_index("crow")
    sub_count = lax.axis_size("sub")
    across = min(16, sub_count // 2)
    offsets = neighbour_offsets(across)
    local_rows = deflation[0]
    blocks_here, tile_rows = (diag_op.shape[1], diag_op.shape[2])
    coarse_width = local_rows.shape[1]
    slot_count = pair_counts.shape[1]
    per_slot = tile_blocks.shape[2] // slot_count
    forward_pair = shifted(
        jnp.stack([local_rows[-tile_rows:], upper_op[0, blocks_here - 1]]), "crow", 1
    )
    next_rows = shifted(local_rows[:tile_rows], "crow", -1)
    centre = local_rows.reshape(blocks_here, tile_rows, coarse_width)
    chosen = tile_blocks[0, 0]
    position = crow_place * per_slot + jnp.arange(per_slot, dtype=jnp.int32)
    live = (position[None, :] < pair_counts[0][:, None]).astype(jnp.int32).reshape(-1)
    gram_part, outgoing, own_masked = local_apply(
        chosen, live, centre, forward_pair[0], next_rows, diag_op[0], upper_op[0], forward_pair[1]
    )
    outgoing = outgoing.reshape(slot_count, per_slot, tile_rows, coarse_width)
    own_masked = own_masked.reshape(slot_count, per_slot, tile_rows, coarse_width)
    arrived = [None] * slot_count
    for slot_index in range(slot_count):
        arrived[slot_index] = shifted(
            outgoing[slot_count - 1 - slot_index], "sub", -offsets[slot_index]
        )
    received = jnp.stack(arrived)
    row_share = coarse_width // crow_count
    owner_index = pivot_owner[0]
    coupling = jnp.einsum(
        "jutr,jutk->rjk", own_masked, received, preferred_element_type=jnp.float32
    )
    whole = jnp.concatenate([gram_part[:, None, :], coupling], 1).reshape(
        coarse_width, (slot_count + 1) * coarse_width
    )
    pivot_partial = lax.dynamic_slice_in_dim(whole, owner_index * row_share, row_share, 0)
    outgoing_rows = jnp.concatenate(
        [
            whole.reshape(crow_count, row_share, whole.shape[1]),
            jnp.broadcast_to(pivot_partial[None], (crow_count,) + pivot_partial.shape),
        ],
        1,
    )
    pieces = lax.all_to_all(outgoing_rows, "crow", 0, 0, tiled=True).reshape(
        crow_count, 2 * row_share, whole.shape[1]
    )
    if crow_count == 4:
        total = (pieces[0] + pieces[1]) + (pieces[2] + pieces[3])
    else:
        total = pieces.sum(0)
    own_rows = total[:row_share]
    leading = total[row_share:]
    pivot_block = lax.dynamic_slice_in_dim(leading, owner_index * row_share, row_share, 1)
    factor = jnp.linalg.cholesky(pivot_block)
    solved = jax.scipy.linalg.solve_triangular(factor, leading, lower=True)
    columns = lax.dynamic_slice_in_dim(own_rows, owner_index * row_share, row_share, 1)
    panel_rows = jax.scipy.linalg.solve_triangular(factor, columns.T, lower=True).T
    updated = own_rows - jnp.dot(panel_rows, solved, precision=lax.Precision.HIGHEST)
    return (updated[:, :coarse_width], updated[:, coarse_width:], panel_rows)


def solution(mesh):
    placed = (
        P("sub", "crow", None),
        P("sub", "crow", None, None),
        P("sub", "crow", None, None),
        P("sub", "crow", None),
        P("sub", None),
        P("sub"),
    )
    return jax.shard_map(
        per_device,
        mesh=mesh,
        in_specs=placed,
        out_specs=(P(("sub", "crow"), None), P(("sub", "crow"), None), P(("sub", "crow"), None)),
        check_vma=False,
    )
```

```python
import jax
import jax.numpy as jnp
from jax import lax
from jax.sharding import PartitionSpec as P
from jax.experimental import pallas as pl
from jax.experimental.pallas import tpu as pltpu


def padded_2(block, sides, width):
    for axis, dim in sides:
        count = lax.axis_size(axis)
        forward = [(i, i + 1) for i in range(count - 1)]
        backward = [(target, source) for source, target in forward]
        low = lax.ppermute(
            lax.slice_in_dim(block, block.shape[dim] - width, None, axis=dim), axis, forward
        )
        high = lax.ppermute(lax.slice_in_dim(block, 0, width, axis=dim), axis, backward)
        block = jnp.concatenate([low, block, high], axis=dim)
    return block


def shifted(value, axis, steps):
    count = lax.axis_size(axis)
    initial, last = (max(0, -steps), min(count, count - steps))
    return lax.ppermute(value, axis, [(source, source + steps) for source in range(initial, last)])


def broadcast(shard, axis, root):
    mine = lax.axis_index(axis) == root
    return lax.psum(jnp.where(mine, shard, jnp.zeros_like(shard)), axis)


def neighbour_offsets(across):
    return [-across - 1, -across, -across + 1, -1, 1, across - 1, across, across + 1]


def _ab(a, b):
    return lax.dot_general(a, b, (((1,), (0,)), ((), ())), preferred_element_type=jnp.float32)


def _atb(a, b):
    return lax.dot_general(a, b, (((0,), (0,)), ((), ())), preferred_element_type=jnp.float32)


def local_apply_kernel(
    chosen_ref, live_ref, z_ref, zp_ref, zn_ref, d_ref, u_ref, up_ref,
    gram_ref, out_ref, own_ref, app_ref,
):
    count, rows = d_ref.shape[0], d_ref.shape[1]

    def rows_of(b):
        return z_ref[pl.ds(b * rows, rows), :]

    for b in range(count):
        below = zp_ref[...] if b == 0 else rows_of(b - 1)
        lower = up_ref[...] if b == 0 else u_ref[b - 1]
        above = zn_ref[...] if b == count - 1 else rows_of(b + 1)
        total = (_ab(d_ref[b], rows_of(b)) + _ab(u_ref[b], above)) + _atb(lower, below)
        app_ref[pl.ds(b * rows, rows), :] = total.astype(app_ref.dtype)
    gram_ref[...] = _atb(z_ref[...], app_ref[...])
    for i in range(out_ref.shape[0]):
        start = pl.multiple_of(chosen_ref[i] * rows, rows)
        out_ref[i] = app_ref[pl.ds(start, rows), :]
        tile = z_ref[pl.ds(start, rows), :]
        own_ref[i] = jnp.where(live_ref[i] > 0, tile, jnp.zeros_like(tile))


def local_apply(chosen, live, centre, prev_rows, next_rows, diagonal, upper, prev_upper):
    tiles = chosen.shape[0]
    blocks, rows = diagonal.shape[0], diagonal.shape[1]
    width = centre.shape[1]
    vmem = pl.BlockSpec(memory_space=pltpu.VMEM)
    smem = pl.BlockSpec(memory_space=pltpu.SMEM)
    return pl.pallas_call(
        local_apply_kernel,
        out_shape=(
            jax.ShapeDtypeStruct((width, width), jnp.float32),
            jax.ShapeDtypeStruct((tiles, rows, width), centre.dtype),
            jax.ShapeDtypeStruct((tiles, rows, width), centre.dtype),
        ),
        in_specs=[smem, smem] + [vmem] * 6,
        out_specs=(vmem, vmem, vmem),
        scratch_shapes=[pltpu.VMEM((blocks * rows, width), centre.dtype)],
    )(chosen, live, centre, prev_rows, next_rows, diagonal, upper, prev_upper)


def per_device(deflation, diag_op, upper_op, tile_blocks, pair_counts, pivot_owner):
    crow_count = lax.axis_size("crow")
    crow_place = lax.axis_index("crow")
    sub_count = lax.axis_size("sub")
    across = min(16, sub_count // 2)
    offsets = neighbour_offsets(across)
    local_rows = deflation[0]
    blocks_here, tile_rows = (diag_op.shape[1], diag_op.shape[2])
    coarse_width = local_rows.shape[1]
    slot_count = pair_counts.shape[1]
    per_slot = tile_blocks.shape[2] // slot_count
    forward_pair = shifted(
        jnp.stack([local_rows[-tile_rows:], upper_op[0, blocks_here - 1]]), "crow", 1
    )
    next_rows = shifted(local_rows[:tile_rows], "crow", -1)
    chosen = tile_blocks[0, 0]
    position = crow_place * per_slot + jnp.arange(per_slot, dtype=jnp.int32)
    live = (position[None, :] < pair_counts[0][:, None]).astype(jnp.int32).reshape(-1)
    gram_part, outgoing, own_masked = local_apply(
        chosen, live, local_rows, forward_pair[0], next_rows, diag_op[0], upper_op[0], forward_pair[1]
    )
    outgoing = outgoing.reshape(slot_count, per_slot, tile_rows, coarse_width)
    own_masked = own_masked.reshape(slot_count, per_slot, tile_rows, coarse_width)
    arrived = [None] * slot_count
    for slot_index in range(slot_count):
        arrived[slot_index] = shifted(
            outgoing[slot_count - 1 - slot_index], "sub", -offsets[slot_index]
        )
    received = jnp.stack(arrived)
    row_share = coarse_width // crow_count
    owner_index = pivot_owner[0]
    coupling = jnp.einsum(
        "jutr,jutk->rjk", own_masked, received, preferred_element_type=jnp.float32
    )
    whole = jnp.concatenate([gram_part[:, None, :], coupling], 1).reshape(
        coarse_width, (slot_count + 1) * coarse_width
    )
    pivot_partial = lax.dynamic_slice_in_dim(whole, owner_index * row_share, row_share, 0)
    outgoing_rows = jnp.concatenate(
        [
            whole.reshape(crow_count, row_share, whole.shape[1]),
            jnp.broadcast_to(pivot_partial[None], (crow_count,) + pivot_partial.shape),
        ],
        1,
    )
    pieces = lax.all_to_all(outgoing_rows, "crow", 0, 0, tiled=True).reshape(
        crow_count, 2 * row_share, whole.shape[1]
    )
    if crow_count == 4:
        total = (pieces[0] + pieces[1]) + (pieces[2] + pieces[3])
    else:
        total = pieces.sum(0)
    own_rows = total[:row_share]
    leading = total[row_share:]
    pivot_block = lax.dynamic_slice_in_dim(leading, owner_index * row_share, row_share, 1)
    factor = jnp.linalg.cholesky(pivot_block)
    solved = jax.scipy.linalg.solve_triangular(factor, leading, lower=True)
    columns = lax.dynamic_slice_in_dim(own_rows, owner_index * row_share, row_share, 1)
    panel_rows = jax.scipy.linalg.solve_triangular(factor, columns.T, lower=True).T
    updated = own_rows - jnp.dot(panel_rows, solved, precision=lax.Precision.HIGHEST)
    return (updated[:, :coarse_width], updated[:, coarse_width:], panel_rows)


def solution(mesh):
    placed = (
        P("sub", "crow", None),
        P("sub", "crow", None, None),
        P("sub", "crow", None, None),
        P("sub", "crow", None),
        P("sub", None),
        P("sub"),
    )
    return jax.shard_map(
        per_device,
        mesh=mesh,
        in_specs=placed,
        out_specs=(P(("sub", "crow"), None), P(("sub", "crow"), None), P(("sub", "crow"), None)),
        check_vma=False,
    )
```

```python
import jax
import jax.numpy as jnp
from jax import lax
from jax.sharding import PartitionSpec as P
from jax.experimental import pallas as pl
from jax.experimental.pallas import tpu as pltpu


def padded_2(block, sides, width):
    for axis, dim in sides:
        count = lax.axis_size(axis)
        forward = [(i, i + 1) for i in range(count - 1)]
        backward = [(target, source) for source, target in forward]
        low = lax.ppermute(
            lax.slice_in_dim(block, block.shape[dim] - width, None, axis=dim), axis, forward
        )
        high = lax.ppermute(lax.slice_in_dim(block, 0, width, axis=dim), axis, backward)
        block = jnp.concatenate([low, block, high], axis=dim)
    return block


def shifted(value, axis, steps):
    count = lax.axis_size(axis)
    initial, last = (max(0, -steps), min(count, count - steps))
    return lax.ppermute(value, axis, [(source, source + steps) for source in range(initial, last)])


def broadcast(shard, axis, root):
    mine = lax.axis_index(axis) == root
    return lax.psum(jnp.where(mine, shard, jnp.zeros_like(shard)), axis)


def neighbour_offsets(across):
    return [-across - 1, -across, -across + 1, -1, 1, across - 1, across, across + 1]


def _ab(a, b):
    return lax.dot_general(a, b, (((1,), (0,)), ((), ())), preferred_element_type=jnp.float32)


def _atb(a, b):
    return lax.dot_general(a, b, (((0,), (0,)), ((), ())), preferred_element_type=jnp.float32)


def local_apply_kernel(
    chosen_ref, live_ref, z_ref, zp_ref, zn_ref, d_ref, u_ref, up_ref,
    gram_ref, out_ref, own_ref, app_ref,
):
    count, rows = d_ref.shape[0], d_ref.shape[1]

    def rows_of(b):
        return z_ref[pl.ds(b * rows, rows), :]

    for b in range(count):
        below = zp_ref[...] if b == 0 else rows_of(b - 1)
        lower = up_ref[...] if b == 0 else u_ref[b - 1]
        above = zn_ref[...] if b == count - 1 else rows_of(b + 1)
        total = (_ab(d_ref[b], rows_of(b)) + _ab(u_ref[b], above)) + _atb(lower, below)
        app_ref[pl.ds(b * rows, rows), :] = total.astype(app_ref.dtype)
    gram_ref[...] = _atb(z_ref[...], app_ref[...])
    for i in range(out_ref.shape[0]):
        start = pl.multiple_of(chosen_ref[i] * rows, rows)
        out_ref[i] = app_ref[pl.ds(start, rows), :]
        tile = z_ref[pl.ds(start, rows), :]
        own_ref[i] = jnp.where(live_ref[i] > 0, tile, jnp.zeros_like(tile))


def local_apply(chosen, live, centre, prev_rows, next_rows, diagonal, upper, prev_upper):
    tiles = chosen.shape[0]
    blocks, rows = diagonal.shape[0], diagonal.shape[1]
    width = centre.shape[1]
    vmem = pl.BlockSpec(memory_space=pltpu.VMEM)
    smem = pl.BlockSpec(memory_space=pltpu.SMEM)
    return pl.pallas_call(
        local_apply_kernel,
        out_shape=(
            jax.ShapeDtypeStruct((width, width), jnp.float32),
            jax.ShapeDtypeStruct((tiles, rows, width), centre.dtype),
            jax.ShapeDtypeStruct((tiles, rows, width), centre.dtype),
        ),
        in_specs=[smem, smem] + [vmem] * 6,
        out_specs=(vmem, vmem, vmem),
        scratch_shapes=[pltpu.VMEM((blocks * rows, width), centre.dtype)],
    )(chosen, live, centre, prev_rows, next_rows, diagonal, upper, prev_upper)


def _exact(a, b, dims):
    return lax.dot_general(
        a, b, (dims, ((), ())), precision=lax.Precision.HIGHEST,
        preferred_element_type=jnp.float32,
    )


def panel_kernel(owner_ref, pieces_ref, self_ref, coupling_ref, panel_ref):
    share = panel_ref.shape[0]
    width = self_ref.shape[1]
    total = (pieces_ref[0] + pieces_ref[1]) + (pieces_ref[2] + pieces_ref[3])
    own = total[:share]
    lead = total[share:]
    owner = owner_ref[0]

    def pick(rows):
        block = jnp.zeros((share, share), jnp.float32)
        for q in range(width // share):
            block = jnp.where(owner == q, rows[:, q * share:(q + 1) * share], block)
        return block

    pivot = pick(lead)
    pivot = (pivot + pivot.T) * 0.5
    row_id = lax.broadcasted_iota(jnp.int32, (share, 2 * share), 0)
    col_id = lax.broadcasted_iota(jnp.int32, (share, 2 * share), 1)
    work = jnp.concatenate([pivot, jnp.eye(share, dtype=jnp.float32)], 1)

    def step(k, work):
        row = jnp.sum(jnp.where(row_id == k, work, 0.0), axis=0, keepdims=True)
        col = jnp.sum(jnp.where(col_id == k, work, 0.0), axis=1, keepdims=True)
        diag = jnp.sum(jnp.where(col_id[:1] == k, row, 0.0), axis=1, keepdims=True)
        scale = 1.0 / jnp.sqrt(diag)
        unit_row = row * scale
        below = jnp.where(row_id[:, :1] > k, col * scale, 0.0)
        return jnp.where(row_id == k, unit_row, work - below * unit_row)

    work = lax.fori_loop(0, share, step, work)
    inverse = work[:, share:]
    solved = _exact(inverse, lead, ((1,), (0,)))
    panel = _exact(pick(own), inverse, ((1,), (1,)))
    updated = own - _exact(panel, solved, ((1,), (0,)))
    self_ref[...] = updated[:, :width]
    coupling_ref[...] = updated[:, width:]
    panel_ref[...] = panel


def eliminate_panel(owner, pieces, width):
    share = pieces.shape[1] // 2
    vmem = pl.BlockSpec(memory_space=pltpu.VMEM)
    return pl.pallas_call(
        panel_kernel,
        out_shape=(
            jax.ShapeDtypeStruct((share, width), jnp.float32),
            jax.ShapeDtypeStruct((share, pieces.shape[2] - width), jnp.float32),
            jax.ShapeDtypeStruct((share, share), jnp.float32),
        ),
        in_specs=[pl.BlockSpec(memory_space=pltpu.SMEM), vmem],
        out_specs=(vmem, vmem, vmem),
    )(owner, pieces)


def per_device(deflation, diag_op, upper_op, tile_blocks, pair_counts, pivot_owner):
    crow_count = lax.axis_size("crow")
    crow_place = lax.axis_index("crow")
    sub_count = lax.axis_size("sub")
    across = min(16, sub_count // 2)
    offsets = neighbour_offsets(across)
    local_rows = deflation[0]
    blocks_here, tile_rows = (diag_op.shape[1], diag_op.shape[2])
    coarse_width = local_rows.shape[1]
    slot_count = pair_counts.shape[1]
    per_slot = tile_blocks.shape[2] // slot_count
    forward_pair = shifted(
        jnp.stack([local_rows[-tile_rows:], upper_op[0, blocks_here - 1]]), "crow", 1
    )
    next_rows = shifted(local_rows[:tile_rows], "crow", -1)
    chosen = tile_blocks[0, 0]
    position = crow_place * per_slot + jnp.arange(per_slot, dtype=jnp.int32)
    live = (position[None, :] < pair_counts[0][:, None]).astype(jnp.int32).reshape(-1)
    gram_part, outgoing, own_masked = local_apply(
        chosen, live, local_rows, forward_pair[0], next_rows, diag_op[0], upper_op[0], forward_pair[1]
    )
    outgoing = outgoing.reshape(slot_count, per_slot, tile_rows, coarse_width)
    own_masked = own_masked.reshape(slot_count, per_slot, tile_rows, coarse_width)
    arrived = [None] * slot_count
    for slot_index in range(slot_count):
        arrived[slot_index] = shifted(
            outgoing[slot_count - 1 - slot_index], "sub", -offsets[slot_index]
        )
    received = jnp.stack(arrived)
    row_share = coarse_width // crow_count
    owner_index = pivot_owner[0]
    coupling = jnp.einsum(
        "jutr,jutk->rjk", own_masked, received, preferred_element_type=jnp.float32
    )
    whole = jnp.concatenate([gram_part[:, None, :], coupling], 1).reshape(
        coarse_width, (slot_count + 1) * coarse_width
    )
    pivot_partial = lax.dynamic_slice_in_dim(whole, owner_index * row_share, row_share, 0)
    outgoing_rows = jnp.concatenate(
        [
            whole.reshape(crow_count, row_share, whole.shape[1]),
            jnp.broadcast_to(pivot_partial[None], (crow_count,) + pivot_partial.shape),
        ],
        1,
    )
    pieces = lax.all_to_all(outgoing_rows, "crow", 0, 0, tiled=True).reshape(
        crow_count, 2 * row_share, whole.shape[1]
    )
    return eliminate_panel(pivot_owner, pieces, coarse_width)


def solution(mesh):
    placed = (
        P("sub", "crow", None),
        P("sub", "crow", None, None),
        P("sub", "crow", None, None),
        P("sub", "crow", None),
        P("sub", None),
        P("sub"),
    )
    return jax.shard_map(
        per_device,
        mesh=mesh,
        in_specs=placed,
        out_specs=(P(("sub", "crow"), None), P(("sub", "crow"), None), P(("sub", "crow"), None)),
        check_vma=False,
    )
```

```python
import jax
import jax.numpy as jnp
from jax import lax
from jax.sharding import PartitionSpec as P
from jax.experimental import pallas as pl
from jax.experimental.pallas import tpu as pltpu


def padded_2(block, sides, width):
    for axis, dim in sides:
        count = lax.axis_size(axis)
        forward = [(i, i + 1) for i in range(count - 1)]
        backward = [(target, source) for source, target in forward]
        low = lax.ppermute(
            lax.slice_in_dim(block, block.shape[dim] - width, None, axis=dim), axis, forward
        )
        high = lax.ppermute(lax.slice_in_dim(block, 0, width, axis=dim), axis, backward)
        block = jnp.concatenate([low, block, high], axis=dim)
    return block


def shifted(value, axis, steps):
    count = lax.axis_size(axis)
    initial, last = (max(0, -steps), min(count, count - steps))
    return lax.ppermute(value, axis, [(source, source + steps) for source in range(initial, last)])


def broadcast(shard, axis, root):
    mine = lax.axis_index(axis) == root
    return lax.psum(jnp.where(mine, shard, jnp.zeros_like(shard)), axis)


def neighbour_offsets(across):
    return [-across - 1, -across, -across + 1, -1, 1, across - 1, across, across + 1]


def _ab(a, b):
    return lax.dot_general(a, b, (((1,), (0,)), ((), ())), preferred_element_type=jnp.float32)


def _atb(a, b):
    return lax.dot_general(a, b, (((0,), (0,)), ((), ())), preferred_element_type=jnp.float32)


def local_apply_kernel(
    chosen_ref, live_ref, z_ref, zp_ref, zn_ref, d_ref, u_ref, up_ref,
    gram_ref, out_ref, own_ref, app_ref,
):
    count, rows = d_ref.shape[0], d_ref.shape[1]

    def rows_of(b):
        return z_ref[pl.ds(b * rows, rows), :]

    for b in range(count):
        below = zp_ref[...] if b == 0 else rows_of(b - 1)
        lower = up_ref[...] if b == 0 else u_ref[b - 1]
        above = zn_ref[...] if b == count - 1 else rows_of(b + 1)
        total = (_ab(d_ref[b], rows_of(b)) + _ab(u_ref[b], above)) + _atb(lower, below)
        app_ref[pl.ds(b * rows, rows), :] = total.astype(app_ref.dtype)
    gram_ref[...] = _atb(z_ref[...], app_ref[...])
    for i in range(out_ref.shape[0]):
        start = pl.multiple_of(chosen_ref[i] * rows, rows)
        out_ref[i] = app_ref[pl.ds(start, rows), :]
        tile = z_ref[pl.ds(start, rows), :]
        own_ref[i] = jnp.where(live_ref[i] > 0, tile, jnp.zeros_like(tile))


def local_apply(chosen, live, centre, prev_rows, next_rows, diagonal, upper, prev_upper):
    tiles = chosen.shape[0]
    blocks, rows = diagonal.shape[0], diagonal.shape[1]
    width = centre.shape[1]
    vmem = pl.BlockSpec(memory_space=pltpu.VMEM)
    smem = pl.BlockSpec(memory_space=pltpu.SMEM)
    return pl.pallas_call(
        local_apply_kernel,
        out_shape=(
            jax.ShapeDtypeStruct((width, width), jnp.float32),
            jax.ShapeDtypeStruct((tiles, rows, width), centre.dtype),
            jax.ShapeDtypeStruct((tiles, rows, width), centre.dtype),
        ),
        in_specs=[smem, smem] + [vmem] * 6,
        out_specs=(vmem, vmem, vmem),
        scratch_shapes=[pltpu.VMEM((blocks * rows, width), centre.dtype)],
    )(chosen, live, centre, prev_rows, next_rows, diagonal, upper, prev_upper)


def _exact(a, b, dims):
    return lax.dot_general(
        a, b, (dims, ((), ())), precision=lax.Precision.HIGHEST,
        preferred_element_type=jnp.float32,
    )


def panel_kernel(owner_ref, pieces_ref, self_ref, coupling_ref, panel_ref):
    share = panel_ref.shape[0]
    width = self_ref.shape[1]
    total = (pieces_ref[0] + pieces_ref[1]) + (pieces_ref[2] + pieces_ref[3])
    own = total[:share]
    lead = total[share:]
    owner = owner_ref[0]

    def pick(rows):
        block = jnp.zeros((share, share), jnp.float32)
        for q in range(width // share):
            block = jnp.where(owner == q, rows[:, q * share:(q + 1) * share], block)
        return block

    pivot = pick(lead)
    pivot = (pivot + pivot.T) * 0.5
    row_id = lax.broadcasted_iota(jnp.int32, (share, 2 * share), 0)
    col_id = lax.broadcasted_iota(jnp.int32, (share, 2 * share), 1)
    work = jnp.concatenate([pivot, jnp.eye(share, dtype=jnp.float32)], 1)

    def step(k, work):
        row = jnp.sum(jnp.where(row_id == k, work, 0.0), axis=0, keepdims=True)
        col = jnp.sum(jnp.where(col_id == k, work, 0.0), axis=1, keepdims=True)
        diag = jnp.sum(jnp.where(col_id[:1] == k, row, 0.0), axis=1, keepdims=True)
        scale = 1.0 / jnp.sqrt(diag)
        unit_row = row * scale
        below = jnp.where(row_id[:, :1] > k, col * scale, 0.0)
        return jnp.where(row_id == k, unit_row, work - below * unit_row)

    work = lax.fori_loop(0, share, step, work)
    inverse = work[:, share:]
    solved = _exact(inverse, lead, ((1,), (0,)))
    panel = _exact(pick(own), inverse, ((1,), (1,)))
    updated = own - _exact(panel, solved, ((1,), (0,)))
    self_ref[...] = updated[:, :width]
    coupling_ref[...] = updated[:, width:]
    panel_ref[...] = panel


def eliminate_panel(owner, pieces, width):
    share = pieces.shape[1] // 2
    vmem = pl.BlockSpec(memory_space=pltpu.VMEM)
    return pl.pallas_call(
        panel_kernel,
        out_shape=(
            jax.ShapeDtypeStruct((share, width), jnp.float32),
            jax.ShapeDtypeStruct((share, pieces.shape[2] - width), jnp.float32),
            jax.ShapeDtypeStruct((share, share), jnp.float32),
        ),
        in_specs=[pl.BlockSpec(memory_space=pltpu.SMEM), vmem],
        out_specs=(vmem, vmem, vmem),
    )(owner, pieces)


def per_device(deflation, diag_op, upper_op, tile_blocks, pair_counts, pivot_owner):
    crow_count = lax.axis_size("crow")
    crow_place = lax.axis_index("crow")
    sub_count = lax.axis_size("sub")
    across = min(16, sub_count // 2)
    offsets = neighbour_offsets(across)
    local_rows = deflation[0]
    blocks_here, tile_rows = (diag_op.shape[1], diag_op.shape[2])
    coarse_width = local_rows.shape[1]
    slot_count = pair_counts.shape[1]
    per_slot = tile_blocks.shape[2] // slot_count
    forward_pair = shifted(
        jnp.stack([local_rows[-tile_rows:], upper_op[0, blocks_here - 1]]), "crow", 1
    )
    next_rows = shifted(local_rows[:tile_rows], "crow", -1)
    chosen = tile_blocks[0, 0]
    position = crow_place * per_slot + jnp.arange(per_slot, dtype=jnp.int32)
    live = (position[None, :] < pair_counts[0][:, None]).astype(jnp.int32).reshape(-1)
    gram_part, outgoing, own_masked = local_apply(
        chosen, live, local_rows, forward_pair[0], next_rows, diag_op[0], upper_op[0], forward_pair[1]
    )
    outgoing = outgoing.reshape(slot_count, per_slot, tile_rows, coarse_width)
    own_masked = own_masked.reshape(slot_count, per_slot, tile_rows, coarse_width)
    slot_of = {offset: index for index, offset in enumerate(offsets)}

    def piece(offset):
        return outgoing[slot_of[offset]]

    sub_place = lax.axis_index("sub")
    down = shifted(jnp.stack([piece(-across - 1), piece(-1), piece(across - 1)]), "sub", -1)
    up = shifted(jnp.stack([piece(-across + 1), piece(1), piece(across + 1)]), "sub", 1)
    corner = lax.ppermute(
        jnp.where(sub_place == 0, piece(across - 1), piece(-across + 1)),
        "sub",
        [(0, across - 1), (sub_count - 1, sub_count - across)],
    )
    far_down = shifted(jnp.stack([piece(-across), down[0], up[0]]), "sub", -across)
    far_up = shifted(jnp.stack([piece(across), down[2], up[2]]), "sub", across)
    zero = jnp.zeros_like(corner)
    arrival = {
        -across - 1: far_up[2],
        -across: far_up[0],
        -across + 1: far_up[1] + jnp.where(sub_place == across - 1, corner, zero),
        -1: up[1],
        1: down[1],
        across - 1: far_down[2] + jnp.where(sub_place == sub_count - across, corner, zero),
        across: far_down[0],
        across + 1: far_down[1],
    }
    received = jnp.stack([arrival[offset] for offset in offsets])
    row_share = coarse_width // crow_count
    owner_index = pivot_owner[0]
    coupling = jnp.einsum(
        "jutr,jutk->rjk", own_masked, received, preferred_element_type=jnp.float32
    )
    whole = jnp.concatenate([gram_part[:, None, :], coupling], 1).reshape(
        coarse_width, (slot_count + 1) * coarse_width
    )
    pivot_partial = lax.dynamic_slice_in_dim(whole, owner_index * row_share, row_share, 0)
    outgoing_rows = jnp.concatenate(
        [
            whole.reshape(crow_count, row_share, whole.shape[1]),
            jnp.broadcast_to(pivot_partial[None], (crow_count,) + pivot_partial.shape),
        ],
        1,
    )
    pieces = lax.all_to_all(outgoing_rows, "crow", 0, 0, tiled=True).reshape(
        crow_count, 2 * row_share, whole.shape[1]
    )
    return eliminate_panel(pivot_owner, pieces, coarse_width)


def solution(mesh):
    placed = (
        P("sub", "crow", None),
        P("sub", "crow", None, None),
        P("sub", "crow", None, None),
        P("sub", "crow", None),
        P("sub", None),
        P("sub"),
    )
    return jax.shard_map(
        per_device,
        mesh=mesh,
        in_specs=placed,
        out_specs=(P(("sub", "crow"), None), P(("sub", "crow"), None), P(("sub", "crow"), None)),
        check_vma=False,
    )
```

```python
import jax
import jax.numpy as jnp
from jax import lax
from jax.sharding import PartitionSpec as P
from jax.experimental import pallas as pl
from jax.experimental.pallas import tpu as pltpu


def padded_2(block, sides, width):
    for axis, dim in sides:
        count = lax.axis_size(axis)
        forward = [(i, i + 1) for i in range(count - 1)]
        backward = [(target, source) for source, target in forward]
        low = lax.ppermute(
            lax.slice_in_dim(block, block.shape[dim] - width, None, axis=dim), axis, forward
        )
        high = lax.ppermute(lax.slice_in_dim(block, 0, width, axis=dim), axis, backward)
        block = jnp.concatenate([low, block, high], axis=dim)
    return block


def shifted(value, axis, steps):
    count = lax.axis_size(axis)
    initial, last = (max(0, -steps), min(count, count - steps))
    return lax.ppermute(value, axis, [(source, source + steps) for source in range(initial, last)])


def broadcast(shard, axis, root):
    mine = lax.axis_index(axis) == root
    return lax.psum(jnp.where(mine, shard, jnp.zeros_like(shard)), axis)


def neighbour_offsets(across):
    return [-across - 1, -across, -across + 1, -1, 1, across - 1, across, across + 1]


def _ab(a, b):
    return lax.dot_general(a, b, (((1,), (0,)), ((), ())), preferred_element_type=jnp.float32)


def _atb(a, b):
    return lax.dot_general(a, b, (((0,), (0,)), ((), ())), preferred_element_type=jnp.float32)


def local_apply_kernel(
    chosen_ref, live_ref, z_ref, zp_ref, zn_ref, d_ref, u_ref, up_ref,
    gram_ref, out_ref, own_ref, app_ref,
):
    count, rows = d_ref.shape[0], d_ref.shape[1]

    def rows_of(b):
        return z_ref[pl.ds(b * rows, rows), :]

    for b in range(count):
        below = zp_ref[...] if b == 0 else rows_of(b - 1)
        lower = up_ref[...] if b == 0 else u_ref[b - 1]
        above = zn_ref[...] if b == count - 1 else rows_of(b + 1)
        total = (_ab(d_ref[b], rows_of(b)) + _ab(u_ref[b], above)) + _atb(lower, below)
        app_ref[pl.ds(b * rows, rows), :] = total.astype(app_ref.dtype)
    gram_ref[...] = _atb(z_ref[...], app_ref[...])
    for i in range(out_ref.shape[0]):
        start = pl.multiple_of(chosen_ref[i] * rows, rows)
        out_ref[i] = app_ref[pl.ds(start, rows), :]
        tile = z_ref[pl.ds(start, rows), :]
        own_ref[i] = jnp.where(live_ref[i] > 0, tile, jnp.zeros_like(tile))


def local_apply(chosen, live, centre, prev_rows, next_rows, diagonal, upper, prev_upper):
    tiles = chosen.shape[0]
    blocks, rows = diagonal.shape[0], diagonal.shape[1]
    width = centre.shape[1]
    vmem = pl.BlockSpec(memory_space=pltpu.VMEM)
    smem = pl.BlockSpec(memory_space=pltpu.SMEM)
    return pl.pallas_call(
        local_apply_kernel,
        out_shape=(
            jax.ShapeDtypeStruct((width, width), jnp.float32),
            jax.ShapeDtypeStruct((tiles, rows, width), centre.dtype),
            jax.ShapeDtypeStruct((tiles, rows, width), centre.dtype),
        ),
        in_specs=[smem, smem] + [vmem] * 6,
        out_specs=(vmem, vmem, vmem),
        scratch_shapes=[pltpu.VMEM((blocks * rows, width), centre.dtype)],
    )(chosen, live, centre, prev_rows, next_rows, diagonal, upper, prev_upper)


def _exact(a, b, dims):
    return lax.dot_general(
        a, b, (dims, ((), ())), precision=lax.Precision.HIGHEST,
        preferred_element_type=jnp.float32,
    )


def panel_kernel(owner_ref, pieces_ref, self_ref, coupling_ref, panel_ref):
    share = panel_ref.shape[0]
    width = self_ref.shape[1]
    total = (pieces_ref[0] + pieces_ref[1]) + (pieces_ref[2] + pieces_ref[3])
    own = total[:share]
    lead = total[share:]
    owner = owner_ref[0]

    def pick(rows):
        block = jnp.zeros((share, share), jnp.float32)
        for q in range(width // share):
            block = jnp.where(owner == q, rows[:, q * share:(q + 1) * share], block)
        return block

    pivot = pick(lead)
    pivot = (pivot + pivot.T) * 0.5
    row_id = lax.broadcasted_iota(jnp.int32, (share, 1), 0)
    work = jnp.concatenate([pivot, jnp.eye(share, dtype=jnp.float32)], 1)
    for k in range(share):
        row = work[k:k + 1, :]
        scale = 1.0 / jnp.sqrt(row[:, k:k + 1])
        unit_row = row * scale
        below = jnp.where(row_id > k, work[:, k:k + 1] * scale, 0.0)
        work = jnp.where(row_id == k, unit_row, work - below * unit_row)
    inverse = work[:, share:]
    solved = _exact(inverse, lead, ((1,), (0,)))
    panel = _exact(pick(own), inverse, ((1,), (1,)))
    updated = own - _exact(panel, solved, ((1,), (0,)))
    self_ref[...] = updated[:, :width]
    coupling_ref[...] = updated[:, width:]
    panel_ref[...] = panel


def eliminate_panel(owner, pieces, width):
    share = pieces.shape[1] // 2
    vmem = pl.BlockSpec(memory_space=pltpu.VMEM)
    return pl.pallas_call(
        panel_kernel,
        out_shape=(
            jax.ShapeDtypeStruct((share, width), jnp.float32),
            jax.ShapeDtypeStruct((share, pieces.shape[2] - width), jnp.float32),
            jax.ShapeDtypeStruct((share, share), jnp.float32),
        ),
        in_specs=[pl.BlockSpec(memory_space=pltpu.SMEM), vmem],
        out_specs=(vmem, vmem, vmem),
    )(owner, pieces)


def per_device(deflation, diag_op, upper_op, tile_blocks, pair_counts, pivot_owner):
    crow_count = lax.axis_size("crow")
    crow_place = lax.axis_index("crow")
    sub_count = lax.axis_size("sub")
    across = min(16, sub_count // 2)
    offsets = neighbour_offsets(across)
    local_rows = deflation[0]
    blocks_here, tile_rows = (diag_op.shape[1], diag_op.shape[2])
    coarse_width = local_rows.shape[1]
    slot_count = pair_counts.shape[1]
    per_slot = tile_blocks.shape[2] // slot_count
    forward_pair = shifted(
        jnp.stack([local_rows[-tile_rows:], upper_op[0, blocks_here - 1]]), "crow", 1
    )
    next_rows = shifted(local_rows[:tile_rows], "crow", -1)
    chosen = tile_blocks[0, 0]
    position = crow_place * per_slot + jnp.arange(per_slot, dtype=jnp.int32)
    live = (position[None, :] < pair_counts[0][:, None]).astype(jnp.int32).reshape(-1)
    gram_part, outgoing, own_masked = local_apply(
        chosen, live, local_rows, forward_pair[0], next_rows, diag_op[0], upper_op[0], forward_pair[1]
    )
    outgoing = outgoing.reshape(slot_count, per_slot, tile_rows, coarse_width)
    own_masked = own_masked.reshape(slot_count, per_slot, tile_rows, coarse_width)
    slot_of = {offset: index for index, offset in enumerate(offsets)}

    def piece(offset):
        return outgoing[slot_of[offset]]

    last = sub_count - 1
    down = lax.ppermute(
        jnp.stack([piece(-across - 1), piece(-1), piece(across - 1)]),
        "sub",
        [(t, t - 1) for t in range(1, sub_count)] + [(0, last)],
    )
    up = lax.ppermute(
        jnp.stack([piece(-across + 1), piece(1), piece(across + 1)]),
        "sub",
        [(t, t + 1) for t in range(last)] + [(last, 0)],
    )
    far_down = lax.ppermute(
        jnp.stack([piece(-across), down[0], up[0]]),
        "sub",
        [(u, u - across) for u in range(across, sub_count)] + [(0, sub_count - across)],
    )
    far_up = lax.ppermute(
        jnp.stack([piece(across), down[2], up[2]]),
        "sub",
        [(u, u + across) for u in range(sub_count - across)] + [(last, across - 1)],
    )
    arrival = {
        -across - 1: far_up[2],
        -across: far_up[0],
        -across + 1: far_up[1],
        -1: up[1],
        1: down[1],
        across - 1: far_down[2],
        across: far_down[0],
        across + 1: far_down[1],
    }
    received = jnp.stack([arrival[offset] for offset in offsets])
    row_share = coarse_width // crow_count
    owner_index = pivot_owner[0]
    coupling = jnp.einsum(
        "jutr,jutk->rjk", own_masked, received, preferred_element_type=jnp.float32
    )
    whole = jnp.concatenate([gram_part[:, None, :], coupling], 1).reshape(
        coarse_width, (slot_count + 1) * coarse_width
    )
    pivot_partial = lax.dynamic_slice_in_dim(whole, owner_index * row_share, row_share, 0)
    outgoing_rows = jnp.concatenate(
        [
            whole.reshape(crow_count, row_share, whole.shape[1]),
            jnp.broadcast_to(pivot_partial[None], (crow_count,) + pivot_partial.shape),
        ],
        1,
    )
    pieces = lax.all_to_all(outgoing_rows, "crow", 0, 0, tiled=True).reshape(
        crow_count, 2 * row_share, whole.shape[1]
    )
    return eliminate_panel(pivot_owner, pieces, coarse_width)


def solution(mesh):
    placed = (
        P("sub", "crow", None),
        P("sub", "crow", None, None),
        P("sub", "crow", None, None),
        P("sub", "crow", None),
        P("sub", None),
        P("sub"),
    )
    return jax.shard_map(
        per_device,
        mesh=mesh,
        in_specs=placed,
        out_specs=(P(("sub", "crow"), None), P(("sub", "crow"), None), P(("sub", "crow"), None)),
        check_vma=False,
    )
```

```python
import functools
import jax
import jax.numpy as jnp
from jax import lax
from jax.sharding import PartitionSpec as P
from jax.experimental import pallas as pl
from jax.experimental.pallas import tpu as pltpu


def padded_2(block, sides, width):
    for axis, dim in sides:
        count = lax.axis_size(axis)
        forward = [(i, i + 1) for i in range(count - 1)]
        backward = [(target, source) for source, target in forward]
        low = lax.ppermute(
            lax.slice_in_dim(block, block.shape[dim] - width, None, axis=dim), axis, forward
        )
        high = lax.ppermute(lax.slice_in_dim(block, 0, width, axis=dim), axis, backward)
        block = jnp.concatenate([low, block, high], axis=dim)
    return block


def shifted(value, axis, steps):
    count = lax.axis_size(axis)
    initial, last = (max(0, -steps), min(count, count - steps))
    return lax.ppermute(value, axis, [(source, source + steps) for source in range(initial, last)])


def broadcast(shard, axis, root):
    mine = lax.axis_index(axis) == root
    return lax.psum(jnp.where(mine, shard, jnp.zeros_like(shard)), axis)


def neighbour_offsets(across):
    return [-across - 1, -across, -across + 1, -1, 1, across - 1, across, across + 1]


def _ab(a, b):
    return lax.dot_general(a, b, (((1,), (0,)), ((), ())), preferred_element_type=jnp.float32)


def _atb(a, b):
    return lax.dot_general(a, b, (((0,), (0,)), ((), ())), preferred_element_type=jnp.float32)


def local_apply_kernel(
    groups, blocks_ref, counts_ref, z_ref, fp_ref, zn_ref, d_ref, u_ref, *refs
):
    group_refs, own_ref, gram_ref, app_ref = refs[:len(groups)], refs[-3], refs[-2], refs[-1]
    count, rows = d_ref.shape[1], d_ref.shape[2]
    per_slot = own_ref.shape[1]
    crow = lax.axis_index("crow")

    def rows_of(b):
        return z_ref[0, pl.ds(b * rows, rows), :]

    for b in range(count):
        below = fp_ref[0] if b == 0 else rows_of(b - 1)
        lower = fp_ref[1] if b == 0 else u_ref[0, b - 1]
        above = zn_ref[...] if b == count - 1 else rows_of(b + 1)
        total = (_ab(d_ref[0, b], rows_of(b)) + _ab(u_ref[0, b], above)) + _atb(lower, below)
        app_ref[pl.ds(b * rows, rows), :] = total.astype(app_ref.dtype)
    gram_ref[...] = _atb(z_ref[0], app_ref[...])
    for slot in range(own_ref.shape[0]):
        for unit in range(per_slot):
            start = pl.multiple_of(blocks_ref[0, 0, slot * per_slot + unit] * rows, rows)
            tile = z_ref[0, pl.ds(start, rows), :]
            live = crow * per_slot + unit < counts_ref[0, slot]
            own_ref[slot, unit] = jnp.where(live, tile, jnp.zeros_like(tile))
    for group, out_ref in zip(groups, group_refs):
        for place, slot in enumerate(group):
            for unit in range(per_slot):
                start = pl.multiple_of(blocks_ref[0, 0, slot * per_slot + unit] * rows, rows)
                out_ref[place, unit] = app_ref[pl.ds(start, rows), :]


def local_apply(groups, tile_blocks, pair_counts, deflation, forward_pair, next_rows, diag_op, upper_op):
    slots = pair_counts.shape[1]
    per_slot = tile_blocks.shape[2] // slots
    blocks, rows = diag_op.shape[1], diag_op.shape[2]
    width = deflation.shape[2]
    vmem = pl.BlockSpec(memory_space=pltpu.VMEM)
    smem = pl.BlockSpec(memory_space=pltpu.SMEM)
    tile = lambda n: jax.ShapeDtypeStruct((n, per_slot, rows, width), deflation.dtype)
    return pl.pallas_call(
        functools.partial(local_apply_kernel, groups),
        out_shape=tuple(tile(len(g)) for g in groups) + (
            tile(slots),
            jax.ShapeDtypeStruct((width, width), jnp.float32),
        ),
        in_specs=[smem, smem] + [vmem] * 5,
        out_specs=tuple(vmem for _ in range(len(groups) + 2)),
        scratch_shapes=[pltpu.VMEM((blocks * rows, width), deflation.dtype)],
    )(tile_blocks, pair_counts, deflation, forward_pair, next_rows, diag_op, upper_op)


def _exact(a, b, dims):
    return lax.dot_general(
        a, b, (dims, ((), ())), precision=lax.Precision.HIGHEST,
        preferred_element_type=jnp.float32,
    )


def panel_kernel(owner_ref, pieces_ref, self_ref, coupling_ref, panel_ref):
    share = panel_ref.shape[0]
    width = self_ref.shape[1]
    total = (pieces_ref[0] + pieces_ref[1]) + (pieces_ref[2] + pieces_ref[3])
    own = total[:share]
    lead = total[share:]
    owner = owner_ref[0]

    def pick(rows):
        block = jnp.zeros((share, share), jnp.float32)
        for q in range(width // share):
            block = jnp.where(owner == q, rows[:, q * share:(q + 1) * share], block)
        return block

    pivot = pick(lead)
    pivot = (pivot + pivot.T) * 0.5
    row_id = lax.broadcasted_iota(jnp.int32, (share, 1), 0)
    work = jnp.concatenate([pivot, jnp.eye(share, dtype=jnp.float32)], 1)
    for k in range(share):
        row = work[k:k + 1, :]
        scale = 1.0 / jnp.sqrt(row[:, k:k + 1])
        unit_row = row * scale
        below = jnp.where(row_id > k, work[:, k:k + 1] * scale, 0.0)
        work = jnp.where(row_id == k, unit_row, work - below * unit_row)
    inverse = work[:, share:]
    solved = _exact(inverse, lead, ((1,), (0,)))
    panel = _exact(pick(own), inverse, ((1,), (1,)))
    updated = own - _exact(panel, solved, ((1,), (0,)))
    self_ref[...] = updated[:, :width]
    coupling_ref[...] = updated[:, width:]
    panel_ref[...] = panel


def eliminate_panel(owner, pieces, width):
    share = pieces.shape[1] // 2
    vmem = pl.BlockSpec(memory_space=pltpu.VMEM)
    return pl.pallas_call(
        panel_kernel,
        out_shape=(
            jax.ShapeDtypeStruct((share, width), jnp.float32),
            jax.ShapeDtypeStruct((share, pieces.shape[2] - width), jnp.float32),
            jax.ShapeDtypeStruct((share, share), jnp.float32),
        ),
        in_specs=[pl.BlockSpec(memory_space=pltpu.SMEM), vmem],
        out_specs=(vmem, vmem, vmem),
    )(owner, pieces)


def per_device(deflation, diag_op, upper_op, tile_blocks, pair_counts, pivot_owner):
    crow_count = lax.axis_size("crow")
    crow_place = lax.axis_index("crow")
    sub_count = lax.axis_size("sub")
    across = min(16, sub_count // 2)
    offsets = neighbour_offsets(across)
    local_rows = deflation[0]
    blocks_here, tile_rows = (diag_op.shape[1], diag_op.shape[2])
    coarse_width = local_rows.shape[1]
    slot_count = pair_counts.shape[1]
    per_slot = tile_blocks.shape[2] // slot_count
    forward_pair = shifted(
        jnp.stack([local_rows[-tile_rows:], upper_op[0, blocks_here - 1]]), "crow", 1
    )
    next_rows = shifted(local_rows[:tile_rows], "crow", -1)
    slot_of = {offset: index for index, offset in enumerate(offsets)}
    groups = (
        (slot_of[-across - 1], slot_of[-1], slot_of[across - 1]),
        (slot_of[-across + 1], slot_of[1], slot_of[across + 1]),
        (slot_of[-across],),
        (slot_of[across],),
    )
    down_out, up_out, near_down, near_up, own_masked, gram_part = local_apply(
        groups, tile_blocks, pair_counts, deflation, forward_pair, next_rows, diag_op, upper_op
    )
    last = sub_count - 1
    down = lax.ppermute(
        down_out, "sub", [(t, t - 1) for t in range(1, sub_count)] + [(0, last)]
    )
    up = lax.ppermute(up_out, "sub", [(t, t + 1) for t in range(last)] + [(last, 0)])
    far_down = lax.ppermute(
        jnp.concatenate([near_down, down[:1], up[:1]]),
        "sub",
        [(u, u - across) for u in range(across, sub_count)] + [(0, sub_count - across)],
    )
    far_up = lax.ppermute(
        jnp.concatenate([near_up, down[2:], up[2:]]),
        "sub",
        [(u, u + across) for u in range(sub_count - across)] + [(last, across - 1)],
    )
    arrival = {
        -across - 1: far_up[2],
        -across: far_up[0],
        -across + 1: far_up[1],
        -1: up[1],
        1: down[1],
        across - 1: far_down[2],
        across: far_down[0],
        across + 1: far_down[1],
    }
    received = jnp.stack([arrival[offset] for offset in offsets])
    row_share = coarse_width // crow_count
    owner_index = pivot_owner[0]
    coupling = jnp.einsum(
        "jutr,jutk->rjk", own_masked, received, preferred_element_type=jnp.float32
    )
    whole = jnp.concatenate([gram_part[:, None, :], coupling], 1).reshape(
        coarse_width, (slot_count + 1) * coarse_width
    )
    pivot_partial = lax.dynamic_slice_in_dim(whole, owner_index * row_share, row_share, 0)
    outgoing_rows = jnp.concatenate(
        [
            whole.reshape(crow_count, row_share, whole.shape[1]),
            jnp.broadcast_to(pivot_partial[None], (crow_count,) + pivot_partial.shape),
        ],
        1,
    )
    pieces = lax.all_to_all(outgoing_rows, "crow", 0, 0, tiled=True).reshape(
        crow_count, 2 * row_share, whole.shape[1]
    )
    return eliminate_panel(pivot_owner, pieces, coarse_width)


def solution(mesh):
    placed = (
        P("sub", "crow", None),
        P("sub", "crow", None, None),
        P("sub", "crow", None, None),
        P("sub", "crow", None),
        P("sub", None),
        P("sub"),
    )
    return jax.shard_map(
        per_device,
        mesh=mesh,
        in_specs=placed,
        out_specs=(P(("sub", "crow"), None), P(("sub", "crow"), None), P(("sub", "crow"), None)),
        check_vma=False,
    )
```

```python
import functools
import jax
import jax.numpy as jnp
from jax import lax
from jax.sharding import PartitionSpec as P
from jax.experimental import pallas as pl
from jax.experimental.pallas import tpu as pltpu


def padded_2(block, sides, width):
    for axis, dim in sides:
        count = lax.axis_size(axis)
        forward = [(i, i + 1) for i in range(count - 1)]
        backward = [(target, source) for source, target in forward]
        low = lax.ppermute(
            lax.slice_in_dim(block, block.shape[dim] - width, None, axis=dim), axis, forward
        )
        high = lax.ppermute(lax.slice_in_dim(block, 0, width, axis=dim), axis, backward)
        block = jnp.concatenate([low, block, high], axis=dim)
    return block


def shifted(value, axis, steps):
    count = lax.axis_size(axis)
    initial, last = (max(0, -steps), min(count, count - steps))
    return lax.ppermute(value, axis, [(source, source + steps) for source in range(initial, last)])


def broadcast(shard, axis, root):
    mine = lax.axis_index(axis) == root
    return lax.psum(jnp.where(mine, shard, jnp.zeros_like(shard)), axis)


def neighbour_offsets(across):
    return [-across - 1, -across, -across + 1, -1, 1, across - 1, across, across + 1]


def _ab(a, b):
    return lax.dot_general(a, b, (((1,), (0,)), ((), ())), preferred_element_type=jnp.float32)


def _atb(a, b):
    return lax.dot_general(a, b, (((0,), (0,)), ((), ())), preferred_element_type=jnp.float32)


def local_apply_kernel(
    groups, blocks_ref, counts_ref, z_ref, fp_ref, zn_ref, d_ref, u_ref, *refs
):
    group_refs, own_ref, gram_ref, app_ref = refs[:len(groups)], refs[-3], refs[-2], refs[-1]
    count, rows = d_ref.shape[1], d_ref.shape[2]
    per_slot = own_ref.shape[1]
    crow = lax.axis_index("crow")

    def rows_of(b):
        return z_ref[0, pl.ds(b * rows, rows), :]

    for b in range(count):
        below = fp_ref[0] if b == 0 else rows_of(b - 1)
        lower = fp_ref[1] if b == 0 else u_ref[0, b - 1]
        above = zn_ref[...] if b == count - 1 else rows_of(b + 1)
        total = (_ab(d_ref[0, b], rows_of(b)) + _ab(u_ref[0, b], above)) + _atb(lower, below)
        app_ref[pl.ds(b * rows, rows), :] = total.astype(app_ref.dtype)
    gram_ref[...] = _atb(z_ref[0], app_ref[...])
    for slot in range(own_ref.shape[0]):
        for unit in range(per_slot):
            start = pl.multiple_of(blocks_ref[0, 0, slot * per_slot + unit] * rows, rows)
            tile = z_ref[0, pl.ds(start, rows), :]
            live = crow * per_slot + unit < counts_ref[0, slot]
            own_ref[slot, unit] = jnp.where(live, tile, jnp.zeros_like(tile))
    for group, out_ref in zip(groups, group_refs):
        for place, slot in enumerate(group):
            for unit in range(per_slot):
                start = pl.multiple_of(blocks_ref[0, 0, slot * per_slot + unit] * rows, rows)
                out_ref[place, unit] = app_ref[pl.ds(start, rows), :]


def local_apply(groups, tile_blocks, pair_counts, deflation, forward_pair, next_rows, diag_op, upper_op):
    slots = pair_counts.shape[1]
    per_slot = tile_blocks.shape[2] // slots
    blocks, rows = diag_op.shape[1], diag_op.shape[2]
    width = deflation.shape[2]
    vmem = pl.BlockSpec(memory_space=pltpu.VMEM)
    smem = pl.BlockSpec(memory_space=pltpu.SMEM)
    tile = lambda n: jax.ShapeDtypeStruct((n, per_slot, rows, width), deflation.dtype)
    return pl.pallas_call(
        functools.partial(local_apply_kernel, groups),
        out_shape=tuple(tile(len(g)) for g in groups) + (
            tile(slots),
            jax.ShapeDtypeStruct((width, width), jnp.float32),
        ),
        in_specs=[smem, smem] + [vmem] * 5,
        out_specs=tuple(vmem for _ in range(len(groups) + 2)),
        scratch_shapes=[pltpu.VMEM((blocks * rows, width), deflation.dtype)],
    )(tile_blocks, pair_counts, deflation, forward_pair, next_rows, diag_op, upper_op)


def _exact(a, b, dims):
    return lax.dot_general(
        a, b, (dims, ((), ())), precision=lax.Precision.HIGHEST,
        preferred_element_type=jnp.float32,
    )


def panel_kernel(owner_ref, pieces_ref, self_ref, coupling_ref, panel_ref):
    share = panel_ref.shape[0]
    width = self_ref.shape[1]
    total = (pieces_ref[0] + pieces_ref[1]) + (pieces_ref[2] + pieces_ref[3])
    own = total[:share]
    lead = total[share:]
    owner = owner_ref[0]

    def pick(rows):
        block = jnp.zeros((share, share), jnp.float32)
        for q in range(width // share):
            block = jnp.where(owner == q, rows[:, q * share:(q + 1) * share], block)
        return block

    pivot = pick(lead)
    pivot = (pivot + pivot.T) * 0.5
    row_id = lax.broadcasted_iota(jnp.int32, (share, 1), 0)
    work = jnp.concatenate([pivot, jnp.eye(share, dtype=jnp.float32)], 1)
    for k in range(share):
        row = work[k:k + 1, :]
        scale = lax.rsqrt(row[:, k:k + 1])
        unit_row = row * scale
        below = jnp.where(row_id > k, work[:, k:k + 1] * scale, 0.0)
        work = jnp.where(row_id == k, unit_row, work - below * unit_row)
    inverse = work[:, share:]
    solved = _exact(inverse, lead, ((1,), (0,)))
    panel = _exact(pick(own), inverse, ((1,), (1,)))
    updated = own - _exact(panel, solved, ((1,), (0,)))
    self_ref[...] = updated[:, :width]
    coupling_ref[...] = updated[:, width:]
    panel_ref[...] = panel


def eliminate_panel(owner, pieces, width):
    share = pieces.shape[1] // 2
    vmem = pl.BlockSpec(memory_space=pltpu.VMEM)
    return pl.pallas_call(
        panel_kernel,
        out_shape=(
            jax.ShapeDtypeStruct((share, width), jnp.float32),
            jax.ShapeDtypeStruct((share, pieces.shape[2] - width), jnp.float32),
            jax.ShapeDtypeStruct((share, share), jnp.float32),
        ),
        in_specs=[pl.BlockSpec(memory_space=pltpu.SMEM), vmem],
        out_specs=(vmem, vmem, vmem),
    )(owner, pieces)


def coarse_rows_kernel(owner_ref, gram_ref, own_ref, down_ref, up_ref, fdn_ref, fup_ref, out_ref, whole_ref):
    width = gram_ref.shape[0]
    share = out_ref.shape[1] // 2
    sources = {
        0: (fup_ref, 2), 1: (fup_ref, 0), 2: (fup_ref, 1), 3: (up_ref, 1),
        4: (down_ref, 1), 5: (fdn_ref, 2), 6: (fdn_ref, 0), 7: (fdn_ref, 1),
    }
    whole_ref[:, :width] = gram_ref[...]
    for slot in range(own_ref.shape[0]):
        ref, place = sources[slot]
        block = _atb(own_ref[slot, 0], ref[place, 0])
        for unit in range(1, own_ref.shape[1]):
            block = block + _atb(own_ref[slot, unit], ref[place, unit])
        whole_ref[:, (slot + 1) * width:(slot + 2) * width] = block
    start = pl.multiple_of(owner_ref[0] * share, share)
    pivot = whole_ref[pl.ds(start, share), :]
    for target in range(out_ref.shape[0]):
        out_ref[target, :share] = whole_ref[target * share:(target + 1) * share, :]
        out_ref[target, share:] = pivot


def coarse_rows(owner, gram, own, down, up, far_down, far_up, crow_count):
    width = gram.shape[0]
    share = width // crow_count
    columns = width * (own.shape[0] + 1)
    vmem = pl.BlockSpec(memory_space=pltpu.VMEM)
    return pl.pallas_call(
        coarse_rows_kernel,
        out_shape=jax.ShapeDtypeStruct((crow_count, 2 * share, columns), jnp.float32),
        in_specs=[pl.BlockSpec(memory_space=pltpu.SMEM)] + [vmem] * 6,
        out_specs=vmem,
        scratch_shapes=[pltpu.VMEM((width, columns), jnp.float32)],
    )(owner, gram, own, down, up, far_down, far_up)


def per_device(deflation, diag_op, upper_op, tile_blocks, pair_counts, pivot_owner):
    crow_count = lax.axis_size("crow")
    crow_place = lax.axis_index("crow")
    sub_count = lax.axis_size("sub")
    across = min(16, sub_count // 2)
    offsets = neighbour_offsets(across)
    local_rows = deflation[0]
    blocks_here, tile_rows = (diag_op.shape[1], diag_op.shape[2])
    coarse_width = local_rows.shape[1]
    slot_count = pair_counts.shape[1]
    per_slot = tile_blocks.shape[2] // slot_count
    forward_pair = shifted(
        jnp.stack([local_rows[-tile_rows:], upper_op[0, blocks_here - 1]]), "crow", 1
    )
    next_rows = shifted(local_rows[:tile_rows], "crow", -1)
    slot_of = {offset: index for index, offset in enumerate(offsets)}
    groups = (
        (slot_of[-across - 1], slot_of[-1], slot_of[across - 1]),
        (slot_of[-across + 1], slot_of[1], slot_of[across + 1]),
        (slot_of[-across],),
        (slot_of[across],),
    )
    down_out, up_out, near_down, near_up, own_masked, gram_part = local_apply(
        groups, tile_blocks, pair_counts, deflation, forward_pair, next_rows, diag_op, upper_op
    )
    last = sub_count - 1
    down = lax.ppermute(
        down_out, "sub", [(t, t - 1) for t in range(1, sub_count)] + [(0, last)]
    )
    up = lax.ppermute(up_out, "sub", [(t, t + 1) for t in range(last)] + [(last, 0)])
    far_down = lax.ppermute(
        jnp.concatenate([near_down, down[:1], up[:1]]),
        "sub",
        [(u, u - across) for u in range(across, sub_count)] + [(0, sub_count - across)],
    )
    far_up = lax.ppermute(
        jnp.concatenate([near_up, down[2:], up[2:]]),
        "sub",
        [(u, u + across) for u in range(sub_count - across)] + [(last, across - 1)],
    )
    assert offsets == [-across - 1, -across, -across + 1, -1, 1, across - 1, across, across + 1]
    outgoing_rows = coarse_rows(
        pivot_owner, gram_part, own_masked, down, up, far_down, far_up, crow_count
    )
    pieces = lax.all_to_all(outgoing_rows, "crow", 0, 0, tiled=True)
    return eliminate_panel(pivot_owner, pieces, coarse_width)


def solution(mesh):
    placed = (
        P("sub", "crow", None),
        P("sub", "crow", None, None),
        P("sub", "crow", None, None),
        P("sub", "crow", None),
        P("sub", None),
        P("sub"),
    )
    return jax.shard_map(
        per_device,
        mesh=mesh,
        in_specs=placed,
        out_specs=(P(("sub", "crow"), None), P(("sub", "crow"), None), P(("sub", "crow"), None)),
        check_vma=False,
    )
```

```python
import functools
import jax
import jax.numpy as jnp
from jax import lax
from jax.sharding import PartitionSpec as P
from jax.experimental import pallas as pl
from jax.experimental.pallas import tpu as pltpu


def padded_2(block, sides, width):
    for axis, dim in sides:
        count = lax.axis_size(axis)
        forward = [(i, i + 1) for i in range(count - 1)]
        backward = [(target, source) for source, target in forward]
        low = lax.ppermute(
            lax.slice_in_dim(block, block.shape[dim] - width, None, axis=dim), axis, forward
        )
        high = lax.ppermute(lax.slice_in_dim(block, 0, width, axis=dim), axis, backward)
        block = jnp.concatenate([low, block, high], axis=dim)
    return block


def shifted(value, axis, steps):
    count = lax.axis_size(axis)
    initial, last = (max(0, -steps), min(count, count - steps))
    return lax.ppermute(value, axis, [(source, source + steps) for source in range(initial, last)])


def broadcast(shard, axis, root):
    mine = lax.axis_index(axis) == root
    return lax.psum(jnp.where(mine, shard, jnp.zeros_like(shard)), axis)


def neighbour_offsets(across):
    return [-across - 1, -across, -across + 1, -1, 1, across - 1, across, across + 1]


def _ab(a, b):
    return lax.dot_general(a, b, (((1,), (0,)), ((), ())), preferred_element_type=jnp.float32)


def _atb(a, b):
    return lax.dot_general(a, b, (((0,), (0,)), ((), ())), preferred_element_type=jnp.float32)


def local_apply_kernel(
    groups, blocks_ref, counts_ref, z_ref, fp_ref, zn_ref, d_ref, u_ref, *refs
):
    group_refs, own_ref, gram_ref, app_ref = refs[:len(groups)], refs[-3], refs[-2], refs[-1]
    count, rows = d_ref.shape[1], d_ref.shape[2]
    per_slot = own_ref.shape[1]
    crow = lax.axis_index("crow")

    def rows_of(b):
        return z_ref[0, pl.ds(b * rows, rows), :]

    for b in range(count):
        below = fp_ref[0] if b == 0 else rows_of(b - 1)
        lower = fp_ref[1] if b == 0 else u_ref[0, b - 1]
        above = zn_ref[...] if b == count - 1 else rows_of(b + 1)
        total = (_ab(d_ref[0, b], rows_of(b)) + _ab(u_ref[0, b], above)) + _atb(lower, below)
        app_ref[pl.ds(b * rows, rows), :] = total.astype(app_ref.dtype)
    gram_ref[...] = _atb(z_ref[0], app_ref[...])
    for slot in range(own_ref.shape[0]):
        for unit in range(per_slot):
            start = pl.multiple_of(blocks_ref[0, 0, slot * per_slot + unit] * rows, rows)
            tile = z_ref[0, pl.ds(start, rows), :]
            live = crow * per_slot + unit < counts_ref[0, slot]
            own_ref[slot, unit] = jnp.where(live, tile, jnp.zeros_like(tile))
    for group, out_ref in zip(groups, group_refs):
        for place, slot in enumerate(group):
            for unit in range(per_slot):
                start = pl.multiple_of(blocks_ref[0, 0, slot * per_slot + unit] * rows, rows)
                out_ref[place, unit] = app_ref[pl.ds(start, rows), :]


def local_apply(groups, tile_blocks, pair_counts, deflation, forward_pair, next_rows, diag_op, upper_op):
    slots = pair_counts.shape[1]
    per_slot = tile_blocks.shape[2] // slots
    blocks, rows = diag_op.shape[1], diag_op.shape[2]
    width = deflation.shape[2]
    vmem = pl.BlockSpec(memory_space=pltpu.VMEM)
    smem = pl.BlockSpec(memory_space=pltpu.SMEM)
    tile = lambda n: jax.ShapeDtypeStruct((n, per_slot, rows, width), deflation.dtype)
    return pl.pallas_call(
        functools.partial(local_apply_kernel, groups),
        out_shape=tuple(tile(len(g)) for g in groups) + (
            tile(slots),
            jax.ShapeDtypeStruct((width, width), jnp.float32),
        ),
        in_specs=[smem, smem] + [vmem] * 5,
        out_specs=tuple(vmem for _ in range(len(groups) + 2)),
        scratch_shapes=[pltpu.VMEM((blocks * rows, width), deflation.dtype)],
    )(tile_blocks, pair_counts, deflation, forward_pair, next_rows, diag_op, upper_op)


def _exact(a, b, dims):
    return lax.dot_general(
        a, b, (dims, ((), ())), precision=lax.Precision.HIGHEST,
        preferred_element_type=jnp.float32,
    )


def pivot_inverse_kernel(blocks_ref, inverse_ref):
    share = inverse_ref.shape[0]
    pivot = (blocks_ref[0] + blocks_ref[1]) + (blocks_ref[2] + blocks_ref[3])
    pivot = (pivot + pivot.T) * 0.5
    row_id = lax.broadcasted_iota(jnp.int32, (share, 1), 0)
    work = jnp.concatenate([pivot, jnp.eye(share, dtype=jnp.float32)], 1)
    for k in range(share):
        row = work[k:k + 1, :]
        scale = lax.rsqrt(row[:, k:k + 1])
        unit_row = row * scale
        below = jnp.where(row_id > k, work[:, k:k + 1] * scale, 0.0)
        work = jnp.where(row_id == k, unit_row, work - below * unit_row)
    inverse_ref[...] = work[:, share:]


def pivot_inverse(blocks):
    share = blocks.shape[1]
    vmem = pl.BlockSpec(memory_space=pltpu.VMEM)
    return pl.pallas_call(
        pivot_inverse_kernel,
        out_shape=jax.ShapeDtypeStruct((share, share), jnp.float32),
        in_specs=[vmem],
        out_specs=vmem,
    )(blocks)


def panel_kernel(owner_ref, pieces_ref, inverse_ref, self_ref, coupling_ref, panel_ref):
    share = panel_ref.shape[0]
    width = self_ref.shape[1]
    total = (pieces_ref[0] + pieces_ref[1]) + (pieces_ref[2] + pieces_ref[3])
    own = total[:share]
    lead = total[share:]
    owner = owner_ref[0]
    columns = jnp.zeros((share, share), jnp.float32)
    for q in range(width // share):
        columns = jnp.where(owner == q, own[:, q * share:(q + 1) * share], columns)
    inverse = inverse_ref[...]
    solved = _exact(inverse, lead, ((1,), (0,)))
    panel = _exact(columns, inverse, ((1,), (1,)))
    updated = own - _exact(panel, solved, ((1,), (0,)))
    self_ref[...] = updated[:, :width]
    coupling_ref[...] = updated[:, width:]
    panel_ref[...] = panel


def eliminate_panel(owner, pieces, inverse, width):
    share = pieces.shape[1] // 2
    vmem = pl.BlockSpec(memory_space=pltpu.VMEM)
    return pl.pallas_call(
        panel_kernel,
        out_shape=(
            jax.ShapeDtypeStruct((share, width), jnp.float32),
            jax.ShapeDtypeStruct((share, pieces.shape[2] - width), jnp.float32),
            jax.ShapeDtypeStruct((share, share), jnp.float32),
        ),
        in_specs=[pl.BlockSpec(memory_space=pltpu.SMEM), vmem, vmem],
        out_specs=(vmem, vmem, vmem),
    )(owner, pieces, inverse)


def coarse_rows_kernel(owner_ref, gram_ref, own_ref, down_ref, up_ref, fdn_ref, fup_ref, out_ref, whole_ref):
    width = gram_ref.shape[0]
    share = out_ref.shape[1] // 2
    sources = {
        0: (fup_ref, 2), 1: (fup_ref, 0), 2: (fup_ref, 1), 3: (up_ref, 1),
        4: (down_ref, 1), 5: (fdn_ref, 2), 6: (fdn_ref, 0), 7: (fdn_ref, 1),
    }
    whole_ref[:, :width] = gram_ref[...]
    for slot in range(own_ref.shape[0]):
        ref, place = sources[slot]
        block = _atb(own_ref[slot, 0], ref[place, 0])
        for unit in range(1, own_ref.shape[1]):
            block = block + _atb(own_ref[slot, unit], ref[place, unit])
        whole_ref[:, (slot + 1) * width:(slot + 2) * width] = block
    start = pl.multiple_of(owner_ref[0] * share, share)
    pivot = whole_ref[pl.ds(start, share), :]
    for target in range(out_ref.shape[0]):
        out_ref[target, :share] = whole_ref[target * share:(target + 1) * share, :]
        out_ref[target, share:] = pivot


def coarse_rows(owner, gram, own, down, up, far_down, far_up, crow_count):
    width = gram.shape[0]
    share = width // crow_count
    columns = width * (own.shape[0] + 1)
    vmem = pl.BlockSpec(memory_space=pltpu.VMEM)
    return pl.pallas_call(
        coarse_rows_kernel,
        out_shape=jax.ShapeDtypeStruct((crow_count, 2 * share, columns), jnp.float32),
        in_specs=[pl.BlockSpec(memory_space=pltpu.SMEM)] + [vmem] * 6,
        out_specs=vmem,
        scratch_shapes=[pltpu.VMEM((width, columns), jnp.float32)],
    )(owner, gram, own, down, up, far_down, far_up)


def per_device(deflation, diag_op, upper_op, tile_blocks, pair_counts, pivot_owner):
    crow_count = lax.axis_size("crow")
    crow_place = lax.axis_index("crow")
    sub_count = lax.axis_size("sub")
    across = min(16, sub_count // 2)
    offsets = neighbour_offsets(across)
    local_rows = deflation[0]
    blocks_here, tile_rows = (diag_op.shape[1], diag_op.shape[2])
    coarse_width = local_rows.shape[1]
    slot_count = pair_counts.shape[1]
    per_slot = tile_blocks.shape[2] // slot_count
    forward_pair = shifted(
        jnp.stack([local_rows[-tile_rows:], upper_op[0, blocks_here - 1]]), "crow", 1
    )
    next_rows = shifted(local_rows[:tile_rows], "crow", -1)
    slot_of = {offset: index for index, offset in enumerate(offsets)}
    groups = (
        (slot_of[-across - 1], slot_of[-1], slot_of[across - 1]),
        (slot_of[-across + 1], slot_of[1], slot_of[across + 1]),
        (slot_of[-across],),
        (slot_of[across],),
    )
    down_out, up_out, near_down, near_up, own_masked, gram_part = local_apply(
        groups, tile_blocks, pair_counts, deflation, forward_pair, next_rows, diag_op, upper_op
    )
    row_share = coarse_width // crow_count
    corner = pivot_owner[0] * row_share
    pivot_part = lax.dynamic_slice(gram_part, (corner, corner), (row_share, row_share))
    pivot_parts = lax.all_to_all(
        jnp.broadcast_to(pivot_part[None], (crow_count, row_share, row_share)),
        "crow", 0, 0, tiled=True,
    )
    inverse = pivot_inverse(pivot_parts)
    last = sub_count - 1
    down = lax.ppermute(
        down_out, "sub", [(t, t - 1) for t in range(1, sub_count)] + [(0, last)]
    )
    up = lax.ppermute(up_out, "sub", [(t, t + 1) for t in range(last)] + [(last, 0)])
    far_down = lax.ppermute(
        jnp.concatenate([near_down, down[:1], up[:1]]),
        "sub",
        [(u, u - across) for u in range(across, sub_count)] + [(0, sub_count - across)],
    )
    far_up = lax.ppermute(
        jnp.concatenate([near_up, down[2:], up[2:]]),
        "sub",
        [(u, u + across) for u in range(sub_count - across)] + [(last, across - 1)],
    )
    assert offsets == [-across - 1, -across, -across + 1, -1, 1, across - 1, across, across + 1]
    outgoing_rows = coarse_rows(
        pivot_owner, gram_part, own_masked, down, up, far_down, far_up, crow_count
    )
    pieces = lax.all_to_all(outgoing_rows, "crow", 0, 0, tiled=True)
    return eliminate_panel(pivot_owner, pieces, inverse, coarse_width)


def solution(mesh):
    placed = (
        P("sub", "crow", None),
        P("sub", "crow", None, None),
        P("sub", "crow", None, None),
        P("sub", "crow", None),
        P("sub", None),
        P("sub"),
    )
    return jax.shard_map(
        per_device,
        mesh=mesh,
        in_specs=placed,
        out_specs=(P(("sub", "crow"), None), P(("sub", "crow"), None), P(("sub", "crow"), None)),
        check_vma=False,
    )
```

```python
import functools
import jax
import jax.numpy as jnp
from jax import lax
from jax.sharding import PartitionSpec as P
from jax.experimental import pallas as pl
from jax.experimental.pallas import tpu as pltpu


def padded_2(block, sides, width):
    for axis, dim in sides:
        count = lax.axis_size(axis)
        forward = [(i, i + 1) for i in range(count - 1)]
        backward = [(target, source) for source, target in forward]
        low = lax.ppermute(
            lax.slice_in_dim(block, block.shape[dim] - width, None, axis=dim), axis, forward
        )
        high = lax.ppermute(lax.slice_in_dim(block, 0, width, axis=dim), axis, backward)
        block = jnp.concatenate([low, block, high], axis=dim)
    return block


def shifted(value, axis, steps):
    count = lax.axis_size(axis)
    initial, last = (max(0, -steps), min(count, count - steps))
    return lax.ppermute(value, axis, [(source, source + steps) for source in range(initial, last)])


def broadcast(shard, axis, root):
    mine = lax.axis_index(axis) == root
    return lax.psum(jnp.where(mine, shard, jnp.zeros_like(shard)), axis)


def neighbour_offsets(across):
    return [-across - 1, -across, -across + 1, -1, 1, across - 1, across, across + 1]


def _ab(a, b):
    return lax.dot_general(a, b, (((1,), (0,)), ((), ())), preferred_element_type=jnp.float32)


def _atb(a, b):
    return lax.dot_general(a, b, (((0,), (0,)), ((), ())), preferred_element_type=jnp.float32)


def local_apply_kernel(
    groups, blocks_ref, counts_ref, z_ref, fp_ref, zn_ref, d_ref, u_ref, *refs
):
    group_refs, own_ref, gram_ref, app_ref = refs[:len(groups)], refs[-3], refs[-2], refs[-1]
    count, rows = d_ref.shape[1], d_ref.shape[2]
    per_slot = own_ref.shape[1]
    crow = lax.axis_index("crow")

    def rows_of(b):
        return z_ref[0, pl.ds(b * rows, rows), :]

    for b in range(count):
        below = fp_ref[0] if b == 0 else rows_of(b - 1)
        lower = fp_ref[1] if b == 0 else u_ref[0, b - 1]
        above = zn_ref[...] if b == count - 1 else rows_of(b + 1)
        total = (_ab(d_ref[0, b], rows_of(b)) + _ab(u_ref[0, b], above)) + _atb(lower, below)
        app_ref[pl.ds(b * rows, rows), :] = total.astype(app_ref.dtype)
    gram_ref[...] = _atb(z_ref[0], app_ref[...])
    for slot in range(own_ref.shape[0]):
        for unit in range(per_slot):
            start = pl.multiple_of(blocks_ref[0, 0, slot * per_slot + unit] * rows, rows)
            tile = z_ref[0, pl.ds(start, rows), :]
            live = crow * per_slot + unit < counts_ref[0, slot]
            own_ref[slot, unit] = jnp.where(live, tile, jnp.zeros_like(tile))
    for group, out_ref in zip(groups, group_refs):
        for place, slot in enumerate(group):
            for unit in range(per_slot):
                start = pl.multiple_of(blocks_ref[0, 0, slot * per_slot + unit] * rows, rows)
                out_ref[place, unit] = app_ref[pl.ds(start, rows), :]


def local_apply(groups, tile_blocks, pair_counts, deflation, forward_pair, next_rows, diag_op, upper_op):
    slots = pair_counts.shape[1]
    per_slot = tile_blocks.shape[2] // slots
    blocks, rows = diag_op.shape[1], diag_op.shape[2]
    width = deflation.shape[2]
    vmem = pl.BlockSpec(memory_space=pltpu.VMEM)
    smem = pl.BlockSpec(memory_space=pltpu.SMEM)
    tile = lambda n: jax.ShapeDtypeStruct((n, per_slot, rows, width), deflation.dtype)
    return pl.pallas_call(
        functools.partial(local_apply_kernel, groups),
        out_shape=tuple(tile(len(g)) for g in groups) + (
            tile(slots),
            jax.ShapeDtypeStruct((width, width), jnp.float32),
        ),
        in_specs=[smem, smem] + [vmem] * 5,
        out_specs=tuple(vmem for _ in range(len(groups) + 2)),
        scratch_shapes=[pltpu.VMEM((blocks * rows, width), deflation.dtype)],
    )(tile_blocks, pair_counts, deflation, forward_pair, next_rows, diag_op, upper_op)


def _exact(a, b, dims):
    return lax.dot_general(
        a, b, (dims, ((), ())), precision=lax.Precision.HIGHEST,
        preferred_element_type=jnp.float32,
    )


def pivot_inverse_kernel(owner_ref, early_ref, inverse_ref):
    share = inverse_ref.shape[0]
    width = 4 * share
    total = (early_ref[0] + early_ref[1]) + (early_ref[2] + early_ref[3])
    lead = total[share:, :width]
    owner = owner_ref[0]
    pivot = jnp.zeros((share, share), jnp.float32)
    for q in range(width // share):
        pivot = jnp.where(owner == q, lead[:, q * share:(q + 1) * share], pivot)
    pivot = (pivot + pivot.T) * 0.5
    row_id = lax.broadcasted_iota(jnp.int32, (share, 1), 0)
    work = jnp.concatenate([pivot, jnp.eye(share, dtype=jnp.float32)], 1)
    for k in range(share):
        row = work[k:k + 1, :]
        scale = lax.rsqrt(row[:, k:k + 1])
        unit_row = row * scale
        below = jnp.where(row_id > k, work[:, k:k + 1] * scale, 0.0)
        work = jnp.where(row_id == k, unit_row, work - below * unit_row)
    inverse_ref[...] = work[:, share:]


def pivot_inverse(owner, early):
    share = early.shape[1] // 2
    vmem = pl.BlockSpec(memory_space=pltpu.VMEM)
    return pl.pallas_call(
        pivot_inverse_kernel,
        out_shape=jax.ShapeDtypeStruct((share, share), jnp.float32),
        in_specs=[pl.BlockSpec(memory_space=pltpu.SMEM), vmem],
        out_specs=vmem,
    )(owner, early)


def panel_kernel(layout, owner_ref, early_ref, late_ref, inverse_ref, self_ref, coupling_ref, panel_ref):
    share = panel_ref.shape[0]
    width = self_ref.shape[1]
    inverse = inverse_ref[...]
    early = (early_ref[0] + early_ref[1]) + (early_ref[2] + early_ref[3])
    late = (late_ref[0] + late_ref[1]) + (late_ref[2] + late_ref[3])
    owner = owner_ref[0]
    columns = jnp.zeros((share, share), jnp.float32)
    for q in range(width // share):
        columns = jnp.where(owner == q, early[:share, q * share:(q + 1) * share], columns)
    panel = _exact(columns, inverse, ((1,), (1,)))
    panel_ref[...] = panel
    updated = []
    for total in (early, late):
        solved = _exact(inverse, total[share:], ((1,), (0,)))
        updated.append(total[:share] - _exact(panel, solved, ((1,), (0,))))
    for part, place, slot in layout:
        block = updated[part][:, place * width:(place + 1) * width]
        if slot < 0:
            self_ref[...] = block
        else:
            coupling_ref[:, slot * width:(slot + 1) * width] = block


def eliminate_panel(layout, owner, early, late, inverse, width):
    share = early.shape[1] // 2
    columns = early.shape[2] + late.shape[2] - width
    vmem = pl.BlockSpec(memory_space=pltpu.VMEM)
    return pl.pallas_call(
        functools.partial(panel_kernel, layout),
        out_shape=(
            jax.ShapeDtypeStruct((share, width), jnp.float32),
            jax.ShapeDtypeStruct((share, columns), jnp.float32),
            jax.ShapeDtypeStruct((share, share), jnp.float32),
        ),
        in_specs=[pl.BlockSpec(memory_space=pltpu.SMEM), vmem, vmem, vmem],
        out_specs=(vmem, vmem, vmem),
    )(owner, early, late, inverse)


def coarse_rows_kernel(columns, owner_ref, gram_ref, own_ref, *refs):
    sources, out_ref, whole_ref = refs[:-2], refs[-2], refs[-1]
    width = gram_ref.shape[0]
    share = out_ref.shape[1] // 2
    for place, (slot, source, index) in enumerate(columns):
        if slot < 0:
            block = gram_ref[...]
        else:
            ref = sources[source]
            block = _atb(own_ref[slot, 0], ref[index, 0])
            for unit in range(1, own_ref.shape[1]):
                block = block + _atb(own_ref[slot, unit], ref[index, unit])
        whole_ref[:, place * width:(place + 1) * width] = block
    start = pl.multiple_of(owner_ref[0] * share, share)
    pivot = whole_ref[pl.ds(start, share), :]
    for target in range(out_ref.shape[0]):
        out_ref[target, :share] = whole_ref[target * share:(target + 1) * share, :]
        out_ref[target, share:] = pivot


def coarse_rows(columns, owner, gram, own, sources, crow_count):
    width = gram.shape[0]
    share = width // crow_count
    total = width * len(columns)
    vmem = pl.BlockSpec(memory_space=pltpu.VMEM)
    return pl.pallas_call(
        functools.partial(coarse_rows_kernel, columns),
        out_shape=jax.ShapeDtypeStruct((crow_count, 2 * share, total), jnp.float32),
        in_specs=[pl.BlockSpec(memory_space=pltpu.SMEM)] + [vmem] * (2 + len(sources)),
        out_specs=vmem,
        scratch_shapes=[pltpu.VMEM((width, total), jnp.float32)],
    )(owner, gram, own, *sources)


def per_device(deflation, diag_op, upper_op, tile_blocks, pair_counts, pivot_owner):
    crow_count = lax.axis_size("crow")
    crow_place = lax.axis_index("crow")
    sub_count = lax.axis_size("sub")
    across = min(16, sub_count // 2)
    offsets = neighbour_offsets(across)
    local_rows = deflation[0]
    blocks_here, tile_rows = (diag_op.shape[1], diag_op.shape[2])
    coarse_width = local_rows.shape[1]
    slot_count = pair_counts.shape[1]
    per_slot = tile_blocks.shape[2] // slot_count
    forward_pair = shifted(
        jnp.stack([local_rows[-tile_rows:], upper_op[0, blocks_here - 1]]), "crow", 1
    )
    next_rows = shifted(local_rows[:tile_rows], "crow", -1)
    slot_of = {offset: index for index, offset in enumerate(offsets)}
    groups = (
        (slot_of[-across - 1], slot_of[-1], slot_of[across - 1]),
        (slot_of[-across + 1], slot_of[1], slot_of[across + 1]),
        (slot_of[-across],),
        (slot_of[across],),
    )
    down_out, up_out, near_down, near_up, own_masked, gram_part = local_apply(
        groups, tile_blocks, pair_counts, deflation, forward_pair, next_rows, diag_op, upper_op
    )
    last = sub_count - 1
    down = lax.ppermute(
        down_out, "sub", [(t, t - 1) for t in range(1, sub_count)] + [(0, last)]
    )
    up = lax.ppermute(up_out, "sub", [(t, t + 1) for t in range(last)] + [(last, 0)])
    far_down = lax.ppermute(
        jnp.concatenate([near_down, down[:1], up[:1]]),
        "sub",
        [(u, u - across) for u in range(across, sub_count)] + [(0, sub_count - across)],
    )
    far_up = lax.ppermute(
        jnp.concatenate([near_up, down[2:], up[2:]]),
        "sub",
        [(u, u + across) for u in range(sub_count - across)] + [(last, across - 1)],
    )
    assert offsets == [-across - 1, -across, -across + 1, -1, 1, across - 1, across, across + 1]
    early_columns = ((-1, 0, 0), (3, 1, 1), (4, 0, 1))
    late_columns = ((0, 1, 2), (1, 1, 0), (2, 1, 1), (5, 0, 2), (6, 0, 0), (7, 0, 1))
    early_rows = coarse_rows(early_columns, pivot_owner, gram_part, own_masked, (down, up), crow_count)
    early = lax.all_to_all(early_rows, "crow", 0, 0, tiled=True)
    inverse = pivot_inverse(pivot_owner, early)
    late_rows = coarse_rows(
        late_columns, pivot_owner, gram_part, own_masked, (far_down, far_up), crow_count
    )
    late = lax.all_to_all(late_rows, "crow", 0, 0, tiled=True)
    layout = ((0, 0, -1), (1, 0, 0), (1, 1, 1), (1, 2, 2), (0, 1, 3), (0, 2, 4), (1, 3, 5), (1, 4, 6), (1, 5, 7))
    return eliminate_panel(layout, pivot_owner, early, late, inverse, coarse_width)


def solution(mesh):
    placed = (
        P("sub", "crow", None),
        P("sub", "crow", None, None),
        P("sub", "crow", None, None),
        P("sub", "crow", None),
        P("sub", None),
        P("sub"),
    )
    return jax.shard_map(
        per_device,
        mesh=mesh,
        in_specs=placed,
        out_specs=(P(("sub", "crow"), None), P(("sub", "crow"), None), P(("sub", "crow"), None)),
        check_vma=False,
    )
```

```python
import functools
import jax
import jax.numpy as jnp
from jax import lax
from jax.sharding import PartitionSpec as P
from jax.experimental import pallas as pl
from jax.experimental.pallas import tpu as pltpu


def padded_2(block, sides, width):
    for axis, dim in sides:
        count = lax.axis_size(axis)
        forward = [(i, i + 1) for i in range(count - 1)]
        backward = [(target, source) for source, target in forward]
        low = lax.ppermute(
            lax.slice_in_dim(block, block.shape[dim] - width, None, axis=dim), axis, forward
        )
        high = lax.ppermute(lax.slice_in_dim(block, 0, width, axis=dim), axis, backward)
        block = jnp.concatenate([low, block, high], axis=dim)
    return block


def shifted(value, axis, steps):
    count = lax.axis_size(axis)
    initial, last = (max(0, -steps), min(count, count - steps))
    return lax.ppermute(value, axis, [(source, source + steps) for source in range(initial, last)])


def broadcast(shard, axis, root):
    mine = lax.axis_index(axis) == root
    return lax.psum(jnp.where(mine, shard, jnp.zeros_like(shard)), axis)


def neighbour_offsets(across):
    return [-across - 1, -across, -across + 1, -1, 1, across - 1, across, across + 1]


def _ab(a, b):
    return lax.dot_general(a, b, (((1,), (0,)), ((), ())), preferred_element_type=jnp.float32)


def _atb(a, b):
    return lax.dot_general(a, b, (((0,), (0,)), ((), ())), preferred_element_type=jnp.float32)


def interior_kernel(blocks_ref, counts_ref, z_ref, d_ref, u_ref, app_ref, edge_ref, own_ref):
    count, rows = d_ref.shape[1], d_ref.shape[2]
    per_slot = own_ref.shape[1]
    crow = lax.axis_index("crow")

    def rows_of(b):
        return z_ref[0, pl.ds(b * rows, rows), :]

    for b in range(1, count - 1):
        total = (_ab(d_ref[0, b], rows_of(b)) + _ab(u_ref[0, b], rows_of(b + 1))) + _atb(
            u_ref[0, b - 1], rows_of(b - 1)
        )
        app_ref[pl.ds(b * rows, rows), :] = total.astype(app_ref.dtype)
    last = count - 1
    edge_ref[0] = _ab(d_ref[0, 0], rows_of(0)) + _ab(u_ref[0, 0], rows_of(1))
    edge_ref[1] = _ab(d_ref[0, last], rows_of(last))
    edge_ref[2] = _atb(u_ref[0, last - 1], rows_of(last - 1))
    for slot in range(own_ref.shape[0]):
        for unit in range(per_slot):
            start = pl.multiple_of(blocks_ref[0, 0, slot * per_slot + unit] * rows, rows)
            tile = z_ref[0, pl.ds(start, rows), :]
            live = crow * per_slot + unit < counts_ref[0, slot]
            own_ref[slot, unit] = jnp.where(live, tile, jnp.zeros_like(tile))


def finish_kernel(groups, blocks_ref, z_ref, fp_ref, zn_ref, u_ref, app_in_ref, edge_ref, *refs):
    group_refs, gram_ref, app_ref = refs[:len(groups)], refs[-2], refs[-1]
    count, rows = u_ref.shape[1], u_ref.shape[2]
    last = count - 1
    app_ref[...] = app_in_ref[...]
    first = edge_ref[0] + _atb(fp_ref[1], fp_ref[0])
    app_ref[pl.ds(0, rows), :] = first.astype(app_ref.dtype)
    final = (edge_ref[1] + _ab(u_ref[0, last], zn_ref[...])) + edge_ref[2]
    app_ref[pl.ds(last * rows, rows), :] = final.astype(app_ref.dtype)
    gram_ref[...] = _atb(z_ref[0], app_ref[...])
    per_slot = group_refs[0].shape[1]
    for group, out_ref in zip(groups, group_refs):
        for place, slot in enumerate(group):
            for unit in range(per_slot):
                start = pl.multiple_of(blocks_ref[0, 0, slot * per_slot + unit] * rows, rows)
                out_ref[place, unit] = app_ref[pl.ds(start, rows), :]


def local_apply(groups, tile_blocks, pair_counts, deflation, forward_pair, next_rows, diag_op, upper_op):
    slots = pair_counts.shape[1]
    per_slot = tile_blocks.shape[2] // slots
    blocks, rows = diag_op.shape[1], diag_op.shape[2]
    width = deflation.shape[2]
    vmem = pl.BlockSpec(memory_space=pltpu.VMEM)
    smem = pl.BlockSpec(memory_space=pltpu.SMEM)
    tile = lambda n: jax.ShapeDtypeStruct((n, per_slot, rows, width), deflation.dtype)
    app, edge, own = pl.pallas_call(
        interior_kernel,
        out_shape=(
            jax.ShapeDtypeStruct((blocks * rows, width), deflation.dtype),
            jax.ShapeDtypeStruct((3, rows, width), jnp.float32),
            tile(slots),
        ),
        in_specs=[smem, smem] + [vmem] * 3,
        out_specs=(vmem, vmem, vmem),
    )(tile_blocks, pair_counts, deflation, diag_op, upper_op)
    outs = pl.pallas_call(
        functools.partial(finish_kernel, groups),
        out_shape=tuple(tile(len(g)) for g in groups) + (
            jax.ShapeDtypeStruct((width, width), jnp.float32),
        ),
        in_specs=[smem] + [vmem] * 6,
        out_specs=tuple(vmem for _ in range(len(groups) + 1)),
        scratch_shapes=[pltpu.VMEM((blocks * rows, width), deflation.dtype)],
    )(tile_blocks, deflation, forward_pair, next_rows, upper_op, app, edge)
    return outs[:-1] + (own, outs[-1])


def _exact(a, b, dims):
    return lax.dot_general(
        a, b, (dims, ((), ())), precision=lax.Precision.HIGHEST,
        preferred_element_type=jnp.float32,
    )


def pivot_inverse_kernel(blocks_ref, inverse_ref):
    share = inverse_ref.shape[0]
    pivot = (blocks_ref[0] + blocks_ref[1]) + (blocks_ref[2] + blocks_ref[3])
    pivot = (pivot + pivot.T) * 0.5
    row_id = lax.broadcasted_iota(jnp.int32, (share, 1), 0)
    work = jnp.concatenate([pivot, jnp.eye(share, dtype=jnp.float32)], 1)
    for k in range(share):
        row = work[k:k + 1, :]
        scale = lax.rsqrt(row[:, k:k + 1])
        unit_row = row * scale
        below = jnp.where(row_id > k, work[:, k:k + 1] * scale, 0.0)
        work = jnp.where(row_id == k, unit_row, work - below * unit_row)
    inverse_ref[...] = work[:, share:]


def pivot_inverse(blocks):
    share = blocks.shape[1]
    vmem = pl.BlockSpec(memory_space=pltpu.VMEM)
    return pl.pallas_call(
        pivot_inverse_kernel,
        out_shape=jax.ShapeDtypeStruct((share, share), jnp.float32),
        in_specs=[vmem],
        out_specs=vmem,
    )(blocks)


def panel_kernel(owner_ref, pieces_ref, inverse_ref, self_ref, coupling_ref, panel_ref):
    share = panel_ref.shape[0]
    width = self_ref.shape[1]
    total = (pieces_ref[0] + pieces_ref[1]) + (pieces_ref[2] + pieces_ref[3])
    own = total[:share]
    lead = total[share:]
    owner = owner_ref[0]
    columns = jnp.zeros((share, share), jnp.float32)
    for q in range(width // share):
        columns = jnp.where(owner == q, own[:, q * share:(q + 1) * share], columns)
    inverse = inverse_ref[...]
    solved = _exact(inverse, lead, ((1,), (0,)))
    panel = _exact(columns, inverse, ((1,), (1,)))
    updated = own - _exact(panel, solved, ((1,), (0,)))
    self_ref[...] = updated[:, :width]
    coupling_ref[...] = updated[:, width:]
    panel_ref[...] = panel


def eliminate_panel(owner, pieces, inverse, width):
    share = pieces.shape[1] // 2
    vmem = pl.BlockSpec(memory_space=pltpu.VMEM)
    return pl.pallas_call(
        panel_kernel,
        out_shape=(
            jax.ShapeDtypeStruct((share, width), jnp.float32),
            jax.ShapeDtypeStruct((share, pieces.shape[2] - width), jnp.float32),
            jax.ShapeDtypeStruct((share, share), jnp.float32),
        ),
        in_specs=[pl.BlockSpec(memory_space=pltpu.SMEM), vmem, vmem],
        out_specs=(vmem, vmem, vmem),
    )(owner, pieces, inverse)


def coarse_rows_kernel(owner_ref, gram_ref, own_ref, down_ref, up_ref, fdn_ref, fup_ref, out_ref, whole_ref):
    width = gram_ref.shape[0]
    share = out_ref.shape[1] // 2
    sources = {
        0: (fup_ref, 2), 1: (fup_ref, 0), 2: (fup_ref, 1), 3: (up_ref, 1),
        4: (down_ref, 1), 5: (fdn_ref, 2), 6: (fdn_ref, 0), 7: (fdn_ref, 1),
    }
    whole_ref[:, :width] = gram_ref[...]
    for slot in range(own_ref.shape[0]):
        ref, place = sources[slot]
        block = _atb(own_ref[slot, 0], ref[place, 0])
        for unit in range(1, own_ref.shape[1]):
            block = block + _atb(own_ref[slot, unit], ref[place, unit])
        whole_ref[:, (slot + 1) * width:(slot + 2) * width] = block
    start = pl.multiple_of(owner_ref[0] * share, share)
    pivot = whole_ref[pl.ds(start, share), :]
    for target in range(out_ref.shape[0]):
        out_ref[target, :share] = whole_ref[target * share:(target + 1) * share, :]
        out_ref[target, share:] = pivot


def coarse_rows(owner, gram, own, down, up, far_down, far_up, crow_count):
    width = gram.shape[0]
    share = width // crow_count
    columns = width * (own.shape[0] + 1)
    vmem = pl.BlockSpec(memory_space=pltpu.VMEM)
    return pl.pallas_call(
        coarse_rows_kernel,
        out_shape=jax.ShapeDtypeStruct((crow_count, 2 * share, columns), jnp.float32),
        in_specs=[pl.BlockSpec(memory_space=pltpu.SMEM)] + [vmem] * 6,
        out_specs=vmem,
        scratch_shapes=[pltpu.VMEM((width, columns), jnp.float32)],
    )(owner, gram, own, down, up, far_down, far_up)


def per_device(deflation, diag_op, upper_op, tile_blocks, pair_counts, pivot_owner):
    crow_count = lax.axis_size("crow")
    crow_place = lax.axis_index("crow")
    sub_count = lax.axis_size("sub")
    across = min(16, sub_count // 2)
    offsets = neighbour_offsets(across)
    local_rows = deflation[0]
    blocks_here, tile_rows = (diag_op.shape[1], diag_op.shape[2])
    coarse_width = local_rows.shape[1]
    slot_count = pair_counts.shape[1]
    per_slot = tile_blocks.shape[2] // slot_count
    forward_pair = shifted(
        jnp.stack([local_rows[-tile_rows:], upper_op[0, blocks_here - 1]]), "crow", 1
    )
    next_rows = shifted(local_rows[:tile_rows], "crow", -1)
    slot_of = {offset: index for index, offset in enumerate(offsets)}
    groups = (
        (slot_of[-across - 1], slot_of[-1], slot_of[across - 1]),
        (slot_of[-across + 1], slot_of[1], slot_of[across + 1]),
        (slot_of[-across],),
        (slot_of[across],),
    )
    down_out, up_out, near_down, near_up, own_masked, gram_part = local_apply(
        groups, tile_blocks, pair_counts, deflation, forward_pair, next_rows, diag_op, upper_op
    )
    row_share = coarse_width // crow_count
    corner = pivot_owner[0] * row_share
    pivot_part = lax.dynamic_slice(gram_part, (corner, corner), (row_share, row_share))
    pivot_parts = lax.all_to_all(
        jnp.broadcast_to(pivot_part[None], (crow_count, row_share, row_share)),
        "crow", 0, 0, tiled=True,
    )
    inverse = pivot_inverse(pivot_parts)
    last = sub_count - 1
    down = lax.ppermute(
        down_out, "sub", [(t, t - 1) for t in range(1, sub_count)] + [(0, last)]
    )
    up = lax.ppermute(up_out, "sub", [(t, t + 1) for t in range(last)] + [(last, 0)])
    far_down = lax.ppermute(
        jnp.concatenate([near_down, down[:1], up[:1]]),
        "sub",
        [(u, u - across) for u in range(across, sub_count)] + [(0, sub_count - across)],
    )
    far_up = lax.ppermute(
        jnp.concatenate([near_up, down[2:], up[2:]]),
        "sub",
        [(u, u + across) for u in range(sub_count - across)] + [(last, across - 1)],
    )
    assert offsets == [-across - 1, -across, -across + 1, -1, 1, across - 1, across, across + 1]
    outgoing_rows = coarse_rows(
        pivot_owner, gram_part, own_masked, down, up, far_down, far_up, crow_count
    )
    pieces = lax.all_to_all(outgoing_rows, "crow", 0, 0, tiled=True)
    return eliminate_panel(pivot_owner, pieces, inverse, coarse_width)


def solution(mesh):
    placed = (
        P("sub", "crow", None),
        P("sub", "crow", None, None),
        P("sub", "crow", None, None),
        P("sub", "crow", None),
        P("sub", None),
        P("sub"),
    )
    return jax.shard_map(
        per_device,
        mesh=mesh,
        in_specs=placed,
        out_specs=(P(("sub", "crow"), None), P(("sub", "crow"), None), P(("sub", "crow"), None)),
        check_vma=False,
    )
```

```python
import functools
import jax
import jax.numpy as jnp
from jax import lax
from jax.sharding import PartitionSpec as P
from jax.experimental import pallas as pl
from jax.experimental.pallas import tpu as pltpu


def padded_2(block, sides, width):
    for axis, dim in sides:
        count = lax.axis_size(axis)
        forward = [(i, i + 1) for i in range(count - 1)]
        backward = [(target, source) for source, target in forward]
        low = lax.ppermute(
            lax.slice_in_dim(block, block.shape[dim] - width, None, axis=dim), axis, forward
        )
        high = lax.ppermute(lax.slice_in_dim(block, 0, width, axis=dim), axis, backward)
        block = jnp.concatenate([low, block, high], axis=dim)
    return block


def shifted(value, axis, steps):
    count = lax.axis_size(axis)
    initial, last = (max(0, -steps), min(count, count - steps))
    return lax.ppermute(value, axis, [(source, source + steps) for source in range(initial, last)])


def broadcast(shard, axis, root):
    mine = lax.axis_index(axis) == root
    return lax.psum(jnp.where(mine, shard, jnp.zeros_like(shard)), axis)


def neighbour_offsets(across):
    return [-across - 1, -across, -across + 1, -1, 1, across - 1, across, across + 1]


def _ab(a, b):
    return lax.dot_general(a, b, (((1,), (0,)), ((), ())), preferred_element_type=jnp.float32)


def _atb(a, b):
    return lax.dot_general(a, b, (((0,), (0,)), ((), ())), preferred_element_type=jnp.float32)


def interior_kernel(blocks_ref, counts_ref, z_ref, d_ref, u_ref, app_ref, edge_ref, own_ref, gram_ref):
    count, rows = d_ref.shape[1], d_ref.shape[2]
    per_slot = own_ref.shape[1]
    crow = lax.axis_index("crow")

    def rows_of(b):
        return z_ref[0, pl.ds(b * rows, rows), :]

    last = count - 1
    for b in range(1, last):
        total = (_ab(d_ref[0, b], rows_of(b)) + _ab(u_ref[0, b], rows_of(b + 1))) + _atb(
            u_ref[0, b - 1], rows_of(b - 1)
        )
        app_ref[pl.ds(b * rows, rows), :] = total.astype(app_ref.dtype)
    edge_ref[0] = _ab(d_ref[0, 0], rows_of(0)) + _ab(u_ref[0, 0], rows_of(1))
    edge_ref[1] = _ab(d_ref[0, last], rows_of(last))
    edge_ref[2] = _atb(u_ref[0, last - 1], rows_of(last - 1))
    app_ref[pl.ds(0, rows), :] = jnp.zeros((rows, app_ref.shape[1]), app_ref.dtype)
    app_ref[pl.ds(last * rows, rows), :] = jnp.zeros((rows, app_ref.shape[1]), app_ref.dtype)
    gram_ref[...] = _atb(
        z_ref[0, pl.ds(rows, (count - 2) * rows), :], app_ref[pl.ds(rows, (count - 2) * rows), :]
    )
    for slot in range(own_ref.shape[0]):
        for unit in range(per_slot):
            start = pl.multiple_of(blocks_ref[0, 0, slot * per_slot + unit] * rows, rows)
            tile = z_ref[0, pl.ds(start, rows), :]
            live = crow * per_slot + unit < counts_ref[0, slot]
            own_ref[slot, unit] = jnp.where(live, tile, jnp.zeros_like(tile))


def finish_kernel(groups, blocks_ref, edge_z_ref, fp_ref, zn_ref, up_ref, app_hbm, edge_ref, part_ref, *refs):
    group_refs, gram_ref, sems = refs[:len(groups)], refs[-2], refs[-1]
    rows = up_ref.shape[0]
    last = app_hbm.shape[0] // rows - 1
    per_slot = group_refs[0].shape[1]
    copies = []
    for group, out_ref in zip(groups, group_refs):
        for place, slot in enumerate(group):
            for unit in range(per_slot):
                start = pl.multiple_of(blocks_ref[0, 0, slot * per_slot + unit] * rows, rows)
                copy = pltpu.make_async_copy(
                    app_hbm.at[pl.ds(start, rows)], out_ref.at[place, unit], sems.at[len(copies)]
                )
                copy.start()
                copies.append(copy)
    first = (edge_ref[0] + _atb(fp_ref[1], fp_ref[0])).astype(app_hbm.dtype)
    final = ((edge_ref[1] + _ab(up_ref[...], zn_ref[...])) + edge_ref[2]).astype(app_hbm.dtype)
    gram_ref[...] = (part_ref[...] + _atb(edge_z_ref[0], first)) + _atb(edge_z_ref[1], final)
    for copy in copies:
        copy.wait()
    for group, out_ref in zip(groups, group_refs):
        for place, slot in enumerate(group):
            for unit in range(per_slot):
                block = blocks_ref[0, 0, slot * per_slot + unit]
                fetched = out_ref[place, unit]
                out_ref[place, unit] = jnp.where(
                    block == 0, first, jnp.where(block == last, final, fetched)
                )


def local_apply(groups, tile_blocks, pair_counts, deflation, forward_pair, next_rows, diag_op, upper_op):
    slots = pair_counts.shape[1]
    per_slot = tile_blocks.shape[2] // slots
    blocks, rows = diag_op.shape[1], diag_op.shape[2]
    width = deflation.shape[2]
    vmem = pl.BlockSpec(memory_space=pltpu.VMEM)
    smem = pl.BlockSpec(memory_space=pltpu.SMEM)
    tile = lambda n: jax.ShapeDtypeStruct((n, per_slot, rows, width), deflation.dtype)
    app, edge, own, part = pl.pallas_call(
        interior_kernel,
        out_shape=(
            jax.ShapeDtypeStruct((blocks * rows, width), deflation.dtype),
            jax.ShapeDtypeStruct((3, rows, width), jnp.float32),
            tile(slots),
            jax.ShapeDtypeStruct((width, width), jnp.float32),
        ),
        in_specs=[smem, smem] + [vmem] * 3,
        out_specs=(vmem, vmem, vmem, vmem),
    )(tile_blocks, pair_counts, deflation, diag_op, upper_op)
    local_rows = deflation[0]
    edge_rows = jnp.stack([local_rows[:rows], local_rows[-rows:]])
    outs = pl.pallas_call(
        functools.partial(finish_kernel, groups),
        out_shape=tuple(tile(len(g)) for g in groups) + (
            jax.ShapeDtypeStruct((width, width), jnp.float32),
        ),
        in_specs=[smem] + [vmem] * 4 + [pl.BlockSpec(memory_space=pl.ANY)] + [vmem] * 2,
        out_specs=tuple(vmem for _ in range(len(groups) + 1)),
        scratch_shapes=[pltpu.SemaphoreType.DMA((tile_blocks.shape[2],))],
    )(tile_blocks, edge_rows, forward_pair, next_rows, upper_op[0, blocks - 1], app, edge, part)
    return outs[:-1] + (own, outs[-1])


def _exact(a, b, dims):
    return lax.dot_general(
        a, b, (dims, ((), ())), precision=lax.Precision.HIGHEST,
        preferred_element_type=jnp.float32,
    )


def pivot_inverse_kernel(blocks_ref, inverse_ref):
    share = inverse_ref.shape[0]
    pivot = (blocks_ref[0] + blocks_ref[1]) + (blocks_ref[2] + blocks_ref[3])
    pivot = (pivot + pivot.T) * 0.5
    row_id = lax.broadcasted_iota(jnp.int32, (share, 1), 0)
    work = jnp.concatenate([pivot, jnp.eye(share, dtype=jnp.float32)], 1)
    for k in range(share):
        row = work[k:k + 1, :]
        scale = lax.rsqrt(row[:, k:k + 1])
        unit_row = row * scale
        below = jnp.where(row_id > k, work[:, k:k + 1] * scale, 0.0)
        work = jnp.where(row_id == k, unit_row, work - below * unit_row)
    inverse_ref[...] = work[:, share:]


def pivot_inverse(blocks):
    share = blocks.shape[1]
    vmem = pl.BlockSpec(memory_space=pltpu.VMEM)
    return pl.pallas_call(
        pivot_inverse_kernel,
        out_shape=jax.ShapeDtypeStruct((share, share), jnp.float32),
        in_specs=[vmem],
        out_specs=vmem,
    )(blocks)


def panel_kernel(owner_ref, pieces_ref, inverse_ref, self_ref, coupling_ref, panel_ref):
    share = panel_ref.shape[0]
    width = self_ref.shape[1]
    total = (pieces_ref[0] + pieces_ref[1]) + (pieces_ref[2] + pieces_ref[3])
    own = total[:share]
    lead = total[share:]
    owner = owner_ref[0]
    columns = jnp.zeros((share, share), jnp.float32)
    for q in range(width // share):
        columns = jnp.where(owner == q, own[:, q * share:(q + 1) * share], columns)
    inverse = inverse_ref[...]
    solved = _exact(inverse, lead, ((1,), (0,)))
    panel = _exact(columns, inverse, ((1,), (1,)))
    updated = own - _exact(panel, solved, ((1,), (0,)))
    self_ref[...] = updated[:, :width]
    coupling_ref[...] = updated[:, width:]
    panel_ref[...] = panel


def eliminate_panel(owner, pieces, inverse, width):
    share = pieces.shape[1] // 2
    vmem = pl.BlockSpec(memory_space=pltpu.VMEM)
    return pl.pallas_call(
        panel_kernel,
        out_shape=(
            jax.ShapeDtypeStruct((share, width), jnp.float32),
            jax.ShapeDtypeStruct((share, pieces.shape[2] - width), jnp.float32),
            jax.ShapeDtypeStruct((share, share), jnp.float32),
        ),
        in_specs=[pl.BlockSpec(memory_space=pltpu.SMEM), vmem, vmem],
        out_specs=(vmem, vmem, vmem),
    )(owner, pieces, inverse)


def coarse_rows_kernel(owner_ref, gram_ref, own_ref, down_ref, up_ref, fdn_ref, fup_ref, out_ref, whole_ref):
    width = gram_ref.shape[0]
    share = out_ref.shape[1] // 2
    sources = {
        0: (fup_ref, 2), 1: (fup_ref, 0), 2: (fup_ref, 1), 3: (up_ref, 1),
        4: (down_ref, 1), 5: (fdn_ref, 2), 6: (fdn_ref, 0), 7: (fdn_ref, 1),
    }
    whole_ref[:, :width] = gram_ref[...]
    for slot in range(own_ref.shape[0]):
        ref, place = sources[slot]
        block = _atb(own_ref[slot, 0], ref[place, 0])
        for unit in range(1, own_ref.shape[1]):
            block = block + _atb(own_ref[slot, unit], ref[place, unit])
        whole_ref[:, (slot + 1) * width:(slot + 2) * width] = block
    start = pl.multiple_of(owner_ref[0] * share, share)
    pivot = whole_ref[pl.ds(start, share), :]
    for target in range(out_ref.shape[0]):
        out_ref[target, :share] = whole_ref[target * share:(target + 1) * share, :]
        out_ref[target, share:] = pivot


def coarse_rows(owner, gram, own, down, up, far_down, far_up, crow_count):
    width = gram.shape[0]
    share = width // crow_count
    columns = width * (own.shape[0] + 1)
    vmem = pl.BlockSpec(memory_space=pltpu.VMEM)
    return pl.pallas_call(
        coarse_rows_kernel,
        out_shape=jax.ShapeDtypeStruct((crow_count, 2 * share, columns), jnp.float32),
        in_specs=[pl.BlockSpec(memory_space=pltpu.SMEM)] + [vmem] * 6,
        out_specs=vmem,
        scratch_shapes=[pltpu.VMEM((width, columns), jnp.float32)],
    )(owner, gram, own, down, up, far_down, far_up)


def per_device(deflation, diag_op, upper_op, tile_blocks, pair_counts, pivot_owner):
    crow_count = lax.axis_size("crow")
    crow_place = lax.axis_index("crow")
    sub_count = lax.axis_size("sub")
    across = min(16, sub_count // 2)
    offsets = neighbour_offsets(across)
    local_rows = deflation[0]
    blocks_here, tile_rows = (diag_op.shape[1], diag_op.shape[2])
    coarse_width = local_rows.shape[1]
    slot_count = pair_counts.shape[1]
    per_slot = tile_blocks.shape[2] // slot_count
    forward_pair = shifted(
        jnp.stack([local_rows[-tile_rows:], upper_op[0, blocks_here - 1]]), "crow", 1
    )
    next_rows = shifted(local_rows[:tile_rows], "crow", -1)
    slot_of = {offset: index for index, offset in enumerate(offsets)}
    groups = (
        (slot_of[-across - 1], slot_of[-1], slot_of[across - 1]),
        (slot_of[-across + 1], slot_of[1], slot_of[across + 1]),
        (slot_of[-across],),
        (slot_of[across],),
    )
    down_out, up_out, near_down, near_up, own_masked, gram_part = local_apply(
        groups, tile_blocks, pair_counts, deflation, forward_pair, next_rows, diag_op, upper_op
    )
    row_share = coarse_width // crow_count
    corner = pivot_owner[0] * row_share
    pivot_part = lax.dynamic_slice(gram_part, (corner, corner), (row_share, row_share))
    pivot_parts = lax.all_to_all(
        jnp.broadcast_to(pivot_part[None], (crow_count, row_share, row_share)),
        "crow", 0, 0, tiled=True,
    )
    inverse = pivot_inverse(pivot_parts)
    last = sub_count - 1
    down = lax.ppermute(
        down_out, "sub", [(t, t - 1) for t in range(1, sub_count)] + [(0, last)]
    )
    up = lax.ppermute(up_out, "sub", [(t, t + 1) for t in range(last)] + [(last, 0)])
    far_down = lax.ppermute(
        jnp.concatenate([near_down, down[:1], up[:1]]),
        "sub",
        [(u, u - across) for u in range(across, sub_count)] + [(0, sub_count - across)],
    )
    far_up = lax.ppermute(
        jnp.concatenate([near_up, down[2:], up[2:]]),
        "sub",
        [(u, u + across) for u in range(sub_count - across)] + [(last, across - 1)],
    )
    assert offsets == [-across - 1, -across, -across + 1, -1, 1, across - 1, across, across + 1]
    outgoing_rows = coarse_rows(
        pivot_owner, gram_part, own_masked, down, up, far_down, far_up, crow_count
    )
    pieces = lax.all_to_all(outgoing_rows, "crow", 0, 0, tiled=True)
    return eliminate_panel(pivot_owner, pieces, inverse, coarse_width)


def solution(mesh):
    placed = (
        P("sub", "crow", None),
        P("sub", "crow", None, None),
        P("sub", "crow", None, None),
        P("sub", "crow", None),
        P("sub", None),
        P("sub"),
    )
    return jax.shard_map(
        per_device,
        mesh=mesh,
        in_specs=placed,
        out_specs=(P(("sub", "crow"), None), P(("sub", "crow"), None), P(("sub", "crow"), None)),
        check_vma=False,
    )
```

```python
import functools
import jax
import jax.numpy as jnp
from jax import lax
from jax.sharding import PartitionSpec as P
from jax.experimental import pallas as pl
from jax.experimental.pallas import tpu as pltpu


def padded_2(block, sides, width):
    for axis, dim in sides:
        count = lax.axis_size(axis)
        forward = [(i, i + 1) for i in range(count - 1)]
        backward = [(target, source) for source, target in forward]
        low = lax.ppermute(
            lax.slice_in_dim(block, block.shape[dim] - width, None, axis=dim), axis, forward
        )
        high = lax.ppermute(lax.slice_in_dim(block, 0, width, axis=dim), axis, backward)
        block = jnp.concatenate([low, block, high], axis=dim)
    return block


def shifted(value, axis, steps):
    count = lax.axis_size(axis)
    initial, last = (max(0, -steps), min(count, count - steps))
    return lax.ppermute(value, axis, [(source, source + steps) for source in range(initial, last)])


def broadcast(shard, axis, root):
    mine = lax.axis_index(axis) == root
    return lax.psum(jnp.where(mine, shard, jnp.zeros_like(shard)), axis)


def neighbour_offsets(across):
    return [-across - 1, -across, -across + 1, -1, 1, across - 1, across, across + 1]


def _ab(a, b):
    return lax.dot_general(a, b, (((1,), (0,)), ((), ())), preferred_element_type=jnp.float32)


def _atb(a, b):
    return lax.dot_general(a, b, (((0,), (0,)), ((), ())), preferred_element_type=jnp.float32)


def local_apply_kernel(
    groups, blocks_ref, counts_ref, z_ref, fp_ref, zn_ref, d_ref, u_ref, *refs
):
    group_refs, own_ref, gram_ref, app_ref = refs[:len(groups)], refs[-3], refs[-2], refs[-1]
    count, rows = d_ref.shape[1], d_ref.shape[2]
    per_slot = own_ref.shape[1]
    crow = lax.axis_index("crow")

    def rows_of(b):
        return z_ref[0, pl.ds(b * rows, rows), :]

    for b in range(count):
        below = fp_ref[0] if b == 0 else rows_of(b - 1)
        lower = fp_ref[1] if b == 0 else u_ref[0, b - 1]
        above = zn_ref[2] if b == count - 1 else rows_of(b + 1)
        total = (_ab(d_ref[0, b], rows_of(b)) + _ab(u_ref[0, b], above)) + _atb(lower, below)
        app_ref[pl.ds(b * rows, rows), :] = total.astype(app_ref.dtype)
    gram_ref[...] = _atb(z_ref[0], app_ref[...])
    for slot in range(own_ref.shape[0]):
        for unit in range(per_slot):
            start = pl.multiple_of(blocks_ref[0, 0, slot * per_slot + unit] * rows, rows)
            tile = z_ref[0, pl.ds(start, rows), :]
            live = crow * per_slot + unit < counts_ref[0, slot]
            own_ref[slot, unit] = jnp.where(live, tile, jnp.zeros_like(tile))
    for group, out_ref in zip(groups, group_refs):
        for place, slot in enumerate(group):
            for unit in range(per_slot):
                start = pl.multiple_of(blocks_ref[0, 0, slot * per_slot + unit] * rows, rows)
                out_ref[place, unit] = app_ref[pl.ds(start, rows), :]


def local_apply(groups, tile_blocks, pair_counts, deflation, forward_pair, next_rows, diag_op, upper_op):
    slots = pair_counts.shape[1]
    per_slot = tile_blocks.shape[2] // slots
    blocks, rows = diag_op.shape[1], diag_op.shape[2]
    width = deflation.shape[2]
    vmem = pl.BlockSpec(memory_space=pltpu.VMEM)
    smem = pl.BlockSpec(memory_space=pltpu.SMEM)
    tile = lambda n: jax.ShapeDtypeStruct((n, per_slot, rows, width), deflation.dtype)
    return pl.pallas_call(
        functools.partial(local_apply_kernel, groups),
        out_shape=tuple(tile(len(g)) for g in groups) + (
            tile(slots),
            jax.ShapeDtypeStruct((width, width), jnp.float32),
        ),
        in_specs=[smem, smem] + [vmem] * 5,
        out_specs=tuple(vmem for _ in range(len(groups) + 2)),
        scratch_shapes=[pltpu.VMEM((blocks * rows, width), deflation.dtype)],
    )(tile_blocks, pair_counts, deflation, forward_pair, next_rows, diag_op, upper_op)


def _exact(a, b, dims):
    return lax.dot_general(
        a, b, (dims, ((), ())), precision=lax.Precision.HIGHEST,
        preferred_element_type=jnp.float32,
    )


def pivot_inverse_kernel(blocks_ref, inverse_ref):
    share = inverse_ref.shape[0]
    pivot = (blocks_ref[0] + blocks_ref[1]) + (blocks_ref[2] + blocks_ref[3])
    pivot = (pivot + pivot.T) * 0.5
    row_id = lax.broadcasted_iota(jnp.int32, (share, 1), 0)
    work = jnp.concatenate([pivot, jnp.eye(share, dtype=jnp.float32)], 1)
    for k in range(share):
        row = work[k:k + 1, :]
        scale = lax.rsqrt(row[:, k:k + 1])
        unit_row = row * scale
        below = jnp.where(row_id > k, work[:, k:k + 1] * scale, 0.0)
        work = jnp.where(row_id == k, unit_row, work - below * unit_row)
    inverse_ref[...] = work[:, share:]


def pivot_inverse(blocks):
    share = blocks.shape[1]
    vmem = pl.BlockSpec(memory_space=pltpu.VMEM)
    return pl.pallas_call(
        pivot_inverse_kernel,
        out_shape=jax.ShapeDtypeStruct((share, share), jnp.float32),
        in_specs=[vmem],
        out_specs=vmem,
    )(blocks)


def panel_kernel(owner_ref, pieces_ref, inverse_ref, self_ref, coupling_ref, panel_ref):
    share = panel_ref.shape[0]
    width = self_ref.shape[1]
    total = (pieces_ref[0] + pieces_ref[1]) + (pieces_ref[2] + pieces_ref[3])
    own = total[:share]
    lead = total[share:]
    owner = owner_ref[0]
    columns = jnp.zeros((share, share), jnp.float32)
    for q in range(width // share):
        columns = jnp.where(owner == q, own[:, q * share:(q + 1) * share], columns)
    inverse = inverse_ref[...]
    solved = _exact(inverse, lead, ((1,), (0,)))
    panel = _exact(columns, inverse, ((1,), (1,)))
    updated = own - _exact(panel, solved, ((1,), (0,)))
    self_ref[...] = updated[:, :width]
    coupling_ref[...] = updated[:, width:]
    panel_ref[...] = panel


def eliminate_panel(owner, pieces, inverse, width):
    share = pieces.shape[1] // 2
    vmem = pl.BlockSpec(memory_space=pltpu.VMEM)
    return pl.pallas_call(
        panel_kernel,
        out_shape=(
            jax.ShapeDtypeStruct((share, width), jnp.float32),
            jax.ShapeDtypeStruct((share, pieces.shape[2] - width), jnp.float32),
            jax.ShapeDtypeStruct((share, share), jnp.float32),
        ),
        in_specs=[pl.BlockSpec(memory_space=pltpu.SMEM), vmem, vmem],
        out_specs=(vmem, vmem, vmem),
    )(owner, pieces, inverse)


def coarse_rows_kernel(owner_ref, gram_ref, own_ref, down_ref, up_ref, fdn_ref, fup_ref, out_ref, whole_ref):
    width = gram_ref.shape[0]
    share = out_ref.shape[1] // 2
    sources = {
        0: (fup_ref, 2), 1: (fup_ref, 0), 2: (fup_ref, 1), 3: (up_ref, 1),
        4: (down_ref, 1), 5: (fdn_ref, 2), 6: (fdn_ref, 0), 7: (fdn_ref, 1),
    }
    whole_ref[:, :width] = gram_ref[...]
    for slot in range(own_ref.shape[0]):
        ref, place = sources[slot]
        block = _atb(own_ref[slot, 0], ref[place, 0])
        for unit in range(1, own_ref.shape[1]):
            block = block + _atb(own_ref[slot, unit], ref[place, unit])
        whole_ref[:, (slot + 1) * width:(slot + 2) * width] = block
    start = pl.multiple_of(owner_ref[0] * share, share)
    pivot = whole_ref[pl.ds(start, share), :]
    for target in range(out_ref.shape[0]):
        out_ref[target, :share] = whole_ref[target * share:(target + 1) * share, :]
        out_ref[target, share:] = pivot


def coarse_rows(owner, gram, own, down, up, far_down, far_up, crow_count):
    width = gram.shape[0]
    share = width // crow_count
    columns = width * (own.shape[0] + 1)
    vmem = pl.BlockSpec(memory_space=pltpu.VMEM)
    return pl.pallas_call(
        coarse_rows_kernel,
        out_shape=jax.ShapeDtypeStruct((crow_count, 2 * share, columns), jnp.float32),
        in_specs=[pl.BlockSpec(memory_space=pltpu.SMEM)] + [vmem] * 6,
        out_specs=vmem,
        scratch_shapes=[pltpu.VMEM((width, columns), jnp.float32)],
    )(owner, gram, own, down, up, far_down, far_up)


def per_device(deflation, diag_op, upper_op, tile_blocks, pair_counts, pivot_owner):
    crow_count = lax.axis_size("crow")
    crow_place = lax.axis_index("crow")
    sub_count = lax.axis_size("sub")
    across = min(16, sub_count // 2)
    offsets = neighbour_offsets(across)
    local_rows = deflation[0]
    blocks_here, tile_rows = (diag_op.shape[1], diag_op.shape[2])
    coarse_width = local_rows.shape[1]
    slot_count = pair_counts.shape[1]
    per_slot = tile_blocks.shape[2] // slot_count
    halo = jnp.stack([local_rows[-tile_rows:], upper_op[0, blocks_here - 1], local_rows[:tile_rows]])
    forward_pair = shifted(halo, "crow", 1)
    next_rows = shifted(halo, "crow", -1)
    slot_of = {offset: index for index, offset in enumerate(offsets)}
    groups = (
        (slot_of[-across - 1], slot_of[-1], slot_of[across - 1]),
        (slot_of[-across + 1], slot_of[1], slot_of[across + 1]),
        (slot_of[-across],),
        (slot_of[across],),
    )
    down_out, up_out, near_down, near_up, own_masked, gram_part = local_apply(
        groups, tile_blocks, pair_counts, deflation, forward_pair, next_rows, diag_op, upper_op
    )
    row_share = coarse_width // crow_count
    corner = pivot_owner[0] * row_share
    pivot_part = lax.dynamic_slice(gram_part, (corner, corner), (row_share, row_share))
    pivot_parts = lax.all_to_all(
        jnp.broadcast_to(pivot_part[None], (crow_count, row_share, row_share)),
        "crow", 0, 0, tiled=True,
    )
    inverse = pivot_inverse(pivot_parts)
    last = sub_count - 1
    down = lax.ppermute(
        down_out, "sub", [(t, t - 1) for t in range(1, sub_count)] + [(0, last)]
    )
    up = lax.ppermute(up_out, "sub", [(t, t + 1) for t in range(last)] + [(last, 0)])
    far_down = lax.ppermute(
        jnp.concatenate([near_down, down[:1], up[:1]]),
        "sub",
        [(u, u - across) for u in range(across, sub_count)] + [(0, sub_count - across)],
    )
    far_up = lax.ppermute(
        jnp.concatenate([near_up, down[2:], up[2:]]),
        "sub",
        [(u, u + across) for u in range(sub_count - across)] + [(last, across - 1)],
    )
    assert offsets == [-across - 1, -across, -across + 1, -1, 1, across - 1, across, across + 1]
    outgoing_rows = coarse_rows(
        pivot_owner, gram_part, own_masked, down, up, far_down, far_up, crow_count
    )
    pieces = lax.all_to_all(outgoing_rows, "crow", 0, 0, tiled=True)
    return eliminate_panel(pivot_owner, pieces, inverse, coarse_width)


def solution(mesh):
    placed = (
        P("sub", "crow", None),
        P("sub", "crow", None, None),
        P("sub", "crow", None, None),
        P("sub", "crow", None),
        P("sub", None),
        P("sub"),
    )
    return jax.shard_map(
        per_device,
        mesh=mesh,
        in_specs=placed,
        out_specs=(P(("sub", "crow"), None), P(("sub", "crow"), None), P(("sub", "crow"), None)),
        check_vma=False,
    )
```

```python
import functools
import jax
import jax.numpy as jnp
from jax import lax
from jax.sharding import PartitionSpec as P
from jax.experimental import pallas as pl
from jax.experimental.pallas import tpu as pltpu


def padded_2(block, sides, width):
    for axis, dim in sides:
        count = lax.axis_size(axis)
        forward = [(i, i + 1) for i in range(count - 1)]
        backward = [(target, source) for source, target in forward]
        low = lax.ppermute(
            lax.slice_in_dim(block, block.shape[dim] - width, None, axis=dim), axis, forward
        )
        high = lax.ppermute(lax.slice_in_dim(block, 0, width, axis=dim), axis, backward)
        block = jnp.concatenate([low, block, high], axis=dim)
    return block


def shifted(value, axis, steps):
    count = lax.axis_size(axis)
    initial, last = (max(0, -steps), min(count, count - steps))
    return lax.ppermute(value, axis, [(source, source + steps) for source in range(initial, last)])


def broadcast(shard, axis, root):
    mine = lax.axis_index(axis) == root
    return lax.psum(jnp.where(mine, shard, jnp.zeros_like(shard)), axis)


def neighbour_offsets(across):
    return [-across - 1, -across, -across + 1, -1, 1, across - 1, across, across + 1]


def _ab(a, b):
    return lax.dot_general(a, b, (((1,), (0,)), ((), ())), preferred_element_type=jnp.float32)


def _atb(a, b):
    return lax.dot_general(a, b, (((0,), (0,)), ((), ())), preferred_element_type=jnp.float32)


def local_apply_kernel(
    groups, blocks_ref, counts_ref, z_ref, fp_ref, zn_ref, d_ref, u_ref, *refs
):
    group_refs, own_ref, gram_ref, app_ref = refs[:len(groups)], refs[-3], refs[-2], refs[-1]
    count, rows = d_ref.shape[1], d_ref.shape[2]
    per_slot = own_ref.shape[1]
    crow = lax.axis_index("crow")

    def rows_of(b):
        return z_ref[0, pl.ds(b * rows, rows), :]

    for b in range(count):
        below = fp_ref[0] if b == 0 else rows_of(b - 1)
        lower = fp_ref[1] if b == 0 else u_ref[0, b - 1]
        above = zn_ref[...] if b == count - 1 else rows_of(b + 1)
        total = (_ab(d_ref[0, b], rows_of(b)) + _ab(u_ref[0, b], above)) + _atb(lower, below)
        app_ref[pl.ds(b * rows, rows), :] = total.astype(app_ref.dtype)
    gram_ref[...] = _atb(z_ref[0], app_ref[...])
    for slot in range(own_ref.shape[0]):
        for unit in range(per_slot):
            start = pl.multiple_of(blocks_ref[0, 0, slot * per_slot + unit] * rows, rows)
            tile = z_ref[0, pl.ds(start, rows), :]
            live = crow * per_slot + unit < counts_ref[0, slot]
            own_ref[slot, unit] = jnp.where(live, tile, jnp.zeros_like(tile))
    for group, out_ref in zip(groups, group_refs):
        for place, slot in enumerate(group):
            for unit in range(per_slot):
                start = pl.multiple_of(blocks_ref[0, 0, slot * per_slot + unit] * rows, rows)
                out_ref[place, unit] = app_ref[pl.ds(start, rows), :]


def local_apply(groups, tile_blocks, pair_counts, deflation, forward_pair, next_rows, diag_op, upper_op):
    slots = pair_counts.shape[1]
    per_slot = tile_blocks.shape[2] // slots
    blocks, rows = diag_op.shape[1], diag_op.shape[2]
    width = deflation.shape[2]
    vmem = pl.BlockSpec(memory_space=pltpu.VMEM)
    smem = pl.BlockSpec(memory_space=pltpu.SMEM)
    tile = lambda n: jax.ShapeDtypeStruct((n, per_slot, rows, width), deflation.dtype)
    return pl.pallas_call(
        functools.partial(local_apply_kernel, groups),
        out_shape=tuple(tile(len(g)) for g in groups) + (
            tile(slots),
            jax.ShapeDtypeStruct((width, width), jnp.float32),
        ),
        in_specs=[smem, smem] + [vmem] * 5,
        out_specs=tuple(vmem for _ in range(len(groups) + 2)),
        scratch_shapes=[pltpu.VMEM((blocks * rows, width), deflation.dtype)],
    )(tile_blocks, pair_counts, deflation, forward_pair, next_rows, diag_op, upper_op)


def _exact(a, b, dims):
    return lax.dot_general(
        a, b, (dims, ((), ())), precision=lax.Precision.HIGHEST,
        preferred_element_type=jnp.float32,
    )


def pivot_inverse_kernel(blocks_ref, inverse_ref):
    share = inverse_ref.shape[0]
    pivot = (blocks_ref[0] + blocks_ref[1]) + (blocks_ref[2] + blocks_ref[3])
    pivot = (pivot + pivot.T) * 0.5
    row_id = lax.broadcasted_iota(jnp.int32, (share, 1), 0)
    work = jnp.concatenate([pivot, jnp.eye(share, dtype=jnp.float32)], 1)
    for k in range(share):
        row = work[k:k + 1, :]
        scale = lax.rsqrt(row[:, k:k + 1])
        unit_row = row * scale
        below = jnp.where(row_id > k, work[:, k:k + 1] * scale, 0.0)
        work = jnp.where(row_id == k, unit_row, work - below * unit_row)
    inverse_ref[...] = work[:, share:]


def pivot_inverse(blocks):
    share = blocks.shape[1]
    vmem = pl.BlockSpec(memory_space=pltpu.VMEM)
    return pl.pallas_call(
        pivot_inverse_kernel,
        out_shape=jax.ShapeDtypeStruct((share, share), jnp.float32),
        in_specs=[vmem],
        out_specs=vmem,
    )(blocks)


def panel_kernel(owner_ref, pieces_ref, inverse_ref, self_ref, coupling_ref, panel_ref):
    share = panel_ref.shape[0]
    width = self_ref.shape[1]
    total = (pieces_ref[0] + pieces_ref[1]) + (pieces_ref[2] + pieces_ref[3])
    own = total[:share]
    lead = total[share:]
    owner = owner_ref[0]
    columns = jnp.zeros((share, share), jnp.float32)
    for q in range(width // share):
        columns = jnp.where(owner == q, own[:, q * share:(q + 1) * share], columns)
    inverse = inverse_ref[...]
    solved = _exact(inverse, lead, ((1,), (0,)))
    panel = _exact(columns, inverse, ((1,), (1,)))
    updated = own - _exact(panel, solved, ((1,), (0,)))
    self_ref[...] = updated[:, :width]
    coupling_ref[...] = updated[:, width:]
    panel_ref[...] = panel


def eliminate_panel(owner, pieces, inverse, width):
    share = pieces.shape[1] // 2
    vmem = pl.BlockSpec(memory_space=pltpu.VMEM)
    return pl.pallas_call(
        panel_kernel,
        out_shape=(
            jax.ShapeDtypeStruct((share, width), jnp.float32),
            jax.ShapeDtypeStruct((share, pieces.shape[2] - width), jnp.float32),
            jax.ShapeDtypeStruct((share, share), jnp.float32),
        ),
        in_specs=[pl.BlockSpec(memory_space=pltpu.SMEM), vmem, vmem],
        out_specs=(vmem, vmem, vmem),
    )(owner, pieces, inverse)


def coarse_rows_kernel(owner_ref, gram_ref, own_ref, down_ref, up_ref, fdn_ref, fup_ref, out_ref, whole_ref):
    width = gram_ref.shape[0]
    share = out_ref.shape[1] // 2
    sources = {
        0: (fup_ref, 2), 1: (fup_ref, 0), 2: (fup_ref, 1), 3: (up_ref, 1),
        4: (down_ref, 1), 5: (fdn_ref, 2), 6: (fdn_ref, 0), 7: (fdn_ref, 1),
    }
    whole_ref[:, :width] = gram_ref[...]
    for slot in range(own_ref.shape[0]):
        ref, place = sources[slot]
        block = _atb(own_ref[slot, 0], ref[place, 0])
        for unit in range(1, own_ref.shape[1]):
            block = block + _atb(own_ref[slot, unit], ref[place, unit])
        whole_ref[:, (slot + 1) * width:(slot + 2) * width] = block
    start = pl.multiple_of(owner_ref[0] * share, share)
    pivot = whole_ref[pl.ds(start, share), :]
    for target in range(out_ref.shape[0]):
        out_ref[target, :share] = whole_ref[target * share:(target + 1) * share, :]
        out_ref[target, share:] = pivot


def coarse_rows(owner, gram, own, down, up, far_down, far_up, crow_count):
    width = gram.shape[0]
    share = width // crow_count
    columns = width * (own.shape[0] + 1)
    vmem = pl.BlockSpec(memory_space=pltpu.VMEM)
    return pl.pallas_call(
        coarse_rows_kernel,
        out_shape=jax.ShapeDtypeStruct((crow_count, 2 * share, columns), jnp.float32),
        in_specs=[pl.BlockSpec(memory_space=pltpu.SMEM)] + [vmem] * 6,
        out_specs=vmem,
        scratch_shapes=[pltpu.VMEM((width, columns), jnp.float32)],
    )(owner, gram, own, down, up, far_down, far_up)


def per_device(deflation, diag_op, upper_op, tile_blocks, pair_counts, pivot_owner):
    crow_count = lax.axis_size("crow")
    crow_place = lax.axis_index("crow")
    sub_count = lax.axis_size("sub")
    across = min(16, sub_count // 2)
    offsets = neighbour_offsets(across)
    local_rows = deflation[0]
    blocks_here, tile_rows = (diag_op.shape[1], diag_op.shape[2])
    coarse_width = local_rows.shape[1]
    slot_count = pair_counts.shape[1]
    per_slot = tile_blocks.shape[2] // slot_count
    forward_pair = shifted(
        jnp.stack([local_rows[-tile_rows:], upper_op[0, blocks_here - 1]]), "crow", 1
    )
    next_rows = shifted(local_rows[:tile_rows], "crow", -1)
    slot_of = {offset: index for index, offset in enumerate(offsets)}
    groups = (
        (slot_of[-across - 1], slot_of[-1], slot_of[across - 1]),
        (slot_of[-across + 1], slot_of[1], slot_of[across + 1]),
        (slot_of[-across],),
        (slot_of[across],),
    )
    down_out, up_out, near_down, near_up, own_masked, gram_part = local_apply(
        groups, tile_blocks, pair_counts, deflation, forward_pair, next_rows, diag_op, upper_op
    )
    row_share = coarse_width // crow_count
    corner = pivot_owner[0] * row_share
    pivot_part = lax.dynamic_slice(gram_part, (corner, corner), (row_share, row_share))
    pivot_parts = lax.all_to_all(
        jnp.broadcast_to(pivot_part[None], (crow_count, row_share, row_share)),
        "crow", 0, 0, tiled=True,
    )
    inverse = pivot_inverse(pivot_parts)
    last = sub_count - 1
    down = lax.ppermute(
        down_out, "sub", [(t, t - 1) for t in range(1, sub_count)] + [(0, last)]
    )
    up = lax.ppermute(up_out, "sub", [(t, t + 1) for t in range(last)] + [(last, 0)])
    down, up, pivot_parts = lax.optimization_barrier((down, up, pivot_parts))
    far_down = lax.ppermute(
        jnp.concatenate([near_down, down[:1], up[:1]]),
        "sub",
        [(u, u - across) for u in range(across, sub_count)] + [(0, sub_count - across)],
    )
    far_up = lax.ppermute(
        jnp.concatenate([near_up, down[2:], up[2:]]),
        "sub",
        [(u, u + across) for u in range(sub_count - across)] + [(last, across - 1)],
    )
    assert offsets == [-across - 1, -across, -across + 1, -1, 1, across - 1, across, across + 1]
    outgoing_rows = coarse_rows(
        pivot_owner, gram_part, own_masked, down, up, far_down, far_up, crow_count
    )
    pieces = lax.all_to_all(outgoing_rows, "crow", 0, 0, tiled=True)
    return eliminate_panel(pivot_owner, pieces, inverse, coarse_width)


def solution(mesh):
    placed = (
        P("sub", "crow", None),
        P("sub", "crow", None, None),
        P("sub", "crow", None, None),
        P("sub", "crow", None),
        P("sub", None),
        P("sub"),
    )
    return jax.shard_map(
        per_device,
        mesh=mesh,
        in_specs=placed,
        out_specs=(P(("sub", "crow"), None), P(("sub", "crow"), None), P(("sub", "crow"), None)),
        check_vma=False,
    )
```

```python
import functools
import jax
import jax.numpy as jnp
from jax import lax
from jax.sharding import PartitionSpec as P
from jax.experimental import pallas as pl
from jax.experimental.pallas import tpu as pltpu


def padded_2(block, sides, width):
    for axis, dim in sides:
        count = lax.axis_size(axis)
        forward = [(i, i + 1) for i in range(count - 1)]
        backward = [(target, source) for source, target in forward]
        low = lax.ppermute(
            lax.slice_in_dim(block, block.shape[dim] - width, None, axis=dim), axis, forward
        )
        high = lax.ppermute(lax.slice_in_dim(block, 0, width, axis=dim), axis, backward)
        block = jnp.concatenate([low, block, high], axis=dim)
    return block


def shifted(value, axis, steps):
    count = lax.axis_size(axis)
    initial, last = (max(0, -steps), min(count, count - steps))
    return lax.ppermute(value, axis, [(source, source + steps) for source in range(initial, last)])


def broadcast(shard, axis, root):
    mine = lax.axis_index(axis) == root
    return lax.psum(jnp.where(mine, shard, jnp.zeros_like(shard)), axis)


def neighbour_offsets(across):
    return [-across - 1, -across, -across + 1, -1, 1, across - 1, across, across + 1]


def _ab(a, b):
    return lax.dot_general(a, b, (((1,), (0,)), ((), ())), preferred_element_type=jnp.float32)


def _atb(a, b):
    return lax.dot_general(a, b, (((0,), (0,)), ((), ())), preferred_element_type=jnp.float32)


def local_apply_kernel(
    groups, blocks_ref, counts_ref, z_ref, fp_ref, zn_ref, d_ref, u_ref, *refs
):
    group_refs, own_ref, gram_ref, app_ref = refs[:len(groups)], refs[-3], refs[-2], refs[-1]
    count, rows = d_ref.shape[1], d_ref.shape[2]
    per_slot = own_ref.shape[1]
    crow = lax.axis_index("crow")

    def rows_of(b):
        return z_ref[0, pl.ds(b * rows, rows), :]

    for b in range(count):
        below = fp_ref[0] if b == 0 else rows_of(b - 1)
        lower = fp_ref[1] if b == 0 else u_ref[0, b - 1]
        above = zn_ref[...] if b == count - 1 else rows_of(b + 1)
        total = (_ab(d_ref[0, b], rows_of(b)) + _ab(u_ref[0, b], above)) + _atb(lower, below)
        app = total.astype(app_ref.dtype)
        app_ref[pl.ds(b * rows, rows), :] = app
        part = _atb(rows_of(b), app)
        gram = part if b == 0 else gram + part
    gram_ref[...] = gram
    for slot in range(own_ref.shape[0]):
        for unit in range(per_slot):
            start = pl.multiple_of(blocks_ref[0, 0, slot * per_slot + unit] * rows, rows)
            tile = z_ref[0, pl.ds(start, rows), :]
            live = crow * per_slot + unit < counts_ref[0, slot]
            own_ref[slot, unit] = jnp.where(live, tile, jnp.zeros_like(tile))
    for group, out_ref in zip(groups, group_refs):
        for place, slot in enumerate(group):
            for unit in range(per_slot):
                start = pl.multiple_of(blocks_ref[0, 0, slot * per_slot + unit] * rows, rows)
                out_ref[place, unit] = app_ref[pl.ds(start, rows), :]


def local_apply(groups, tile_blocks, pair_counts, deflation, forward_pair, next_rows, diag_op, upper_op):
    slots = pair_counts.shape[1]
    per_slot = tile_blocks.shape[2] // slots
    blocks, rows = diag_op.shape[1], diag_op.shape[2]
    width = deflation.shape[2]
    vmem = pl.BlockSpec(memory_space=pltpu.VMEM)
    smem = pl.BlockSpec(memory_space=pltpu.SMEM)
    tile = lambda n: jax.ShapeDtypeStruct((n, per_slot, rows, width), deflation.dtype)
    return pl.pallas_call(
        functools.partial(local_apply_kernel, groups),
        out_shape=tuple(tile(len(g)) for g in groups) + (
            tile(slots),
            jax.ShapeDtypeStruct((width, width), jnp.float32),
        ),
        in_specs=[smem, smem] + [vmem] * 5,
        out_specs=tuple(vmem for _ in range(len(groups) + 2)),
        scratch_shapes=[pltpu.VMEM((blocks * rows, width), deflation.dtype)],
    )(tile_blocks, pair_counts, deflation, forward_pair, next_rows, diag_op, upper_op)


def _exact(a, b, dims):
    return lax.dot_general(
        a, b, (dims, ((), ())), precision=lax.Precision.HIGHEST,
        preferred_element_type=jnp.float32,
    )


def pivot_inverse_kernel(blocks_ref, inverse_ref):
    share = inverse_ref.shape[0]
    pivot = (blocks_ref[0] + blocks_ref[1]) + (blocks_ref[2] + blocks_ref[3])
    pivot = (pivot + pivot.T) * 0.5
    row_id = lax.broadcasted_iota(jnp.int32, (share, 1), 0)
    work = jnp.concatenate([pivot, jnp.eye(share, dtype=jnp.float32)], 1)
    for k in range(share):
        row = work[k:k + 1, :]
        scale = lax.rsqrt(row[:, k:k + 1])
        unit_row = row * scale
        below = jnp.where(row_id > k, work[:, k:k + 1] * scale, 0.0)
        work = jnp.where(row_id == k, unit_row, work - below * unit_row)
    inverse_ref[...] = work[:, share:]


def pivot_inverse(blocks):
    share = blocks.shape[1]
    vmem = pl.BlockSpec(memory_space=pltpu.VMEM)
    return pl.pallas_call(
        pivot_inverse_kernel,
        out_shape=jax.ShapeDtypeStruct((share, share), jnp.float32),
        in_specs=[vmem],
        out_specs=vmem,
    )(blocks)


def panel_kernel(owner_ref, pieces_ref, inverse_ref, self_ref, coupling_ref, panel_ref):
    share = panel_ref.shape[0]
    width = self_ref.shape[1]
    total = (pieces_ref[0] + pieces_ref[1]) + (pieces_ref[2] + pieces_ref[3])
    own = total[:share]
    lead = total[share:]
    owner = owner_ref[0]
    columns = jnp.zeros((share, share), jnp.float32)
    for q in range(width // share):
        columns = jnp.where(owner == q, own[:, q * share:(q + 1) * share], columns)
    inverse = inverse_ref[...]
    solved = _exact(inverse, lead, ((1,), (0,)))
    panel = _exact(columns, inverse, ((1,), (1,)))
    updated = own - _exact(panel, solved, ((1,), (0,)))
    self_ref[...] = updated[:, :width]
    coupling_ref[...] = updated[:, width:]
    panel_ref[...] = panel


def eliminate_panel(owner, pieces, inverse, width):
    share = pieces.shape[1] // 2
    vmem = pl.BlockSpec(memory_space=pltpu.VMEM)
    return pl.pallas_call(
        panel_kernel,
        out_shape=(
            jax.ShapeDtypeStruct((share, width), jnp.float32),
            jax.ShapeDtypeStruct((share, pieces.shape[2] - width), jnp.float32),
            jax.ShapeDtypeStruct((share, share), jnp.float32),
        ),
        in_specs=[pl.BlockSpec(memory_space=pltpu.SMEM), vmem, vmem],
        out_specs=(vmem, vmem, vmem),
    )(owner, pieces, inverse)


def coarse_rows_kernel(owner_ref, gram_ref, own_ref, down_ref, up_ref, fdn_ref, fup_ref, out_ref, whole_ref):
    width = gram_ref.shape[0]
    share = out_ref.shape[1] // 2
    sources = {
        0: (fup_ref, 2), 1: (fup_ref, 0), 2: (fup_ref, 1), 3: (up_ref, 1),
        4: (down_ref, 1), 5: (fdn_ref, 2), 6: (fdn_ref, 0), 7: (fdn_ref, 1),
    }
    whole_ref[:, :width] = gram_ref[...]
    for slot in range(own_ref.shape[0]):
        ref, place = sources[slot]
        block = _atb(own_ref[slot, 0], ref[place, 0])
        for unit in range(1, own_ref.shape[1]):
            block = block + _atb(own_ref[slot, unit], ref[place, unit])
        whole_ref[:, (slot + 1) * width:(slot + 2) * width] = block
    start = pl.multiple_of(owner_ref[0] * share, share)
    pivot = whole_ref[pl.ds(start, share), :]
    for target in range(out_ref.shape[0]):
        out_ref[target, :share] = whole_ref[target * share:(target + 1) * share, :]
        out_ref[target, share:] = pivot


def coarse_rows(owner, gram, own, down, up, far_down, far_up, crow_count):
    width = gram.shape[0]
    share = width // crow_count
    columns = width * (own.shape[0] + 1)
    vmem = pl.BlockSpec(memory_space=pltpu.VMEM)
    return pl.pallas_call(
        coarse_rows_kernel,
        out_shape=jax.ShapeDtypeStruct((crow_count, 2 * share, columns), jnp.float32),
        in_specs=[pl.BlockSpec(memory_space=pltpu.SMEM)] + [vmem] * 6,
        out_specs=vmem,
        scratch_shapes=[pltpu.VMEM((width, columns), jnp.float32)],
    )(owner, gram, own, down, up, far_down, far_up)


def per_device(deflation, diag_op, upper_op, tile_blocks, pair_counts, pivot_owner):
    crow_count = lax.axis_size("crow")
    crow_place = lax.axis_index("crow")
    sub_count = lax.axis_size("sub")
    across = min(16, sub_count // 2)
    offsets = neighbour_offsets(across)
    local_rows = deflation[0]
    blocks_here, tile_rows = (diag_op.shape[1], diag_op.shape[2])
    coarse_width = local_rows.shape[1]
    slot_count = pair_counts.shape[1]
    per_slot = tile_blocks.shape[2] // slot_count
    forward_pair = shifted(
        jnp.stack([local_rows[-tile_rows:], upper_op[0, blocks_here - 1]]), "crow", 1
    )
    next_rows = shifted(local_rows[:tile_rows], "crow", -1)
    slot_of = {offset: index for index, offset in enumerate(offsets)}
    groups = (
        (slot_of[-across - 1], slot_of[-1], slot_of[across - 1]),
        (slot_of[-across + 1], slot_of[1], slot_of[across + 1]),
        (slot_of[-across],),
        (slot_of[across],),
    )
    down_out, up_out, near_down, near_up, own_masked, gram_part = local_apply(
        groups, tile_blocks, pair_counts, deflation, forward_pair, next_rows, diag_op, upper_op
    )
    row_share = coarse_width // crow_count
    corner = pivot_owner[0] * row_share
    pivot_part = lax.dynamic_slice(gram_part, (corner, corner), (row_share, row_share))
    pivot_parts = lax.all_to_all(
        jnp.broadcast_to(pivot_part[None], (crow_count, row_share, row_share)),
        "crow", 0, 0, tiled=True,
    )
    inverse = pivot_inverse(pivot_parts)
    last = sub_count - 1
    down = lax.ppermute(
        down_out, "sub", [(t, t - 1) for t in range(1, sub_count)] + [(0, last)]
    )
    up = lax.ppermute(up_out, "sub", [(t, t + 1) for t in range(last)] + [(last, 0)])
    far_down = lax.ppermute(
        jnp.concatenate([near_down, down[:1], up[:1]]),
        "sub",
        [(u, u - across) for u in range(across, sub_count)] + [(0, sub_count - across)],
    )
    far_up = lax.ppermute(
        jnp.concatenate([near_up, down[2:], up[2:]]),
        "sub",
        [(u, u + across) for u in range(sub_count - across)] + [(last, across - 1)],
    )
    assert offsets == [-across - 1, -across, -across + 1, -1, 1, across - 1, across, across + 1]
    outgoing_rows = coarse_rows(
        pivot_owner, gram_part, own_masked, down, up, far_down, far_up, crow_count
    )
    pieces = lax.all_to_all(outgoing_rows, "crow", 0, 0, tiled=True)
    return eliminate_panel(pivot_owner, pieces, inverse, coarse_width)


def solution(mesh):
    placed = (
        P("sub", "crow", None),
        P("sub", "crow", None, None),
        P("sub", "crow", None, None),
        P("sub", "crow", None),
        P("sub", None),
        P("sub"),
    )
    return jax.shard_map(
        per_device,
        mesh=mesh,
        in_specs=placed,
        out_specs=(P(("sub", "crow"), None), P(("sub", "crow"), None), P(("sub", "crow"), None)),
        check_vma=False,
    )
```

```python
import functools
import jax
import jax.numpy as jnp
from jax import lax
from jax.sharding import PartitionSpec as P
from jax.experimental import pallas as pl
from jax.experimental.pallas import tpu as pltpu


def padded_2(block, sides, width):
    for axis, dim in sides:
        count = lax.axis_size(axis)
        forward = [(i, i + 1) for i in range(count - 1)]
        backward = [(target, source) for source, target in forward]
        low = lax.ppermute(
            lax.slice_in_dim(block, block.shape[dim] - width, None, axis=dim), axis, forward
        )
        high = lax.ppermute(lax.slice_in_dim(block, 0, width, axis=dim), axis, backward)
        block = jnp.concatenate([low, block, high], axis=dim)
    return block


def shifted(value, axis, steps):
    count = lax.axis_size(axis)
    initial, last = (max(0, -steps), min(count, count - steps))
    return lax.ppermute(value, axis, [(source, source + steps) for source in range(initial, last)])


def broadcast(shard, axis, root):
    mine = lax.axis_index(axis) == root
    return lax.psum(jnp.where(mine, shard, jnp.zeros_like(shard)), axis)


def neighbour_offsets(across):
    return [-across - 1, -across, -across + 1, -1, 1, across - 1, across, across + 1]


def _ab(a, b):
    return lax.dot_general(a, b, (((1,), (0,)), ((), ())), preferred_element_type=jnp.float32)


def _atb(a, b):
    return lax.dot_general(a, b, (((0,), (0,)), ((), ())), preferred_element_type=jnp.float32)


def local_apply_kernel(
    groups, blocks_ref, counts_ref, z_ref, fp_ref, zn_ref, d_ref, u_ref, *refs
):
    group_refs, own_ref, gram_ref, app_ref = refs[:len(groups)], refs[-3], refs[-2], refs[-1]
    count, rows = d_ref.shape[1], d_ref.shape[2]
    per_slot = own_ref.shape[1]
    crow = lax.axis_index("crow")

    def rows_of(b):
        return z_ref[0, pl.ds(b * rows, rows), :]

    for b in range(count):
        if 0 < b < count - 1:
            left = jnp.concatenate([u_ref[0, b - 1].T, d_ref[0, b], u_ref[0, b]], 1)
            total = _ab(left, z_ref[0, pl.ds((b - 1) * rows, 3 * rows), :])
        else:
            below = fp_ref[0] if b == 0 else rows_of(b - 1)
            lower = fp_ref[1] if b == 0 else u_ref[0, b - 1]
            above = zn_ref[...] if b == count - 1 else rows_of(b + 1)
            total = (_ab(d_ref[0, b], rows_of(b)) + _ab(u_ref[0, b], above)) + _atb(lower, below)
        app_ref[pl.ds(b * rows, rows), :] = total.astype(app_ref.dtype)
    gram_ref[...] = _atb(z_ref[0], app_ref[...])
    for slot in range(own_ref.shape[0]):
        for unit in range(per_slot):
            start = pl.multiple_of(blocks_ref[0, 0, slot * per_slot + unit] * rows, rows)
            tile = z_ref[0, pl.ds(start, rows), :]
            live = crow * per_slot + unit < counts_ref[0, slot]
            own_ref[slot, unit] = jnp.where(live, tile, jnp.zeros_like(tile))
    for group, out_ref in zip(groups, group_refs):
        for place, slot in enumerate(group):
            for unit in range(per_slot):
                start = pl.multiple_of(blocks_ref[0, 0, slot * per_slot + unit] * rows, rows)
                out_ref[place, unit] = app_ref[pl.ds(start, rows), :]


def local_apply(groups, tile_blocks, pair_counts, deflation, forward_pair, next_rows, diag_op, upper_op):
    slots = pair_counts.shape[1]
    per_slot = tile_blocks.shape[2] // slots
    blocks, rows = diag_op.shape[1], diag_op.shape[2]
    width = deflation.shape[2]
    vmem = pl.BlockSpec(memory_space=pltpu.VMEM)
    smem = pl.BlockSpec(memory_space=pltpu.SMEM)
    tile = lambda n: jax.ShapeDtypeStruct((n, per_slot, rows, width), deflation.dtype)
    return pl.pallas_call(
        functools.partial(local_apply_kernel, groups),
        out_shape=tuple(tile(len(g)) for g in groups) + (
            tile(slots),
            jax.ShapeDtypeStruct((width, width), jnp.float32),
        ),
        in_specs=[smem, smem] + [vmem] * 5,
        out_specs=tuple(vmem for _ in range(len(groups) + 2)),
        scratch_shapes=[pltpu.VMEM((blocks * rows, width), deflation.dtype)],
    )(tile_blocks, pair_counts, deflation, forward_pair, next_rows, diag_op, upper_op)


def _exact(a, b, dims):
    return lax.dot_general(
        a, b, (dims, ((), ())), precision=lax.Precision.HIGHEST,
        preferred_element_type=jnp.float32,
    )


def pivot_inverse_kernel(blocks_ref, inverse_ref):
    share = inverse_ref.shape[0]
    pivot = (blocks_ref[0] + blocks_ref[1]) + (blocks_ref[2] + blocks_ref[3])
    pivot = (pivot + pivot.T) * 0.5
    row_id = lax.broadcasted_iota(jnp.int32, (share, 1), 0)
    work = jnp.concatenate([pivot, jnp.eye(share, dtype=jnp.float32)], 1)
    for k in range(share):
        row = work[k:k + 1, :]
        scale = lax.rsqrt(row[:, k:k + 1])
        unit_row = row * scale
        below = jnp.where(row_id > k, work[:, k:k + 1] * scale, 0.0)
        work = jnp.where(row_id == k, unit_row, work - below * unit_row)
    inverse_ref[...] = work[:, share:]


def pivot_inverse(blocks):
    share = blocks.shape[1]
    vmem = pl.BlockSpec(memory_space=pltpu.VMEM)
    return pl.pallas_call(
        pivot_inverse_kernel,
        out_shape=jax.ShapeDtypeStruct((share, share), jnp.float32),
        in_specs=[vmem],
        out_specs=vmem,
    )(blocks)


def panel_kernel(owner_ref, pieces_ref, inverse_ref, self_ref, coupling_ref, panel_ref):
    share = panel_ref.shape[0]
    width = self_ref.shape[1]
    total = (pieces_ref[0] + pieces_ref[1]) + (pieces_ref[2] + pieces_ref[3])
    own = total[:share]
    lead = total[share:]
    owner = owner_ref[0]
    columns = jnp.zeros((share, share), jnp.float32)
    for q in range(width // share):
        columns = jnp.where(owner == q, own[:, q * share:(q + 1) * share], columns)
    inverse = inverse_ref[...]
    solved = _exact(inverse, lead, ((1,), (0,)))
    panel = _exact(columns, inverse, ((1,), (1,)))
    updated = own - _exact(panel, solved, ((1,), (0,)))
    self_ref[...] = updated[:, :width]
    coupling_ref[...] = updated[:, width:]
    panel_ref[...] = panel


def eliminate_panel(owner, pieces, inverse, width):
    share = pieces.shape[1] // 2
    vmem = pl.BlockSpec(memory_space=pltpu.VMEM)
    return pl.pallas_call(
        panel_kernel,
        out_shape=(
            jax.ShapeDtypeStruct((share, width), jnp.float32),
            jax.ShapeDtypeStruct((share, pieces.shape[2] - width), jnp.float32),
            jax.ShapeDtypeStruct((share, share), jnp.float32),
        ),
        in_specs=[pl.BlockSpec(memory_space=pltpu.SMEM), vmem, vmem],
        out_specs=(vmem, vmem, vmem),
    )(owner, pieces, inverse)


def coarse_rows_kernel(owner_ref, gram_ref, own_ref, down_ref, up_ref, fdn_ref, fup_ref, out_ref, whole_ref):
    width = gram_ref.shape[0]
    share = out_ref.shape[1] // 2
    sources = {
        0: (fup_ref, 2), 1: (fup_ref, 0), 2: (fup_ref, 1), 3: (up_ref, 1),
        4: (down_ref, 1), 5: (fdn_ref, 2), 6: (fdn_ref, 0), 7: (fdn_ref, 1),
    }
    whole_ref[:, :width] = gram_ref[...]
    for slot in range(own_ref.shape[0]):
        ref, place = sources[slot]
        block = _atb(own_ref[slot, 0], ref[place, 0])
        for unit in range(1, own_ref.shape[1]):
            block = block + _atb(own_ref[slot, unit], ref[place, unit])
        whole_ref[:, (slot + 1) * width:(slot + 2) * width] = block
    start = pl.multiple_of(owner_ref[0] * share, share)
    pivot = whole_ref[pl.ds(start, share), :]
    for target in range(out_ref.shape[0]):
        out_ref[target, :share] = whole_ref[target * share:(target + 1) * share, :]
        out_ref[target, share:] = pivot


def coarse_rows(owner, gram, own, down, up, far_down, far_up, crow_count):
    width = gram.shape[0]
    share = width // crow_count
    columns = width * (own.shape[0] + 1)
    vmem = pl.BlockSpec(memory_space=pltpu.VMEM)
    return pl.pallas_call(
        coarse_rows_kernel,
        out_shape=jax.ShapeDtypeStruct((crow_count, 2 * share, columns), jnp.float32),
        in_specs=[pl.BlockSpec(memory_space=pltpu.SMEM)] + [vmem] * 6,
        out_specs=vmem,
        scratch_shapes=[pltpu.VMEM((width, columns), jnp.float32)],
    )(owner, gram, own, down, up, far_down, far_up)


def per_device(deflation, diag_op, upper_op, tile_blocks, pair_counts, pivot_owner):
    crow_count = lax.axis_size("crow")
    crow_place = lax.axis_index("crow")
    sub_count = lax.axis_size("sub")
    across = min(16, sub_count // 2)
    offsets = neighbour_offsets(across)
    local_rows = deflation[0]
    blocks_here, tile_rows = (diag_op.shape[1], diag_op.shape[2])
    coarse_width = local_rows.shape[1]
    slot_count = pair_counts.shape[1]
    per_slot = tile_blocks.shape[2] // slot_count
    forward_pair = shifted(
        jnp.stack([local_rows[-tile_rows:], upper_op[0, blocks_here - 1]]), "crow", 1
    )
    next_rows = shifted(local_rows[:tile_rows], "crow", -1)
    slot_of = {offset: index for index, offset in enumerate(offsets)}
    groups = (
        (slot_of[-across - 1], slot_of[-1], slot_of[across - 1]),
        (slot_of[-across + 1], slot_of[1], slot_of[across + 1]),
        (slot_of[-across],),
        (slot_of[across],),
    )
    down_out, up_out, near_down, near_up, own_masked, gram_part = local_apply(
        groups, tile_blocks, pair_counts, deflation, forward_pair, next_rows, diag_op, upper_op
    )
    row_share = coarse_width // crow_count
    corner = pivot_owner[0] * row_share
    pivot_part = lax.dynamic_slice(gram_part, (corner, corner), (row_share, row_share))
    pivot_parts = lax.all_to_all(
        jnp.broadcast_to(pivot_part[None], (crow_count, row_share, row_share)),
        "crow", 0, 0, tiled=True,
    )
    inverse = pivot_inverse(pivot_parts)
    last = sub_count - 1
    down = lax.ppermute(
        down_out, "sub", [(t, t - 1) for t in range(1, sub_count)] + [(0, last)]
    )
    up = lax.ppermute(up_out, "sub", [(t, t + 1) for t in range(last)] + [(last, 0)])
    far_down = lax.ppermute(
        jnp.concatenate([near_down, down[:1], up[:1]]),
        "sub",
        [(u, u - across) for u in range(across, sub_count)] + [(0, sub_count - across)],
    )
    far_up = lax.ppermute(
        jnp.concatenate([near_up, down[2:], up[2:]]),
        "sub",
        [(u, u + across) for u in range(sub_count - across)] + [(last, across - 1)],
    )
    assert offsets == [-across - 1, -across, -across + 1, -1, 1, across - 1, across, across + 1]
    outgoing_rows = coarse_rows(
        pivot_owner, gram_part, own_masked, down, up, far_down, far_up, crow_count
    )
    pieces = lax.all_to_all(outgoing_rows, "crow", 0, 0, tiled=True)
    return eliminate_panel(pivot_owner, pieces, inverse, coarse_width)


def solution(mesh):
    placed = (
        P("sub", "crow", None),
        P("sub", "crow", None, None),
        P("sub", "crow", None, None),
        P("sub", "crow", None),
        P("sub", None),
        P("sub"),
    )
    return jax.shard_map(
        per_device,
        mesh=mesh,
        in_specs=placed,
        out_specs=(P(("sub", "crow"), None), P(("sub", "crow"), None), P(("sub", "crow"), None)),
        check_vma=False,
    )
```

```python
import functools
import jax
import jax.numpy as jnp
from jax import lax
from jax.sharding import PartitionSpec as P
from jax.experimental import pallas as pl
from jax.experimental.pallas import tpu as pltpu


def padded_2(block, sides, width):
    for axis, dim in sides:
        count = lax.axis_size(axis)
        forward = [(i, i + 1) for i in range(count - 1)]
        backward = [(target, source) for source, target in forward]
        low = lax.ppermute(
            lax.slice_in_dim(block, block.shape[dim] - width, None, axis=dim), axis, forward
        )
        high = lax.ppermute(lax.slice_in_dim(block, 0, width, axis=dim), axis, backward)
        block = jnp.concatenate([low, block, high], axis=dim)
    return block


def shifted(value, axis, steps):
    count = lax.axis_size(axis)
    initial, last = (max(0, -steps), min(count, count - steps))
    return lax.ppermute(value, axis, [(source, source + steps) for source in range(initial, last)])


def broadcast(shard, axis, root):
    mine = lax.axis_index(axis) == root
    return lax.psum(jnp.where(mine, shard, jnp.zeros_like(shard)), axis)


def neighbour_offsets(across):
    return [-across - 1, -across, -across + 1, -1, 1, across - 1, across, across + 1]


def _ab(a, b):
    return lax.dot_general(a, b, (((1,), (0,)), ((), ())), preferred_element_type=jnp.float32)


def _atb(a, b):
    return lax.dot_general(a, b, (((0,), (0,)), ((), ())), preferred_element_type=jnp.float32)


def local_apply_kernel(
    groups, blocks_ref, counts_ref, z_hbm, fp_ref, zn_ref, d_hbm, u_hbm, *refs
):
    group_refs = refs[:len(groups)]
    own_ref, gram_ref, app_ref, z_ref, d_ref, u_ref, sems = refs[len(groups):]
    count, rows = d_ref.shape[0], d_ref.shape[1]
    per_slot = own_ref.shape[1]
    crow = lax.axis_index("crow")
    copies = {}
    for b in range(count):
        for kind, (src, dst) in enumerate((
            (z_hbm.at[0, pl.ds(b * rows, rows)], z_ref.at[pl.ds(b * rows, rows)]),
            (d_hbm.at[0, b], d_ref.at[b]),
            (u_hbm.at[0, b], u_ref.at[b]),
        )):
            copy = pltpu.make_async_copy(src, dst, sems.at[kind, b])
            copy.start()
            copies[kind, b] = copy

    def need(kind, b):
        if (kind, b) in copies:
            copies.pop((kind, b)).wait()

    def rows_of(b):
        return z_ref[pl.ds(b * rows, rows), :]

    for b in range(count):
        for step in (b - 1, b, b + 1):
            if 0 <= step < count:
                need(0, step)
        need(1, b)
        need(2, b)
        below = fp_ref[0] if b == 0 else rows_of(b - 1)
        lower = fp_ref[1] if b == 0 else u_ref[b - 1]
        above = zn_ref[...] if b == count - 1 else rows_of(b + 1)
        total = (_ab(d_ref[b], rows_of(b)) + _ab(u_ref[b], above)) + _atb(lower, below)
        app_ref[pl.ds(b * rows, rows), :] = total.astype(app_ref.dtype)
    gram_ref[...] = _atb(z_ref[...], app_ref[...])
    for slot in range(own_ref.shape[0]):
        for unit in range(per_slot):
            start = pl.multiple_of(blocks_ref[0, 0, slot * per_slot + unit] * rows, rows)
            tile = z_ref[pl.ds(start, rows), :]
            live = crow * per_slot + unit < counts_ref[0, slot]
            own_ref[slot, unit] = jnp.where(live, tile, jnp.zeros_like(tile))
    for group, out_ref in zip(groups, group_refs):
        for place, slot in enumerate(group):
            for unit in range(per_slot):
                start = pl.multiple_of(blocks_ref[0, 0, slot * per_slot + unit] * rows, rows)
                out_ref[place, unit] = app_ref[pl.ds(start, rows), :]


def local_apply(groups, tile_blocks, pair_counts, deflation, forward_pair, next_rows, diag_op, upper_op):
    slots = pair_counts.shape[1]
    per_slot = tile_blocks.shape[2] // slots
    blocks, rows = diag_op.shape[1], diag_op.shape[2]
    width = deflation.shape[2]
    vmem = pl.BlockSpec(memory_space=pltpu.VMEM)
    smem = pl.BlockSpec(memory_space=pltpu.SMEM)
    hbm = pl.BlockSpec(memory_space=pl.ANY)
    tile = lambda n: jax.ShapeDtypeStruct((n, per_slot, rows, width), deflation.dtype)
    return pl.pallas_call(
        functools.partial(local_apply_kernel, groups),
        out_shape=tuple(tile(len(g)) for g in groups) + (
            tile(slots),
            jax.ShapeDtypeStruct((width, width), jnp.float32),
        ),
        in_specs=[smem, smem, hbm, vmem, vmem, hbm, hbm],
        out_specs=tuple(vmem for _ in range(len(groups) + 2)),
        scratch_shapes=[
            pltpu.VMEM((blocks * rows, width), deflation.dtype),
            pltpu.VMEM((blocks * rows, width), deflation.dtype),
            pltpu.VMEM((blocks, rows, rows), diag_op.dtype),
            pltpu.VMEM((blocks, rows, rows), upper_op.dtype),
            pltpu.SemaphoreType.DMA((3, blocks)),
        ],
    )(tile_blocks, pair_counts, deflation, forward_pair, next_rows, diag_op, upper_op)


def _exact(a, b, dims):
    return lax.dot_general(
        a, b, (dims, ((), ())), precision=lax.Precision.HIGHEST,
        preferred_element_type=jnp.float32,
    )


def pivot_inverse_kernel(blocks_ref, inverse_ref):
    share = inverse_ref.shape[0]
    pivot = (blocks_ref[0] + blocks_ref[1]) + (blocks_ref[2] + blocks_ref[3])
    pivot = (pivot + pivot.T) * 0.5
    row_id = lax.broadcasted_iota(jnp.int32, (share, 1), 0)
    work = jnp.concatenate([pivot, jnp.eye(share, dtype=jnp.float32)], 1)
    for k in range(share):
        row = work[k:k + 1, :]
        scale = lax.rsqrt(row[:, k:k + 1])
        unit_row = row * scale
        below = jnp.where(row_id > k, work[:, k:k + 1] * scale, 0.0)
        work = jnp.where(row_id == k, unit_row, work - below * unit_row)
    inverse_ref[...] = work[:, share:]


def pivot_inverse(blocks):
    share = blocks.shape[1]
    vmem = pl.BlockSpec(memory_space=pltpu.VMEM)
    return pl.pallas_call(
        pivot_inverse_kernel,
        out_shape=jax.ShapeDtypeStruct((share, share), jnp.float32),
        in_specs=[vmem],
        out_specs=vmem,
    )(blocks)


def panel_kernel(owner_ref, pieces_ref, inverse_ref, self_ref, coupling_ref, panel_ref):
    share = panel_ref.shape[0]
    width = self_ref.shape[1]
    total = (pieces_ref[0] + pieces_ref[1]) + (pieces_ref[2] + pieces_ref[3])
    own = total[:share]
    lead = total[share:]
    owner = owner_ref[0]
    columns = jnp.zeros((share, share), jnp.float32)
    for q in range(width // share):
        columns = jnp.where(owner == q, own[:, q * share:(q + 1) * share], columns)
    inverse = inverse_ref[...]
    solved = _exact(inverse, lead, ((1,), (0,)))
    panel = _exact(columns, inverse, ((1,), (1,)))
    updated = own - _exact(panel, solved, ((1,), (0,)))
    self_ref[...] = updated[:, :width]
    coupling_ref[...] = updated[:, width:]
    panel_ref[...] = panel


def eliminate_panel(owner, pieces, inverse, width):
    share = pieces.shape[1] // 2
    vmem = pl.BlockSpec(memory_space=pltpu.VMEM)
    return pl.pallas_call(
        panel_kernel,
        out_shape=(
            jax.ShapeDtypeStruct((share, width), jnp.float32),
            jax.ShapeDtypeStruct((share, pieces.shape[2] - width), jnp.float32),
            jax.ShapeDtypeStruct((share, share), jnp.float32),
        ),
        in_specs=[pl.BlockSpec(memory_space=pltpu.SMEM), vmem, vmem],
        out_specs=(vmem, vmem, vmem),
    )(owner, pieces, inverse)


def coarse_rows_kernel(owner_ref, gram_ref, own_ref, down_ref, up_ref, fdn_ref, fup_ref, out_ref, whole_ref):
    width = gram_ref.shape[0]
    share = out_ref.shape[1] // 2
    sources = {
        0: (fup_ref, 2), 1: (fup_ref, 0), 2: (fup_ref, 1), 3: (up_ref, 1),
        4: (down_ref, 1), 5: (fdn_ref, 2), 6: (fdn_ref, 0), 7: (fdn_ref, 1),
    }
    whole_ref[:, :width] = gram_ref[...]
    for slot in range(own_ref.shape[0]):
        ref, place = sources[slot]
        block = _atb(own_ref[slot, 0], ref[place, 0])
        for unit in range(1, own_ref.shape[1]):
            block = block + _atb(own_ref[slot, unit], ref[place, unit])
        whole_ref[:, (slot + 1) * width:(slot + 2) * width] = block
    start = pl.multiple_of(owner_ref[0] * share, share)
    pivot = whole_ref[pl.ds(start, share), :]
    for target in range(out_ref.shape[0]):
        out_ref[target, :share] = whole_ref[target * share:(target + 1) * share, :]
        out_ref[target, share:] = pivot


def coarse_rows(owner, gram, own, down, up, far_down, far_up, crow_count):
    width = gram.shape[0]
    share = width // crow_count
    columns = width * (own.shape[0] + 1)
    vmem = pl.BlockSpec(memory_space=pltpu.VMEM)
    return pl.pallas_call(
        coarse_rows_kernel,
        out_shape=jax.ShapeDtypeStruct((crow_count, 2 * share, columns), jnp.float32),
        in_specs=[pl.BlockSpec(memory_space=pltpu.SMEM)] + [vmem] * 6,
        out_specs=vmem,
        scratch_shapes=[pltpu.VMEM((width, columns), jnp.float32)],
    )(owner, gram, own, down, up, far_down, far_up)


def per_device(deflation, diag_op, upper_op, tile_blocks, pair_counts, pivot_owner):
    crow_count = lax.axis_size("crow")
    crow_place = lax.axis_index("crow")
    sub_count = lax.axis_size("sub")
    across = min(16, sub_count // 2)
    offsets = neighbour_offsets(across)
    local_rows = deflation[0]
    blocks_here, tile_rows = (diag_op.shape[1], diag_op.shape[2])
    coarse_width = local_rows.shape[1]
    slot_count = pair_counts.shape[1]
    per_slot = tile_blocks.shape[2] // slot_count
    forward_pair = shifted(
        jnp.stack([local_rows[-tile_rows:], upper_op[0, blocks_here - 1]]), "crow", 1
    )
    next_rows = shifted(local_rows[:tile_rows], "crow", -1)
    slot_of = {offset: index for index, offset in enumerate(offsets)}
    groups = (
        (slot_of[-across - 1], slot_of[-1], slot_of[across - 1]),
        (slot_of[-across + 1], slot_of[1], slot_of[across + 1]),
        (slot_of[-across],),
        (slot_of[across],),
    )
    down_out, up_out, near_down, near_up, own_masked, gram_part = local_apply(
        groups, tile_blocks, pair_counts, deflation, forward_pair, next_rows, diag_op, upper_op
    )
    row_share = coarse_width // crow_count
    corner = pivot_owner[0] * row_share
    pivot_part = lax.dynamic_slice(gram_part, (corner, corner), (row_share, row_share))
    pivot_parts = lax.all_to_all(
        jnp.broadcast_to(pivot_part[None], (crow_count, row_share, row_share)),
        "crow", 0, 0, tiled=True,
    )
    inverse = pivot_inverse(pivot_parts)
    last = sub_count - 1
    down = lax.ppermute(
        down_out, "sub", [(t, t - 1) for t in range(1, sub_count)] + [(0, last)]
    )
    up = lax.ppermute(up_out, "sub", [(t, t + 1) for t in range(last)] + [(last, 0)])
    far_down = lax.ppermute(
        jnp.concatenate([near_down, down[:1], up[:1]]),
        "sub",
        [(u, u - across) for u in range(across, sub_count)] + [(0, sub_count - across)],
    )
    far_up = lax.ppermute(
        jnp.concatenate([near_up, down[2:], up[2:]]),
        "sub",
        [(u, u + across) for u in range(sub_count - across)] + [(last, across - 1)],
    )
    assert offsets == [-across - 1, -across, -across + 1, -1, 1, across - 1, across, across + 1]
    outgoing_rows = coarse_rows(
        pivot_owner, gram_part, own_masked, down, up, far_down, far_up, crow_count
    )
    pieces = lax.all_to_all(outgoing_rows, "crow", 0, 0, tiled=True)
    return eliminate_panel(pivot_owner, pieces, inverse, coarse_width)


def solution(mesh):
    placed = (
        P("sub", "crow", None),
        P("sub", "crow", None, None),
        P("sub", "crow", None, None),
        P("sub", "crow", None),
        P("sub", None),
        P("sub"),
    )
    return jax.shard_map(
        per_device,
        mesh=mesh,
        in_specs=placed,
        out_specs=(P(("sub", "crow"), None), P(("sub", "crow"), None), P(("sub", "crow"), None)),
        check_vma=False,
    )
```

```python
import functools
import jax
import jax.numpy as jnp
from jax import lax
from jax.sharding import PartitionSpec as P
from jax.experimental import pallas as pl
from jax.experimental.pallas import tpu as pltpu


def padded_2(block, sides, width):
    for axis, dim in sides:
        count = lax.axis_size(axis)
        forward = [(i, i + 1) for i in range(count - 1)]
        backward = [(target, source) for source, target in forward]
        low = lax.ppermute(
            lax.slice_in_dim(block, block.shape[dim] - width, None, axis=dim), axis, forward
        )
        high = lax.ppermute(lax.slice_in_dim(block, 0, width, axis=dim), axis, backward)
        block = jnp.concatenate([low, block, high], axis=dim)
    return block


def shifted(value, axis, steps):
    count = lax.axis_size(axis)
    initial, last = (max(0, -steps), min(count, count - steps))
    return lax.ppermute(value, axis, [(source, source + steps) for source in range(initial, last)])


def broadcast(shard, axis, root):
    mine = lax.axis_index(axis) == root
    return lax.psum(jnp.where(mine, shard, jnp.zeros_like(shard)), axis)


def neighbour_offsets(across):
    return [-across - 1, -across, -across + 1, -1, 1, across - 1, across, across + 1]


def _ab(a, b):
    return lax.dot_general(a, b, (((1,), (0,)), ((), ())), preferred_element_type=jnp.float32)


def _atb(a, b):
    return lax.dot_general(a, b, (((0,), (0,)), ((), ())), preferred_element_type=jnp.float32)


def local_apply_kernel(
    groups, blocks_ref, counts_ref, z_hbm, fp_ref, zn_ref, d_hbm, u_hbm, *refs
):
    group_refs = refs[:len(groups)]
    own_ref, gram_ref, app_ref, z_ref, d_ref, u_ref, sems = refs[len(groups):]
    count, rows = d_ref.shape[0], d_ref.shape[1]
    per_slot = own_ref.shape[1]
    crow = lax.axis_index("crow")
    half = count // 2
    spans = ((0, half), (half, count - half))
    copies = {}
    for part, (first, size) in enumerate(spans):
        for kind, (src, dst) in enumerate((
            (z_hbm.at[0, pl.ds(first * rows, size * rows)], z_ref.at[pl.ds(first * rows, size * rows)]),
            (d_hbm.at[0, pl.ds(first, size)], d_ref.at[pl.ds(first, size)]),
            (u_hbm.at[0, pl.ds(first, size)], u_ref.at[pl.ds(first, size)]),
        )):
            copy = pltpu.make_async_copy(src, dst, sems.at[kind, part])
            copy.start()
            copies[kind, part] = copy

    def need(kind, b):
        part = 0 if b < half else 1
        if (kind, part) in copies:
            copies.pop((kind, part)).wait()

    def rows_of(b):
        return z_ref[pl.ds(b * rows, rows), :]

    for b in range(count):
        for step in (b - 1, b, b + 1):
            if 0 <= step < count:
                need(0, step)
        need(1, b)
        need(2, b)
        below = fp_ref[0] if b == 0 else rows_of(b - 1)
        lower = fp_ref[1] if b == 0 else u_ref[b - 1]
        above = zn_ref[...] if b == count - 1 else rows_of(b + 1)
        total = (_ab(d_ref[b], rows_of(b)) + _ab(u_ref[b], above)) + _atb(lower, below)
        app_ref[pl.ds(b * rows, rows), :] = total.astype(app_ref.dtype)
    gram_ref[...] = _atb(z_ref[...], app_ref[...])
    for slot in range(own_ref.shape[0]):
        for unit in range(per_slot):
            start = pl.multiple_of(blocks_ref[0, 0, slot * per_slot + unit] * rows, rows)
            tile = z_ref[pl.ds(start, rows), :]
            live = crow * per_slot + unit < counts_ref[0, slot]
            own_ref[slot, unit] = jnp.where(live, tile, jnp.zeros_like(tile))
    for group, out_ref in zip(groups, group_refs):
        for place, slot in enumerate(group):
            for unit in range(per_slot):
                start = pl.multiple_of(blocks_ref[0, 0, slot * per_slot + unit] * rows, rows)
                out_ref[place, unit] = app_ref[pl.ds(start, rows), :]


def local_apply(groups, tile_blocks, pair_counts, deflation, forward_pair, next_rows, diag_op, upper_op):
    slots = pair_counts.shape[1]
    per_slot = tile_blocks.shape[2] // slots
    blocks, rows = diag_op.shape[1], diag_op.shape[2]
    width = deflation.shape[2]
    vmem = pl.BlockSpec(memory_space=pltpu.VMEM)
    smem = pl.BlockSpec(memory_space=pltpu.SMEM)
    hbm = pl.BlockSpec(memory_space=pl.ANY)
    tile = lambda n: jax.ShapeDtypeStruct((n, per_slot, rows, width), deflation.dtype)
    return pl.pallas_call(
        functools.partial(local_apply_kernel, groups),
        out_shape=tuple(tile(len(g)) for g in groups) + (
            tile(slots),
            jax.ShapeDtypeStruct((width, width), jnp.float32),
        ),
        in_specs=[smem, smem, hbm, vmem, vmem, hbm, hbm],
        out_specs=tuple(vmem for _ in range(len(groups) + 2)),
        scratch_shapes=[
            pltpu.VMEM((blocks * rows, width), deflation.dtype),
            pltpu.VMEM((blocks * rows, width), deflation.dtype),
            pltpu.VMEM((blocks, rows, rows), diag_op.dtype),
            pltpu.VMEM((blocks, rows, rows), upper_op.dtype),
            pltpu.SemaphoreType.DMA((3, 2)),
        ],
    )(tile_blocks, pair_counts, deflation, forward_pair, next_rows, diag_op, upper_op)


def _exact(a, b, dims):
    return lax.dot_general(
        a, b, (dims, ((), ())), precision=lax.Precision.HIGHEST,
        preferred_element_type=jnp.float32,
    )


def pivot_inverse_kernel(blocks_ref, inverse_ref):
    share = inverse_ref.shape[0]
    pivot = (blocks_ref[0] + blocks_ref[1]) + (blocks_ref[2] + blocks_ref[3])
    pivot = (pivot + pivot.T) * 0.5
    row_id = lax.broadcasted_iota(jnp.int32, (share, 1), 0)
    work = jnp.concatenate([pivot, jnp.eye(share, dtype=jnp.float32)], 1)
    for k in range(share):
        row = work[k:k + 1, :]
        scale = lax.rsqrt(row[:, k:k + 1])
        unit_row = row * scale
        below = jnp.where(row_id > k, work[:, k:k + 1] * scale, 0.0)
        work = jnp.where(row_id == k, unit_row, work - below * unit_row)
    inverse_ref[...] = work[:, share:]


def pivot_inverse(blocks):
    share = blocks.shape[1]
    vmem = pl.BlockSpec(memory_space=pltpu.VMEM)
    return pl.pallas_call(
        pivot_inverse_kernel,
        out_shape=jax.ShapeDtypeStruct((share, share), jnp.float32),
        in_specs=[vmem],
        out_specs=vmem,
    )(blocks)


def panel_kernel(owner_ref, pieces_ref, inverse_ref, self_ref, coupling_ref, panel_ref):
    share = panel_ref.shape[0]
    width = self_ref.shape[1]
    total = (pieces_ref[0] + pieces_ref[1]) + (pieces_ref[2] + pieces_ref[3])
    own = total[:share]
    lead = total[share:]
    owner = owner_ref[0]
    columns = jnp.zeros((share, share), jnp.float32)
    for q in range(width // share):
        columns = jnp.where(owner == q, own[:, q * share:(q + 1) * share], columns)
    inverse = inverse_ref[...]
    solved = _exact(inverse, lead, ((1,), (0,)))
    panel = _exact(columns, inverse, ((1,), (1,)))
    updated = own - _exact(panel, solved, ((1,), (0,)))
    self_ref[...] = updated[:, :width]
    coupling_ref[...] = updated[:, width:]
    panel_ref[...] = panel


def eliminate_panel(owner, pieces, inverse, width):
    share = pieces.shape[1] // 2
    vmem = pl.BlockSpec(memory_space=pltpu.VMEM)
    return pl.pallas_call(
        panel_kernel,
        out_shape=(
            jax.ShapeDtypeStruct((share, width), jnp.float32),
            jax.ShapeDtypeStruct((share, pieces.shape[2] - width), jnp.float32),
            jax.ShapeDtypeStruct((share, share), jnp.float32),
        ),
        in_specs=[pl.BlockSpec(memory_space=pltpu.SMEM), vmem, vmem],
        out_specs=(vmem, vmem, vmem),
    )(owner, pieces, inverse)


def coarse_rows_kernel(owner_ref, gram_ref, own_ref, down_ref, up_ref, fdn_ref, fup_ref, out_ref, whole_ref):
    width = gram_ref.shape[0]
    share = out_ref.shape[1] // 2
    sources = {
        0: (fup_ref, 2), 1: (fup_ref, 0), 2: (fup_ref, 1), 3: (up_ref, 1),
        4: (down_ref, 1), 5: (fdn_ref, 2), 6: (fdn_ref, 0), 7: (fdn_ref, 1),
    }
    whole_ref[:, :width] = gram_ref[...]
    for slot in range(own_ref.shape[0]):
        ref, place = sources[slot]
        block = _atb(own_ref[slot, 0], ref[place, 0])
        for unit in range(1, own_ref.shape[1]):
            block = block + _atb(own_ref[slot, unit], ref[place, unit])
        whole_ref[:, (slot + 1) * width:(slot + 2) * width] = block
    start = pl.multiple_of(owner_ref[0] * share, share)
    pivot = whole_ref[pl.ds(start, share), :]
    for target in range(out_ref.shape[0]):
        out_ref[target, :share] = whole_ref[target * share:(target + 1) * share, :]
        out_ref[target, share:] = pivot


def coarse_rows(owner, gram, own, down, up, far_down, far_up, crow_count):
    width = gram.shape[0]
    share = width // crow_count
    columns = width * (own.shape[0] + 1)
    vmem = pl.BlockSpec(memory_space=pltpu.VMEM)
    return pl.pallas_call(
        coarse_rows_kernel,
        out_shape=jax.ShapeDtypeStruct((crow_count, 2 * share, columns), jnp.float32),
        in_specs=[pl.BlockSpec(memory_space=pltpu.SMEM)] + [vmem] * 6,
        out_specs=vmem,
        scratch_shapes=[pltpu.VMEM((width, columns), jnp.float32)],
    )(owner, gram, own, down, up, far_down, far_up)


def per_device(deflation, diag_op, upper_op, tile_blocks, pair_counts, pivot_owner):
    crow_count = lax.axis_size("crow")
    crow_place = lax.axis_index("crow")
    sub_count = lax.axis_size("sub")
    across = min(16, sub_count // 2)
    offsets = neighbour_offsets(across)
    local_rows = deflation[0]
    blocks_here, tile_rows = (diag_op.shape[1], diag_op.shape[2])
    coarse_width = local_rows.shape[1]
    slot_count = pair_counts.shape[1]
    per_slot = tile_blocks.shape[2] // slot_count
    forward_pair = shifted(
        jnp.stack([local_rows[-tile_rows:], upper_op[0, blocks_here - 1]]), "crow", 1
    )
    next_rows = shifted(local_rows[:tile_rows], "crow", -1)
    slot_of = {offset: index for index, offset in enumerate(offsets)}
    groups = (
        (slot_of[-across - 1], slot_of[-1], slot_of[across - 1]),
        (slot_of[-across + 1], slot_of[1], slot_of[across + 1]),
        (slot_of[-across],),
        (slot_of[across],),
    )
    down_out, up_out, near_down, near_up, own_masked, gram_part = local_apply(
        groups, tile_blocks, pair_counts, deflation, forward_pair, next_rows, diag_op, upper_op
    )
    row_share = coarse_width // crow_count
    corner = pivot_owner[0] * row_share
    pivot_part = lax.dynamic_slice(gram_part, (corner, corner), (row_share, row_share))
    pivot_parts = lax.all_to_all(
        jnp.broadcast_to(pivot_part[None], (crow_count, row_share, row_share)),
        "crow", 0, 0, tiled=True,
    )
    inverse = pivot_inverse(pivot_parts)
    last = sub_count - 1
    down = lax.ppermute(
        down_out, "sub", [(t, t - 1) for t in range(1, sub_count)] + [(0, last)]
    )
    up = lax.ppermute(up_out, "sub", [(t, t + 1) for t in range(last)] + [(last, 0)])
    far_down = lax.ppermute(
        jnp.concatenate([near_down, down[:1], up[:1]]),
        "sub",
        [(u, u - across) for u in range(across, sub_count)] + [(0, sub_count - across)],
    )
    far_up = lax.ppermute(
        jnp.concatenate([near_up, down[2:], up[2:]]),
        "sub",
        [(u, u + across) for u in range(sub_count - across)] + [(last, across - 1)],
    )
    assert offsets == [-across - 1, -across, -across + 1, -1, 1, across - 1, across, across + 1]
    outgoing_rows = coarse_rows(
        pivot_owner, gram_part, own_masked, down, up, far_down, far_up, crow_count
    )
    pieces = lax.all_to_all(outgoing_rows, "crow", 0, 0, tiled=True)
    return eliminate_panel(pivot_owner, pieces, inverse, coarse_width)


def solution(mesh):
    placed = (
        P("sub", "crow", None),
        P("sub", "crow", None, None),
        P("sub", "crow", None, None),
        P("sub", "crow", None),
        P("sub", None),
        P("sub"),
    )
    return jax.shard_map(
        per_device,
        mesh=mesh,
        in_specs=placed,
        out_specs=(P(("sub", "crow"), None), P(("sub", "crow"), None), P(("sub", "crow"), None)),
        check_vma=False,
    )
```

```python
import functools
import jax
import jax.numpy as jnp
from jax import lax
from jax.sharding import PartitionSpec as P
from jax.experimental import pallas as pl
from jax.experimental.pallas import tpu as pltpu


def padded_2(block, sides, width):
    for axis, dim in sides:
        count = lax.axis_size(axis)
        forward = [(i, i + 1) for i in range(count - 1)]
        backward = [(target, source) for source, target in forward]
        low = lax.ppermute(
            lax.slice_in_dim(block, block.shape[dim] - width, None, axis=dim), axis, forward
        )
        high = lax.ppermute(lax.slice_in_dim(block, 0, width, axis=dim), axis, backward)
        block = jnp.concatenate([low, block, high], axis=dim)
    return block


def shifted(value, axis, steps):
    count = lax.axis_size(axis)
    initial, last = (max(0, -steps), min(count, count - steps))
    return lax.ppermute(value, axis, [(source, source + steps) for source in range(initial, last)])


def broadcast(shard, axis, root):
    mine = lax.axis_index(axis) == root
    return lax.psum(jnp.where(mine, shard, jnp.zeros_like(shard)), axis)


def neighbour_offsets(across):
    return [-across - 1, -across, -across + 1, -1, 1, across - 1, across, across + 1]


def _ab(a, b):
    return lax.dot_general(a, b, (((1,), (0,)), ((), ())), preferred_element_type=jnp.float32)


def _atb(a, b):
    return lax.dot_general(a, b, (((0,), (0,)), ((), ())), preferred_element_type=jnp.float32)


def local_apply_kernel(
    groups, blocks_ref, counts_ref, z_ref, fp_ref, zn_ref, d_ref, u_ref, *refs
):
    group_refs, own_ref, gram_ref, app_ref = refs[:len(groups)], refs[-3], refs[-2], refs[-1]
    count, rows = d_ref.shape[1], d_ref.shape[2]
    per_slot = own_ref.shape[1]
    crow = lax.axis_index("crow")

    def rows_of(b):
        return z_ref[0, pl.ds(b * rows, rows), :]

    for b in range(count):
        below = fp_ref[0] if b == 0 else rows_of(b - 1)
        lower = fp_ref[1] if b == 0 else u_ref[0, b - 1]
        above = zn_ref[...] if b == count - 1 else rows_of(b + 1)
        total = (_ab(d_ref[0, b], rows_of(b)) + _ab(u_ref[0, b], above)) + _atb(lower, below)
        app_ref[pl.ds(b * rows, rows), :] = total.astype(app_ref.dtype)
    gram_ref[...] = _atb(z_ref[0], app_ref[...])
    for slot in range(own_ref.shape[0]):
        for unit in range(per_slot):
            start = pl.multiple_of(blocks_ref[0, 0, slot * per_slot + unit] * rows, rows)
            tile = z_ref[0, pl.ds(start, rows), :]
            live = crow * per_slot + unit < counts_ref[0, slot]
            own_ref[slot, unit] = jnp.where(live, tile, jnp.zeros_like(tile))
    for group, out_ref in zip(groups, group_refs):
        for place, slot in enumerate(group):
            for unit in range(per_slot):
                start = pl.multiple_of(blocks_ref[0, 0, slot * per_slot + unit] * rows, rows)
                out_ref[place, unit] = app_ref[pl.ds(start, rows), :]


def local_apply(groups, tile_blocks, pair_counts, deflation, forward_pair, next_rows, diag_op, upper_op):
    slots = pair_counts.shape[1]
    per_slot = tile_blocks.shape[2] // slots
    blocks, rows = diag_op.shape[1], diag_op.shape[2]
    width = deflation.shape[2]
    vmem = pl.BlockSpec(memory_space=pltpu.VMEM)
    smem = pl.BlockSpec(memory_space=pltpu.SMEM)
    tile = lambda n: jax.ShapeDtypeStruct((n, per_slot, rows, width), deflation.dtype)
    return pl.pallas_call(
        functools.partial(local_apply_kernel, groups),
        out_shape=tuple(tile(len(g)) for g in groups) + (
            tile(slots),
            jax.ShapeDtypeStruct((width, width), jnp.float32),
        ),
        in_specs=[smem, smem] + [vmem] * 5,
        out_specs=tuple(vmem for _ in range(len(groups) + 2)),
        scratch_shapes=[pltpu.VMEM((blocks * rows, width), deflation.dtype)],
    )(tile_blocks, pair_counts, deflation, forward_pair, next_rows, diag_op, upper_op)


def _exact(a, b, dims):
    return lax.dot_general(
        a, b, (dims, ((), ())), precision=lax.Precision.HIGHEST,
        preferred_element_type=jnp.float32,
    )


def pivot_inverse_kernel(blocks_ref, inverse_ref):
    share = inverse_ref.shape[0]
    pivot = (blocks_ref[0] + blocks_ref[1]) + (blocks_ref[2] + blocks_ref[3])
    pivot = (pivot + pivot.T) * 0.5
    row_id = lax.broadcasted_iota(jnp.int32, (share, 1), 0)
    work = jnp.concatenate([pivot, jnp.eye(share, dtype=jnp.float32)], 1)
    for k in range(share):
        row = work[k:k + 1, :]
        scale = lax.rsqrt(row[:, k:k + 1])
        unit_row = row * scale
        below = jnp.where(row_id > k, work[:, k:k + 1] * scale, 0.0)
        work = jnp.where(row_id == k, unit_row, work - below * unit_row)
    inverse_ref[...] = work[:, share:]


def pivot_inverse(blocks):
    share = blocks.shape[1]
    vmem = pl.BlockSpec(memory_space=pltpu.VMEM)
    return pl.pallas_call(
        pivot_inverse_kernel,
        out_shape=jax.ShapeDtypeStruct((share, share), jnp.float32),
        in_specs=[vmem],
        out_specs=vmem,
    )(blocks)


def panel_kernel(owner_ref, pieces_ref, inverse_ref, self_ref, coupling_ref, panel_ref):
    share = panel_ref.shape[0]
    width = self_ref.shape[1]
    total = (pieces_ref[0] + pieces_ref[1]) + (pieces_ref[2] + pieces_ref[3])
    own = total[:share]
    lead = total[share:]
    owner = owner_ref[0]
    columns = jnp.zeros((share, share), jnp.float32)
    for q in range(width // share):
        columns = jnp.where(owner == q, own[:, q * share:(q + 1) * share], columns)
    inverse = inverse_ref[...]
    panel = _exact(columns, inverse, ((1,), (1,)))
    weights = _exact(panel, inverse, ((1,), (0,)))
    updated = own - _exact(weights, lead, ((1,), (0,)))
    self_ref[...] = updated[:, :width]
    coupling_ref[...] = updated[:, width:]
    panel_ref[...] = panel


def eliminate_panel(owner, pieces, inverse, width):
    share = pieces.shape[1] // 2
    vmem = pl.BlockSpec(memory_space=pltpu.VMEM)
    return pl.pallas_call(
        panel_kernel,
        out_shape=(
            jax.ShapeDtypeStruct((share, width), jnp.float32),
            jax.ShapeDtypeStruct((share, pieces.shape[2] - width), jnp.float32),
            jax.ShapeDtypeStruct((share, share), jnp.float32),
        ),
        in_specs=[pl.BlockSpec(memory_space=pltpu.SMEM), vmem, vmem],
        out_specs=(vmem, vmem, vmem),
    )(owner, pieces, inverse)


def coarse_rows_kernel(owner_ref, gram_ref, own_ref, down_ref, up_ref, fdn_ref, fup_ref, out_ref, whole_ref):
    width = gram_ref.shape[0]
    share = out_ref.shape[1] // 2
    sources = {
        0: (fup_ref, 2), 1: (fup_ref, 0), 2: (fup_ref, 1), 3: (up_ref, 1),
        4: (down_ref, 1), 5: (fdn_ref, 2), 6: (fdn_ref, 0), 7: (fdn_ref, 1),
    }
    whole_ref[:, :width] = gram_ref[...]
    for slot in range(own_ref.shape[0]):
        ref, place = sources[slot]
        block = _atb(own_ref[slot, 0], ref[place, 0])
        for unit in range(1, own_ref.shape[1]):
            block = block + _atb(own_ref[slot, unit], ref[place, unit])
        whole_ref[:, (slot + 1) * width:(slot + 2) * width] = block
    start = pl.multiple_of(owner_ref[0] * share, share)
    pivot = whole_ref[pl.ds(start, share), :]
    for target in range(out_ref.shape[0]):
        out_ref[target, :share] = whole_ref[target * share:(target + 1) * share, :]
        out_ref[target, share:] = pivot


def coarse_rows(owner, gram, own, down, up, far_down, far_up, crow_count):
    width = gram.shape[0]
    share = width // crow_count
    columns = width * (own.shape[0] + 1)
    vmem = pl.BlockSpec(memory_space=pltpu.VMEM)
    return pl.pallas_call(
        coarse_rows_kernel,
        out_shape=jax.ShapeDtypeStruct((crow_count, 2 * share, columns), jnp.float32),
        in_specs=[pl.BlockSpec(memory_space=pltpu.SMEM)] + [vmem] * 6,
        out_specs=vmem,
        scratch_shapes=[pltpu.VMEM((width, columns), jnp.float32)],
    )(owner, gram, own, down, up, far_down, far_up)


def per_device(deflation, diag_op, upper_op, tile_blocks, pair_counts, pivot_owner):
    crow_count = lax.axis_size("crow")
    crow_place = lax.axis_index("crow")
    sub_count = lax.axis_size("sub")
    across = min(16, sub_count // 2)
    offsets = neighbour_offsets(across)
    local_rows = deflation[0]
    blocks_here, tile_rows = (diag_op.shape[1], diag_op.shape[2])
    coarse_width = local_rows.shape[1]
    slot_count = pair_counts.shape[1]
    per_slot = tile_blocks.shape[2] // slot_count
    forward_pair = shifted(
        jnp.stack([local_rows[-tile_rows:], upper_op[0, blocks_here - 1]]), "crow", 1
    )
    next_rows = shifted(local_rows[:tile_rows], "crow", -1)
    slot_of = {offset: index for index, offset in enumerate(offsets)}
    groups = (
        (slot_of[-across - 1], slot_of[-1], slot_of[across - 1]),
        (slot_of[-across + 1], slot_of[1], slot_of[across + 1]),
        (slot_of[-across],),
        (slot_of[across],),
    )
    down_out, up_out, near_down, near_up, own_masked, gram_part = local_apply(
        groups, tile_blocks, pair_counts, deflation, forward_pair, next_rows, diag_op, upper_op
    )
    row_share = coarse_width // crow_count
    corner = pivot_owner[0] * row_share
    pivot_part = lax.dynamic_slice(gram_part, (corner, corner), (row_share, row_share))
    pivot_parts = lax.all_to_all(
        jnp.broadcast_to(pivot_part[None], (crow_count, row_share, row_share)),
        "crow", 0, 0, tiled=True,
    )
    inverse = pivot_inverse(pivot_parts)
    last = sub_count - 1
    down = lax.ppermute(
        down_out, "sub", [(t, t - 1) for t in range(1, sub_count)] + [(0, last)]
    )
    up = lax.ppermute(up_out, "sub", [(t, t + 1) for t in range(last)] + [(last, 0)])
    far_down = lax.ppermute(
        jnp.concatenate([near_down, down[:1], up[:1]]),
        "sub",
        [(u, u - across) for u in range(across, sub_count)] + [(0, sub_count - across)],
    )
    far_up = lax.ppermute(
        jnp.concatenate([near_up, down[2:], up[2:]]),
        "sub",
        [(u, u + across) for u in range(sub_count - across)] + [(last, across - 1)],
    )
    assert offsets == [-across - 1, -across, -across + 1, -1, 1, across - 1, across, across + 1]
    outgoing_rows = coarse_rows(
        pivot_owner, gram_part, own_masked, down, up, far_down, far_up, crow_count
    )
    pieces = lax.all_to_all(outgoing_rows, "crow", 0, 0, tiled=True)
    return eliminate_panel(pivot_owner, pieces, inverse, coarse_width)


def solution(mesh):
    placed = (
        P("sub", "crow", None),
        P("sub", "crow", None, None),
        P("sub", "crow", None, None),
        P("sub", "crow", None),
        P("sub", None),
        P("sub"),
    )
    return jax.shard_map(
        per_device,
        mesh=mesh,
        in_specs=placed,
        out_specs=(P(("sub", "crow"), None), P(("sub", "crow"), None), P(("sub", "crow"), None)),
        check_vma=False,
    )
```
